32 devices in a mesh: groups: 2 (over y), gx: 4 (over z), gy: 2 (over x), gz: 2 (over core).
Axes of the slice: x: 2, y: 2, z: 4, core: 2. Of those that a mesh axis runs over, the one named last changes fastest.
Arguments:
- stream: float32 [256, 64, 512], P('groups', 'gx', 'gy'), parts along dimension 0, may hold values from -6 to 6
- inductance: bfloat16 [16, 32, 8, 2, 128, 128], P(('groups', 'gx'), ('gy', 'gz')), parts along dimension 0, may hold values from -0.25 to 1.25
- near_lists: int32 [16, 32, 8], P(('groups', 'gx'), ('gy', 'gz')), parts along dimension 0, may hold values from 0 to 8, as said below
- filament_leaf: int32 [16384], P(('groups', 'gx', 'gy', 'gz')), parts along dimension 0, may hold values from 0 to 255, as said below
- filament_current: bfloat16 [16384, 128], P(('groups', 'gx', 'gy', 'gz')), parts along dimension 0, may hold values from -6 to 6
- filament_coupling: bfloat16 [16384, 2, 128], P(('groups', 'gx', 'gy', 'gz')), parts along dimension 0, may hold values from -0.75 to 0.75
Outputs:
- loop_voltage: float32 [256, 64, 512], P('groups', 'gx', ('gy', 'gz')), parts along dimension 0
- filament_voltage: bfloat16 [16384, 128], P(('groups', 'gx', 'gy', 'gz')), parts along dimension 0
The draws below stay inside these ranges and needn't reach their ends.
There are 2 independent parts, one for each index of `groups`. The reference program is written for one: setup_inputs(seed, part) draws one part's arguments, and reference() takes and returns one part's arrays. A program takes and returns all parts, laid end to end along the dimension named above; each array names one. Nothing has to cross between parts.
Inputs may be any that keep to these rules, and one draw needn't show every extreme that they name: `near_lists`: entry 0 of every list is 4, the leaf itself; code k names the leaf k // 3 - 1 rows and k % 3 - 1 columns away, and repeats may occur. `filament_leaf`: leaves are numbered row by row over 8 x 32. Device d along gx+gy+gz holds the 2 x 8 leaves of leaf rows (d // (2 * 2)) * 2 on and leaf columns (d % (2 * 2)) * 8 on. Of the 512 filaments of one device, at most 64 lie over the leaves of any one device, and in every device's block some device gets exactly 64.
All inputs are finite; a program needn't handle non-finite values.
Results may differ from the reference program's by a relative error of at most 0.0049.
Values may be sent and summed in bfloat16 or wider, within the bound.
No kernel may reach another device: no remote copies, remote signals or barrier semaphores. Data moves between devices by JAX's collectives and lax.ppermute only.
A program may use at most 128 MiB of HBM per device.

```python
import math
import jax
import jax.numpy as jnp
from jax import lax

P_SIZE = 128
FIL_DEV = 512
LEAF_R = 8
LEAF_C = 16
NEAR = 8
NX = 64
NY = 512
NXL = 8
NYL = 32
LC = 128
LEAF_ROWS_DEV = 2
LEAF_COLS_DEV = 8
LEAF_DEV = 16
OWNERS = 16
CAP = 64
FIL = 8192


def draw_inductance(key, part):
    spread_scale = 1.0 / math.sqrt(NEAR * LC)
    tile_shape = (NXL, NYL, NEAR, 2, LC, LC)
    entries = jnp.clip(jax.random.normal(key, tile_shape, jnp.float32), -6.0, 6.0)
    offdiag = jnp.clip(entries * spread_scale, -0.25, 0.25)
    selfmask = (jnp.arange(NEAR) == 0).astype(jnp.float32)[:, None, None, None]
    diagonal = selfmask * jnp.eye(LC, dtype=jnp.float32)[None, None, :, :]
    return (offdiag + diagonal).astype(jnp.bfloat16)


def draw_near_lists(key, part):
    codes = jax.random.randint(key, (NXL, NYL, NEAR), 0, 9, dtype=jnp.int32)
    return codes.at[:, :, 0].set(4)


def draw_filament_leaf(key, part):
    hot_key, block_key = jax.random.split(jax.random.fold_in(key, 7))
    ranked = jax.random.permutation(hot_key, OWNERS)
    heated = (ranked < OWNERS // 4).astype(jnp.int32)
    slot_total = OWNERS * CAP
    candidate = jnp.arange(slot_total, dtype=jnp.int32)
    owner_table = candidate // CAP
    owner_cols = NYL // LEAF_COLS_DEV

    def one_block(number):
        block_seed = jax.random.fold_in(block_key, number)
        jitter_key, pinned_key, leaf_key = jax.random.split(block_seed, 3)
        jitter = jax.random.randint(jitter_key, (slot_total,), 0, 1024, dtype=jnp.int32)
        pinned = jax.random.randint(pinned_key, (), 0, OWNERS, dtype=jnp.int32)
        priority = jitter + 512 * heated[owner_table] + 4096 * (owner_table == pinned).astype(jnp.int32)
        distinct = priority * slot_total + candidate
        ordered_values, chosen = lax.top_k(distinct, FIL_DEV)
        owner_ids = owner_table[chosen]
        local_ids = jax.random.randint(leaf_key, (FIL_DEV,), 0, LEAF_DEV, dtype=jnp.int32)
        leaf_row = owner_ids // owner_cols * LEAF_ROWS_DEV + local_ids // LEAF_COLS_DEV
        leaf_col = owner_ids % owner_cols * LEAF_COLS_DEV + local_ids % LEAF_COLS_DEV
        return leaf_row * NYL + leaf_col
    return lax.map(one_block, jnp.arange(OWNERS, dtype=jnp.int32)).reshape(-1).astype(jnp.int32)


def shard_levels(stream_key, shape, cuts, least, top_value):
    def one(axis_at, parts):
        heights = jax.random.uniform(jax.random.fold_in(jax.random.fold_in(stream_key, 6), axis_at), (parts,), jnp.float32, least / len(cuts), top_value / len(cuts))
        return jnp.repeat(jnp.exp(heights), shape[axis_at] // parts).reshape((-1,) + (1,) * (len(shape) - axis_at - 1))

    loudness = one(*cuts[0])
    for cut in cuts[1:]:
        loudness = loudness * one(*cut)
    return loudness


def centred(rng, shape, width, most, cuts=(), kind=jnp.bfloat16):
    level = shard_levels(rng, shape, cuts, -0.22, 0.18) if cuts else 1.0
    array = jax.random.normal(rng, shape, jnp.float32) * width * level
    return jnp.minimum(jnp.maximum(array, -most), most).astype(kind)


def setup_inputs(seed: int = 0, part: int = 0) -> dict:
    key_of = jax.random.split(jax.random.key(seed), 7)
    part_splits = jax.random.split(jax.random.fold_in(key_of[6], part), 7)
    stream = centred(part_splits[0], (P_SIZE, NX, NY), 1.0, 6.0, ((1, 4), (2, 2)), jnp.float32)
    inductance = draw_inductance(jax.random.fold_in(jax.random.fold_in(key_of[6], part), 71), part)
    near_lists = draw_near_lists(jax.random.fold_in(jax.random.fold_in(key_of[6], part), 71), part)
    filament_leaf = draw_filament_leaf(jax.random.fold_in(jax.random.fold_in(key_of[6], part), 71), part)
    filament_current = centred(part_splits[4], (FIL, P_SIZE), 1.0, 6.0, ((0, 16),))
    filament_coupling = centred(part_splits[5], (FIL, 2, LC), 0.125, 0.75, ((0, 16),))
    return dict(stream=stream, inductance=inductance, near_lists=near_lists, filament_leaf=filament_leaf, filament_current=filament_current, filament_coupling=filament_coupling)


def plane_curl(padded):
    along_y = padded[:, 1:-1, 2:] - padded[:, 1:-1, :-2]
    along_x = padded[:, :-2, 1:-1] - padded[:, 2:, 1:-1]
    return jnp.stack([along_y, along_x])


def to_leaves(grid_values):
    components, port_count, row_count, col_count = grid_values.shape
    blocks = grid_values.reshape(components, port_count, row_count // LEAF_R, LEAF_R, col_count // LEAF_C, LEAF_C)
    blocks = blocks.transpose(2, 4, 0, 1, 3, 5)
    return blocks.reshape(row_count // LEAF_R, col_count // LEAF_C, components, port_count, LEAF_R * LEAF_C)


def from_leaves(leaves):
    leaf_rows, leaf_cols, components, port_count, leaf_cells = leaves.shape
    blocks = leaves.reshape(leaf_rows, leaf_cols, components, port_count, LEAF_R, LEAF_C)
    blocks = blocks.transpose(2, 3, 0, 4, 1, 5)
    return blocks.reshape(components, port_count, leaf_rows * LEAF_R, leaf_cols * LEAF_C)


def reference(stream, inductance, near_lists, filament_leaf, filament_current, filament_coupling):
    padded = jnp.pad(stream, ((0, 0), (1, 1), (1, 1)))
    currents = plane_curl(padded).astype(jnp.bfloat16)
    leaves = to_leaves(currents)
    bordered = jnp.pad(leaves, ((1, 1), (1, 1), (0, 0), (0, 0), (0, 0)))
    row_stride = NYL + 2
    flattened = bordered.reshape((NXL + 2) * row_stride, 2, P_SIZE, LC)
    row_shift = near_lists // 3 - 1
    col_shift = near_lists % 3 - 1
    source = (jnp.arange(NXL, dtype=jnp.int32)[:, None, None] + 1 + row_shift) * row_stride
    source = (source + jnp.arange(NYL, dtype=jnp.int32)[None, :, None] + 1 + col_shift).astype(jnp.int32)

    def one_row(operands):
        kernels, chosen = operands
        gathered = jnp.take(flattened, chosen.reshape(-1), axis=0).reshape(NYL, NEAR, 2, P_SIZE, LC)
        return jnp.einsum("jncab,jncpb->jcpa", kernels.astype(jnp.float32), gathered.astype(jnp.float32))

    near_field = lax.map(one_row, (inductance, source))

    leaf_total = NXL * NYL
    leaves_flat = leaves.reshape(leaf_total, 2, P_SIZE, LC)

    def one_block(carried, operands):
        leaf_ids, current, coupling = operands
        current_wide = current.astype(jnp.float32)
        coupling_wide = coupling.astype(jnp.float32)
        beneath = jnp.take(leaves_flat, leaf_ids, axis=0).astype(jnp.float32)
        voltage = jnp.einsum("fca,fcpa->fp", coupling_wide, beneath)
        deposit = jnp.einsum("fca,fp->fcpa", coupling_wide, current_wide)
        carried = carried.at[leaf_ids].add(deposit)
        return carried, voltage.astype(jnp.bfloat16)

    initial = jnp.zeros((leaf_total, 2, P_SIZE, LC), jnp.float32)
    filament_field, voltages = lax.scan(
        one_block,
        initial,
        (filament_leaf.reshape(OWNERS, FIL_DEV).astype(jnp.int32),
         filament_current.reshape(OWNERS, FIL_DEV, P_SIZE),
         filament_coupling.reshape(OWNERS, FIL_DEV, 2, LC)))
    total_field = (near_field + filament_field.reshape(NXL, NYL, 2, P_SIZE, LC)).astype(jnp.bfloat16)
    grid_field = jnp.pad(from_leaves(total_field), ((0, 0), (0, 0), (1, 1), (1, 1))).astype(jnp.float32)
    x_field = grid_field[0]
    y_field = grid_field[1]
    loop_voltage = (x_field[:, 1:-1, :-2] - x_field[:, 1:-1, 2:]) + (y_field[:, 2:, 1:-1] - y_field[:, :-2, 1:-1])
    return loop_voltage, voltages.reshape(FIL, P_SIZE)
```

```python
import jax
import jax.numpy as jnp
from jax import lax
from jax.sharding import PartitionSpec as P

LEAF_R = 8
LEAF_C = 16
AXES = ("gx", "gy", "gz")


def plane_curl(padded):
    along_y = padded[:, 1:-1, 2:] - padded[:, 1:-1, :-2]
    along_x = padded[:, :-2, 1:-1] - padded[:, 2:, 1:-1]
    return jnp.stack([along_y, along_x])


def to_leaves(grid_values):
    components, port_count, row_count, col_count = grid_values.shape
    blocks = grid_values.reshape(
        components, port_count, row_count // LEAF_R, LEAF_R, col_count // LEAF_C, LEAF_C
    )
    blocks = blocks.transpose(2, 4, 0, 1, 3, 5)
    return blocks.reshape(
        row_count // LEAF_R, col_count // LEAF_C, components, port_count, LEAF_R * LEAF_C
    )


def from_leaves(leaves):
    leaf_rows, leaf_cols, components, port_count, leaf_cells = leaves.shape
    blocks = leaves.reshape(leaf_rows, leaf_cols, components, port_count, LEAF_R, LEAF_C)
    blocks = blocks.transpose(2, 3, 0, 4, 1, 5)
    return blocks.reshape(components, port_count, leaf_rows * LEAF_R, leaf_cols * LEAF_C)


def device_grid():
    nx, ny, nz = (lax.axis_size(a) for a in AXES)
    return nx, ny, nz


def pairs_by(fn):
    nx, ny, nz = device_grid()
    out = []
    for x in range(nx):
        for y in range(ny):
            for z in range(nz):
                target = fn(x, y, z)
                if target is None:
                    continue
                tx, ty, tz = target
                if 0 <= tx < nx and 0 <= ty < ny and 0 <= tz < nz:
                    out.append(((x * ny + y) * nz + z, (tx * ny + ty) * nz + tz))
    return out


def send(value, fn):
    return lax.ppermute(value, AXES, pairs_by(fn))


def sideways(x, y, z, dx):
    nz = lax.axis_size("gz")
    if z == nz - 1:
        return (x + dx, y + 1, 0)
    if z == 0:
        return (x + dx, y - 1, nz - 1)
    return None


def stream_window(stream, half):
    nx, ny, nz = device_grid()
    gz = lax.axis_index("gz")
    rows, width = stream.shape[1], stream.shape[2]
    hr, hc = LEAF_R + 1, LEAF_C + 1
    mid_w = half + hc
    mid = lax.dynamic_slice_in_dim(stream, gz * (width - mid_w), mid_w, 2)
    side = lax.dynamic_slice_in_dim(stream, gz * (width - hc), hc, 2)
    h_got = send(side, lambda x, y, z: sideways(x, y, z, 0))
    v_top = send(mid[:, rows - hr :], lambda x, y, z: (x + 1, y, z))
    v_bot = send(mid[:, :hr], lambda x, y, z: (x - 1, y, z))
    d_top = send(side[:, rows - hr :], lambda x, y, z: sideways(x, y, z, 1))
    d_bot = send(side[:, :hr], lambda x, y, z: sideways(x, y, z, -1))
    left = gz == 0

    def join(core, edge):
        return jnp.where(left, jnp.concatenate([edge, core], 2), jnp.concatenate([core, edge], 2))

    return jnp.concatenate([join(v_top, d_top), join(mid, h_got), join(v_bot, d_bot)], 1)


def field_halo(grid_field):
    x_field = grid_field[0]
    y_field = grid_field[1]
    rows = y_field.shape[1]
    cols = x_field.shape[2]

    def step(x, y, z, dc):
        nz = lax.axis_size("gz")
        c = y * nz + z + dc
        return (x, c // nz, c % nz) if c >= 0 else None

    x_left = send(x_field[:, :, cols - 1 :], lambda x, y, z: step(x, y, z, 1))
    x_right = send(x_field[:, :, :1], lambda x, y, z: step(x, y, z, -1))
    y_top = send(y_field[:, rows - 1 :], lambda x, y, z: (x + 1, y, z))
    y_bot = send(y_field[:, :1], lambda x, y, z: (x - 1, y, z))
    x_pad = jnp.concatenate([x_left, x_field, x_right], 2).astype(jnp.float32)
    y_pad = jnp.concatenate([y_top, y_field, y_bot], 1).astype(jnp.float32)
    return x_pad[:, :, :-2] - x_pad[:, :, 2:] + (y_pad[:, 2:] - y_pad[:, :-2])


def body(stream, inductance, near_lists, filament_leaf, filament_current, filament_coupling):
    port_count = stream.shape[0]
    leaf_rows = inductance.shape[0]
    leaf_cols = inductance.shape[1]
    near_count = inductance.shape[2]
    leaf_cells = inductance.shape[4]
    leaf_count = leaf_rows * leaf_cols
    half_cols = leaf_cols * LEAF_C
    nx, ny, nz = device_grid()
    gx = lax.axis_index("gx")
    col_index = lax.axis_index("gy") * nz + lax.axis_index("gz")
    me = gx * (ny * nz) + col_index
    owners = nx * ny * nz

    filament_count = filament_leaf.shape[0]
    capacity = max(2, 2 * filament_count // owners)
    slot_count = owners * capacity
    plane_cols = leaf_cols * ny * nz

    def owner_and_local(leaf):
        leaf_row = leaf // plane_cols
        leaf_col = leaf % plane_cols
        owner = leaf_row // leaf_rows * (ny * nz) + leaf_col // leaf_cols
        local = leaf_row % leaf_rows * leaf_cols + leaf_col % leaf_cols
        return owner, local

    owner_ids, _ = owner_and_local(filament_leaf)
    owner_hits = (owner_ids[:, None] == jnp.arange(owners, dtype=jnp.int32)[None, :]).astype(
        jnp.int32
    )
    position = jnp.sum((jnp.cumsum(owner_hits, axis=0) - 1) * owner_hits, axis=1)
    target_slot = owner_ids * capacity + position
    placement_mask = target_slot[None, :] == jnp.arange(slot_count, dtype=jnp.int32)[:, None]
    placement = placement_mask.astype(jnp.bfloat16)
    rows_out = jnp.concatenate(
        [filament_coupling.reshape(filament_count, 2 * leaf_cells), filament_current], 1
    )
    sent = jnp.dot(placement, rows_out, preferred_element_type=jnp.float32).astype(jnp.bfloat16)
    got = lax.all_to_all(
        sent.reshape(owners, capacity, -1), AXES, split_axis=0, concat_axis=0, tiled=True
    ).reshape(slot_count, -1)
    got_coupling = got[:, : 2 * leaf_cells]
    got_current = got[:, 2 * leaf_cells :]

    all_leaf = lax.all_gather(filament_leaf, AXES, tiled=True).reshape(owners, filament_count)
    src_owner, src_local = owner_and_local(all_leaf)
    mine = (src_owner == me).astype(jnp.int32)
    src_pos = jnp.cumsum(mine, axis=1) - 1
    slot_hit = (mine[:, :, None] > 0) & (
        src_pos[:, :, None] == jnp.arange(capacity, dtype=jnp.int32)[None, None, :]
    )
    got_leaf = jnp.max(jnp.where(slot_hit, src_local[:, :, None], -1), axis=1).reshape(slot_count)

    window = stream_window(stream, half_cols)
    currents = plane_curl(window).astype(jnp.bfloat16)
    bordered = to_leaves(currents)
    ring_rows = jnp.arange(leaf_rows + 2, dtype=jnp.int32)
    ring_cols = jnp.arange(leaf_cols + 2, dtype=jnp.int32)
    row_ok = ((ring_rows > 0) | (gx > 0)) & ((ring_rows < leaf_rows + 1) | (gx < nx - 1))
    col_ok = ((ring_cols > 0) | (col_index > 0)) & (
        (ring_cols < leaf_cols + 1) | (col_index < ny * nz - 1)
    )
    inside = (row_ok[:, None] & col_ok[None, :]).astype(jnp.bfloat16)
    bordered = bordered * inside[:, :, None, None, None]

    row_stride = leaf_cols + 2
    flattened = bordered.reshape((leaf_rows + 2) * row_stride, 2, port_count, leaf_cells)
    row_shift = near_lists // 3 - 1
    col_shift = near_lists % 3 - 1
    source = (jnp.arange(leaf_rows, dtype=jnp.int32)[:, None, None] + 1 + row_shift) * row_stride
    source = source + jnp.arange(leaf_cols, dtype=jnp.int32)[None, :, None] + 1 + col_shift
    sources = jnp.take(flattened, source.reshape(-1), axis=0).reshape(
        leaf_count, near_count, 2, port_count, leaf_cells
    )
    kernels = inductance.reshape(leaf_count, near_count, 2, leaf_cells, leaf_cells)
    near_field = lax.dot_general(
        sources, kernels, (((1, 4), (1, 4)), ((0, 2), (0, 2))), preferred_element_type=jnp.float32
    )
    own_leaves = bordered[1:-1, 1:-1].reshape(leaf_count, 2, port_count, leaf_cells)

    leaf_hits = (got_leaf[:, None] == jnp.arange(leaf_count, dtype=jnp.int32)[None, :]).astype(
        jnp.bfloat16
    )
    spread = (leaf_hits[:, :, None] * got_coupling[:, None, :]).reshape(
        slot_count, leaf_count * 2 * leaf_cells
    )
    filament_field = lax.dot_general(
        got_current, spread, (((0,), (0,)), ((), ())), preferred_element_type=jnp.float32
    )
    filament_field = filament_field.reshape(port_count, leaf_count, 2, leaf_cells).transpose(
        1, 2, 0, 3
    )
    plane_rows = own_leaves.transpose(2, 0, 1, 3).reshape(port_count, leaf_count * 2 * leaf_cells)
    induced = lax.dot_general(
        spread, plane_rows, (((1,), (1,)), ((), ())), preferred_element_type=jnp.float32
    ).astype(jnp.bfloat16)
    returned = lax.all_to_all(
        induced.reshape(owners, capacity, port_count), AXES, split_axis=0, concat_axis=0, tiled=True
    ).reshape(slot_count, port_count)
    filament_voltage = lax.dot_general(
        placement, returned, (((0,), (0,)), ((), ())), preferred_element_type=jnp.float32
    ).astype(jnp.bfloat16)

    total_field = (near_field + filament_field).astype(jnp.bfloat16)
    grid_field = from_leaves(total_field.reshape(leaf_rows, leaf_cols, 2, port_count, leaf_cells))
    loop_voltage = field_halo(grid_field)
    return (loop_voltage, filament_voltage)


def solution(mesh):
    return jax.shard_map(
        body,
        mesh=mesh,
        in_specs=(
            P("groups", "gx", "gy"),
            P(("groups", "gx"), ("gy", "gz"), None, None, None, None),
            P(("groups", "gx"), ("gy", "gz"), None),
            P(("groups", "gx", "gy", "gz")),
            P(("groups", "gx", "gy", "gz"), None),
            P(("groups", "gx", "gy", "gz"), None, None),
        ),
        out_specs=(P("groups", "gx", ("gy", "gz")), P(("groups", "gx", "gy", "gz"), None)),
        check_vma=False,
    )
```

```python
import jax
import jax.numpy as jnp
from jax import lax
from jax.experimental import pallas as pl
from jax.experimental.pallas import tpu as pltpu
from jax.sharding import PartitionSpec as P

LEAF_R = 8
LEAF_C = 16
AXES = ("gx", "gy", "gz")


def plane_curl(padded):
    along_y = padded[:, 1:-1, 2:] - padded[:, 1:-1, :-2]
    along_x = padded[:, :-2, 1:-1] - padded[:, 2:, 1:-1]
    return jnp.stack([along_y, along_x])


def to_leaves(grid_values):
    components, port_count, row_count, col_count = grid_values.shape
    blocks = grid_values.reshape(
        components, port_count, row_count // LEAF_R, LEAF_R, col_count // LEAF_C, LEAF_C
    )
    blocks = blocks.transpose(2, 4, 0, 1, 3, 5)
    return blocks.reshape(
        row_count // LEAF_R, col_count // LEAF_C, components, port_count, LEAF_R * LEAF_C
    )


def from_leaves(leaves):
    leaf_rows, leaf_cols, components, port_count, leaf_cells = leaves.shape
    blocks = leaves.reshape(leaf_rows, leaf_cols, components, port_count, LEAF_R, LEAF_C)
    blocks = blocks.transpose(2, 3, 0, 4, 1, 5)
    return blocks.reshape(components, port_count, leaf_rows * LEAF_R, leaf_cols * LEAF_C)


def device_grid():
    nx, ny, nz = (lax.axis_size(a) for a in AXES)
    return nx, ny, nz


def pairs_by(fn):
    nx, ny, nz = device_grid()
    out = []
    for x in range(nx):
        for y in range(ny):
            for z in range(nz):
                target = fn(x, y, z)
                if target is None:
                    continue
                tx, ty, tz = target
                if 0 <= tx < nx and 0 <= ty < ny and 0 <= tz < nz:
                    out.append(((x * ny + y) * nz + z, (tx * ny + ty) * nz + tz))
    return out


def send(value, fn):
    return lax.ppermute(value, AXES, pairs_by(fn))


def sideways(x, y, z, dx):
    nz = lax.axis_size("gz")
    if z == nz - 1:
        return (x + dx, y + 1, 0)
    if z == 0:
        return (x + dx, y - 1, nz - 1)
    return None


def stream_window(stream, half):
    nx, ny, nz = device_grid()
    gz = lax.axis_index("gz")
    rows, width = stream.shape[1], stream.shape[2]
    hr, hc = LEAF_R + 1, LEAF_C + 1
    mid_w = half + hc
    mid = lax.dynamic_slice_in_dim(stream, gz * (width - mid_w), mid_w, 2)
    side = lax.dynamic_slice_in_dim(stream, gz * (width - hc), hc, 2)
    h_got = send(side, lambda x, y, z: sideways(x, y, z, 0))
    v_top = send(mid[:, rows - hr :], lambda x, y, z: (x + 1, y, z))
    v_bot = send(mid[:, :hr], lambda x, y, z: (x - 1, y, z))
    d_top = send(side[:, rows - hr :], lambda x, y, z: sideways(x, y, z, 1))
    d_bot = send(side[:, :hr], lambda x, y, z: sideways(x, y, z, -1))
    left = gz == 0

    def join(core, edge):
        return jnp.where(left, jnp.concatenate([edge, core], 2), jnp.concatenate([core, edge], 2))

    return jnp.concatenate([join(v_top, d_top), join(mid, h_got), join(v_bot, d_bot)], 1)


def field_halo(grid_field):
    x_field = grid_field[0]
    y_field = grid_field[1]
    rows = y_field.shape[1]
    cols = x_field.shape[2]

    def step(x, y, z, dc):
        nz = lax.axis_size("gz")
        c = y * nz + z + dc
        return (x, c // nz, c % nz) if c >= 0 else None

    x_left = send(x_field[:, :, cols - 1 :], lambda x, y, z: step(x, y, z, 1))
    x_right = send(x_field[:, :, :1], lambda x, y, z: step(x, y, z, -1))
    y_top = send(y_field[:, rows - 1 :], lambda x, y, z: (x + 1, y, z))
    y_bot = send(y_field[:, :1], lambda x, y, z: (x - 1, y, z))
    x_pad = jnp.concatenate([x_left, x_field, x_right], 2).astype(jnp.float32)
    y_pad = jnp.concatenate([y_top, y_field, y_bot], 1).astype(jnp.float32)
    return x_pad[:, :, :-2] - x_pad[:, :, 2:] + (y_pad[:, 2:] - y_pad[:, :-2])


def leaf_kernel(codes_ref, bord_ref, ind_ref, leaf_ref, cpl_ref, cur_ref, field_ref, volt_ref, acc_ref):
    leaf = pl.program_id(0)
    leaf_cols = bord_ref.shape[1] - 2
    near_count = ind_ref.shape[1]
    components = ind_ref.shape[2]
    cells = ind_ref.shape[3]
    row = leaf // leaf_cols
    col = leaf % leaf_cols

    @pl.when(leaf == 0)
    def _():
        acc_ref[...] = jnp.zeros_like(acc_ref)

    mask = leaf_ref[...] == leaf
    coupling = jnp.where(mask, cpl_ref[...], jnp.zeros_like(cpl_ref[...]))
    current = cur_ref[...]
    volt = acc_ref[...]
    for c in range(components):
        total = jnp.zeros((current.shape[0], cells), jnp.float32)
        for n in range(near_count):
            code = codes_ref[leaf * near_count + n]
            src_row = jnp.minimum(jnp.maximum(row + code // 3, 0), bord_ref.shape[0] - 1)
            src_col = jnp.minimum(jnp.maximum(col + code % 3, 0), bord_ref.shape[1] - 1)
            total += lax.dot_general(
                bord_ref[src_row, src_col, c],
                ind_ref[0, n, c],
                (((1,), (1,)), ((), ())),
                preferred_element_type=jnp.float32,
            )
        part = coupling[:, c * cells : (c + 1) * cells]
        total += jnp.dot(current, part, preferred_element_type=jnp.float32)
        field_ref[0, c] = total.astype(field_ref.dtype)
        volt += lax.dot_general(
            part, bord_ref[row + 1, col + 1, c], (((1,), (1,)), ((), ())),
            preferred_element_type=jnp.float32,
        )
    acc_ref[...] = volt

    @pl.when(leaf == pl.num_programs(0) - 1)
    def _():
        volt_ref[...] = volt.astype(volt_ref.dtype)


def leaf_fields(codes, bordered, kernels, slot_leaf, coupling, current_t):
    leaf_count, near_count, components, cells, _ = kernels.shape
    port_count, slot_count = current_t.shape

    def whole(shape):
        return pl.BlockSpec(shape, lambda l, codes: (0,) * len(shape))

    grid_spec = pltpu.PrefetchScalarGridSpec(
        num_scalar_prefetch=1,
        grid=(leaf_count,),
        in_specs=[
            whole(bordered.shape),
            pl.BlockSpec((1, near_count, components, cells, cells), lambda l, codes: (l, 0, 0, 0, 0)),
            whole(slot_leaf.shape),
            whole(coupling.shape),
            whole(current_t.shape),
        ],
        out_specs=[
            pl.BlockSpec((1, components, port_count, cells), lambda l, codes: (l, 0, 0, 0)),
            whole((slot_count, port_count)),
        ],
        scratch_shapes=[pltpu.VMEM((slot_count, port_count), jnp.float32)],
    )
    return pl.pallas_call(
        leaf_kernel,
        grid_spec=grid_spec,
        out_shape=[
            jax.ShapeDtypeStruct((leaf_count, components, port_count, cells), jnp.bfloat16),
            jax.ShapeDtypeStruct((slot_count, port_count), jnp.bfloat16),
        ],
        compiler_params=pltpu.CompilerParams(dimension_semantics=("arbitrary",)),
    )(codes, bordered, kernels, slot_leaf, coupling, current_t)


def body(stream, inductance, near_lists, filament_leaf, filament_current, filament_coupling):
    port_count = stream.shape[0]
    leaf_rows = inductance.shape[0]
    leaf_cols = inductance.shape[1]
    near_count = inductance.shape[2]
    leaf_cells = inductance.shape[4]
    leaf_count = leaf_rows * leaf_cols
    half_cols = leaf_cols * LEAF_C
    nx, ny, nz = device_grid()
    gx = lax.axis_index("gx")
    col_index = lax.axis_index("gy") * nz + lax.axis_index("gz")
    owners = nx * ny * nz

    filament_count = filament_leaf.shape[0]
    capacity = max(2, 2 * filament_count // owners)
    slot_count = owners * capacity
    plane_cols = leaf_cols * ny * nz
    leaf_row = filament_leaf // plane_cols
    leaf_col = filament_leaf % plane_cols
    owner_ids = leaf_row // leaf_rows * (ny * nz) + leaf_col // leaf_cols
    local_ids = leaf_row % leaf_rows * leaf_cols + leaf_col % leaf_cols
    owner_hits = (owner_ids[:, None] == jnp.arange(owners, dtype=jnp.int32)[None, :]).astype(
        jnp.int32
    )
    position = jnp.sum((jnp.cumsum(owner_hits, axis=0) - 1) * owner_hits, axis=1)
    target_slot = owner_ids * capacity + position
    placement_mask = target_slot[None, :] == jnp.arange(slot_count, dtype=jnp.int32)[:, None]
    placement = placement_mask.astype(jnp.bfloat16)
    row_width = 2 * leaf_cells + port_count
    rows_out = jnp.concatenate(
        [filament_coupling.reshape(filament_count, 2 * leaf_cells), filament_current], 1
    )
    sent = jnp.dot(placement, rows_out, preferred_element_type=jnp.float32).astype(jnp.bfloat16)
    sent_leaf = jnp.max(jnp.where(placement_mask, local_ids[None, :], -1), axis=1)
    payload = jnp.concatenate(
        [
            sent.reshape(owners, capacity * row_width),
            sent_leaf.astype(jnp.bfloat16).reshape(owners, capacity),
        ],
        1,
    )
    got = lax.all_to_all(payload, AXES, split_axis=0, concat_axis=0, tiled=True)
    got_rows = got[:, : capacity * row_width].reshape(slot_count, row_width)
    got_leaf = got[:, capacity * row_width :].reshape(slot_count, 1).astype(jnp.int32)
    got_coupling = got_rows[:, : 2 * leaf_cells]
    got_current_t = got_rows[:, 2 * leaf_cells :].T

    window = stream_window(stream, half_cols)
    currents = plane_curl(window).astype(jnp.bfloat16)
    bordered = to_leaves(currents)
    ring_rows = jnp.arange(leaf_rows + 2, dtype=jnp.int32)
    ring_cols = jnp.arange(leaf_cols + 2, dtype=jnp.int32)
    row_ok = ((ring_rows > 0) | (gx > 0)) & ((ring_rows < leaf_rows + 1) | (gx < nx - 1))
    col_ok = ((ring_cols > 0) | (col_index > 0)) & (
        (ring_cols < leaf_cols + 1) | (col_index < ny * nz - 1)
    )
    inside = (row_ok[:, None] & col_ok[None, :]).astype(jnp.bfloat16)
    bordered = bordered * inside[:, :, None, None, None]

    kernels = inductance.reshape(leaf_count, near_count, 2, leaf_cells, leaf_cells)
    total_field, induced = leaf_fields(
        near_lists.reshape(-1), bordered, kernels, got_leaf, got_coupling, got_current_t
    )
    returned = lax.all_to_all(
        induced.reshape(owners, capacity, port_count), AXES, split_axis=0, concat_axis=0, tiled=True
    ).reshape(slot_count, port_count)
    filament_voltage = lax.dot_general(
        placement, returned, (((0,), (0,)), ((), ())), preferred_element_type=jnp.float32
    ).astype(jnp.bfloat16)

    grid_field = from_leaves(total_field.reshape(leaf_rows, leaf_cols, 2, port_count, leaf_cells))
    loop_voltage = field_halo(grid_field)
    return (loop_voltage, filament_voltage)


def solution(mesh):
    return jax.shard_map(
        body,
        mesh=mesh,
        in_specs=(
            P("groups", "gx", "gy"),
            P(("groups", "gx"), ("gy", "gz"), None, None, None, None),
            P(("groups", "gx"), ("gy", "gz"), None),
            P(("groups", "gx", "gy", "gz")),
            P(("groups", "gx", "gy", "gz"), None),
            P(("groups", "gx", "gy", "gz"), None, None),
        ),
        out_specs=(P("groups", "gx", ("gy", "gz")), P(("groups", "gx", "gy", "gz"), None)),
        check_vma=False,
    )
```

```python
import jax
import jax.numpy as jnp
from jax import lax
from jax.experimental import pallas as pl
from jax.experimental.pallas import tpu as pltpu
from jax.sharding import PartitionSpec as P

LEAF_R = 8
LEAF_C = 16
AXES = ("gx", "gy", "gz")


def plane_curl(padded):
    along_y = padded[1:-1, 2:] - padded[1:-1, :-2]
    along_x = padded[:-2, 1:-1] - padded[2:, 1:-1]
    return jnp.stack([along_y, along_x])


def to_leaves(grid_values):
    components, row_count, col_count, port_count = grid_values.shape
    blocks = grid_values.reshape(
        components, row_count // LEAF_R, LEAF_R, col_count // LEAF_C, LEAF_C, port_count
    )
    blocks = blocks.transpose(1, 3, 0, 2, 4, 5)
    return blocks.reshape(
        row_count // LEAF_R, col_count // LEAF_C, components, LEAF_R * LEAF_C, port_count
    )


def from_leaves(leaves):
    leaf_rows, leaf_cols, components, leaf_cells, port_count = leaves.shape
    blocks = leaves.reshape(leaf_rows, leaf_cols, components, LEAF_R, LEAF_C, port_count)
    blocks = blocks.transpose(2, 0, 3, 1, 4, 5)
    return blocks.reshape(components, leaf_rows * LEAF_R, leaf_cols * LEAF_C, port_count)


def device_grid():
    nx, ny, nz = (lax.axis_size(a) for a in AXES)
    return nx, ny, nz


def pairs_by(fn):
    nx, ny, nz = device_grid()
    out = []
    for x in range(nx):
        for y in range(ny):
            for z in range(nz):
                target = fn(x, y, z)
                if target is None:
                    continue
                tx, ty, tz = target
                if 0 <= tx < nx and 0 <= ty < ny and 0 <= tz < nz:
                    out.append(((x * ny + y) * nz + z, (tx * ny + ty) * nz + tz))
    return out


def send(value, fn):
    return lax.ppermute(value, AXES, pairs_by(fn))


def sideways(x, y, z, dx):
    nz = lax.axis_size("gz")
    if z == nz - 1:
        return (x + dx, y + 1, 0)
    if z == 0:
        return (x + dx, y - 1, nz - 1)
    return None


def stream_window(stream, half):
    gz = lax.axis_index("gz")
    rows, width = stream.shape[0], stream.shape[1]
    hr, hc = LEAF_R + 1, LEAF_C + 1
    mid_w = half + hc
    mid = lax.dynamic_slice_in_dim(stream, gz * (width - mid_w), mid_w, 1)
    side = lax.dynamic_slice_in_dim(stream, gz * (width - hc), hc, 1)
    h_got = send(side, lambda x, y, z: sideways(x, y, z, 0))
    v_top = send(mid[rows - hr :], lambda x, y, z: (x + 1, y, z))
    v_bot = send(mid[:hr], lambda x, y, z: (x - 1, y, z))
    d_top = send(side[rows - hr :], lambda x, y, z: sideways(x, y, z, 1))
    d_bot = send(side[:hr], lambda x, y, z: sideways(x, y, z, -1))
    left = gz == 0

    def join(core, edge):
        return jnp.where(left, jnp.concatenate([edge, core], 1), jnp.concatenate([core, edge], 1))

    return jnp.concatenate([join(v_top, d_top), join(mid, h_got), join(v_bot, d_bot)], 0)


def field_halo(grid_field):
    x_field = grid_field[0]
    y_field = grid_field[1]
    rows = y_field.shape[0]
    cols = x_field.shape[1]

    def step(x, y, z, dc):
        nz = lax.axis_size("gz")
        c = y * nz + z + dc
        return (x, c // nz, c % nz) if c >= 0 else None

    x_left = send(x_field[:, cols - 1 :], lambda x, y, z: step(x, y, z, 1))
    x_right = send(x_field[:, :1], lambda x, y, z: step(x, y, z, -1))
    y_top = send(y_field[rows - 1 :], lambda x, y, z: (x + 1, y, z))
    y_bot = send(y_field[:1], lambda x, y, z: (x - 1, y, z))
    x_pad = jnp.concatenate([x_left, x_field, x_right], 1).astype(jnp.float32)
    y_pad = jnp.concatenate([y_top, y_field, y_bot], 0).astype(jnp.float32)
    return x_pad[:, :-2] - x_pad[:, 2:] + (y_pad[2:] - y_pad[:-2])


def leaf_kernel(
    codes_ref, scale_ref, bord_ref, ind_ref, row_leaf_ref, col_leaf_ref, cpl_ref, cpl_t_ref,
    cur_ref, field_ref, volt_ref, acc_ref,
):
    leaf = pl.program_id(0)
    leaf_cols = bord_ref.shape[1] - 2
    near_count = ind_ref.shape[1]
    components = ind_ref.shape[2]
    cells = ind_ref.shape[3]
    row = leaf // leaf_cols
    col = leaf % leaf_cols

    @pl.when(leaf == 0)
    def _():
        acc_ref[...] = jnp.zeros_like(acc_ref)

    coupling_t = cpl_t_ref[...]
    coupling_t = jnp.where(row_leaf_ref[...] == leaf, coupling_t, jnp.zeros_like(coupling_t))
    coupling = cpl_ref[...]
    coupling = jnp.where(col_leaf_ref[...] == leaf, coupling, jnp.zeros_like(coupling))
    current = cur_ref[...]
    volt = acc_ref[...]
    for c in range(components):
        total = jnp.dot(
            coupling_t[c * cells : (c + 1) * cells], current, preferred_element_type=jnp.float32
        )
        for n in range(near_count):
            code = codes_ref[leaf * near_count + n]
            src_row = jnp.minimum(jnp.maximum(row + code // 3, 0), bord_ref.shape[0] - 1)
            src_col = jnp.minimum(jnp.maximum(col + code % 3, 0), bord_ref.shape[1] - 1)
            part = jnp.dot(
                ind_ref[0, n, c], bord_ref[src_row, src_col, c], preferred_element_type=jnp.float32
            )
            total += part * scale_ref[leaf * near_count + n]
        field_ref[0, c] = total.astype(field_ref.dtype)
        volt += jnp.dot(
            coupling[:, c * cells : (c + 1) * cells],
            bord_ref[row + 1, col + 1, c],
            preferred_element_type=jnp.float32,
        )
    acc_ref[...] = volt

    @pl.when(leaf == pl.num_programs(0) - 1)
    def _():
        volt_ref[...] = volt.astype(volt_ref.dtype)


def leaf_fields(codes, scales, bordered, kernels, slot_leaf, coupling, current):
    leaf_count, near_count, components, cells, _ = kernels.shape
    slot_count, port_count = current.shape
    coupling_t = coupling.T
    row_leaf = slot_leaf.reshape(1, slot_count)
    col_leaf = slot_leaf.reshape(slot_count, 1)
    operands = (bordered, kernels, row_leaf, col_leaf, coupling, coupling_t, current)

    def whole(shape):
        return pl.BlockSpec(shape, lambda l, codes, scales: (0,) * len(shape))

    in_specs = [whole(x.shape) for x in operands]
    in_specs[1] = pl.BlockSpec(
        (1, near_count, components, cells, cells), lambda l, codes, scales: (l, 0, 0, 0, 0)
    )
    grid_spec = pltpu.PrefetchScalarGridSpec(
        num_scalar_prefetch=2,
        grid=(leaf_count,),
        in_specs=in_specs,
        out_specs=[
            pl.BlockSpec((1, components, cells, port_count), lambda l, codes, scales: (l, 0, 0, 0)),
            whole((slot_count, port_count)),
        ],
        scratch_shapes=[pltpu.VMEM((slot_count, port_count), jnp.float32)],
    )
    return pl.pallas_call(
        leaf_kernel,
        grid_spec=grid_spec,
        out_shape=[
            jax.ShapeDtypeStruct((leaf_count, components, cells, port_count), jnp.bfloat16),
            jax.ShapeDtypeStruct((slot_count, port_count), jnp.bfloat16),
        ],
        compiler_params=pltpu.CompilerParams(dimension_semantics=("arbitrary",)),
    )(codes, scales, *operands)


def body(stream, inductance, near_lists, filament_leaf, filament_current, filament_coupling):
    port_count = stream.shape[0]
    leaf_rows = inductance.shape[0]
    leaf_cols = inductance.shape[1]
    near_count = inductance.shape[2]
    leaf_cells = inductance.shape[4]
    leaf_count = leaf_rows * leaf_cols
    half_cols = leaf_cols * LEAF_C
    nx, ny, nz = device_grid()
    gx = lax.axis_index("gx")
    col_index = lax.axis_index("gy") * nz + lax.axis_index("gz")
    owners = nx * ny * nz

    filament_count = filament_leaf.shape[0]
    capacity = max(2, 2 * filament_count // owners)
    slot_count = owners * capacity
    plane_cols = leaf_cols * ny * nz
    leaf_row = filament_leaf // plane_cols
    leaf_col = filament_leaf % plane_cols
    owner_ids = leaf_row // leaf_rows * (ny * nz) + leaf_col // leaf_cols
    local_ids = leaf_row % leaf_rows * leaf_cols + leaf_col % leaf_cols
    owner_hits = (owner_ids[:, None] == jnp.arange(owners, dtype=jnp.int32)[None, :]).astype(
        jnp.int32
    )
    position = jnp.sum((jnp.cumsum(owner_hits, axis=0) - 1) * owner_hits, axis=1)
    target_slot = owner_ids * capacity + position
    placement_mask = target_slot[None, :] == jnp.arange(slot_count, dtype=jnp.int32)[:, None]
    placement = placement_mask.astype(jnp.bfloat16)
    row_width = 2 * leaf_cells + port_count
    rows_out = jnp.concatenate(
        [filament_coupling.reshape(filament_count, 2 * leaf_cells), filament_current], 1
    )
    sent = jnp.dot(placement, rows_out, preferred_element_type=jnp.float32).astype(jnp.bfloat16)
    sent_leaf = jnp.max(jnp.where(placement_mask, local_ids[None, :], -1), axis=1)
    leaf_row_block = jnp.pad(
        sent_leaf.astype(jnp.bfloat16).reshape(owners, 1, capacity),
        ((0, 0), (0, 0), (0, row_width - capacity)),
    )
    payload = jnp.concatenate([sent.reshape(owners, capacity, row_width), leaf_row_block], 1)
    got = lax.all_to_all(payload, AXES, split_axis=0, concat_axis=0, tiled=True)
    got_rows = got[:, :capacity].reshape(slot_count, row_width)
    got_leaf = got[:, capacity, :capacity].reshape(slot_count).astype(jnp.int32)
    got_coupling = got_rows[:, : 2 * leaf_cells]
    got_current = got_rows[:, 2 * leaf_cells :]

    window = stream_window(stream.transpose(1, 2, 0), half_cols)
    currents = plane_curl(window).astype(jnp.bfloat16)
    bordered = to_leaves(currents)
    ring_rows = jnp.arange(leaf_rows + 2, dtype=jnp.int32)
    ring_cols = jnp.arange(leaf_cols + 2, dtype=jnp.int32)
    row_ok = ((ring_rows > 0) | (gx > 0)) & ((ring_rows < leaf_rows + 1) | (gx < nx - 1))
    col_ok = ((ring_cols > 0) | (col_index > 0)) & (
        (ring_cols < leaf_cols + 1) | (col_index < ny * nz - 1)
    )
    src_row = jnp.arange(leaf_rows, dtype=jnp.int32)[:, None, None] + near_lists // 3
    src_col = jnp.arange(leaf_cols, dtype=jnp.int32)[None, :, None] + near_lists % 3
    scales = (row_ok[src_row] & col_ok[src_col]).astype(jnp.float32).reshape(-1)

    kernels = inductance.reshape(leaf_count, near_count, 2, leaf_cells, leaf_cells)
    total_field, induced = leaf_fields(
        near_lists.reshape(-1), scales, bordered, kernels, got_leaf, got_coupling, got_current
    )
    returned = lax.all_to_all(
        induced.reshape(owners, capacity, port_count), AXES, split_axis=0, concat_axis=0, tiled=True
    ).reshape(slot_count, port_count)
    filament_voltage = lax.dot_general(
        placement, returned, (((0,), (0,)), ((), ())), preferred_element_type=jnp.float32
    ).astype(jnp.bfloat16)

    grid_field = from_leaves(total_field.reshape(leaf_rows, leaf_cols, 2, leaf_cells, port_count))
    loop_voltage = field_halo(grid_field).transpose(2, 0, 1)
    return (loop_voltage, filament_voltage)


def solution(mesh):
    return jax.shard_map(
        body,
        mesh=mesh,
        in_specs=(
            P("groups", "gx", "gy"),
            P(("groups", "gx"), ("gy", "gz"), None, None, None, None),
            P(("groups", "gx"), ("gy", "gz"), None),
            P(("groups", "gx", "gy", "gz")),
            P(("groups", "gx", "gy", "gz"), None),
            P(("groups", "gx", "gy", "gz"), None, None),
        ),
        out_specs=(P("groups", "gx", ("gy", "gz")), P(("groups", "gx", "gy", "gz"), None)),
        check_vma=False,
    )
```

```python
import jax
import jax.numpy as jnp
from jax import lax
from jax.experimental import pallas as pl
from jax.experimental.pallas import tpu as pltpu
from jax.sharding import PartitionSpec as P

LEAF_R = 8
LEAF_C = 16
AXES = ("gx", "gy", "gz")


def plane_curl(padded):
    along_y = padded[1:-1, 2:] - padded[1:-1, :-2]
    along_x = padded[:-2, 1:-1] - padded[2:, 1:-1]
    return jnp.stack([along_y, along_x])


def to_leaves(grid_values):
    components, row_count, col_count, port_count = grid_values.shape
    blocks = grid_values.reshape(
        components, row_count // LEAF_R, LEAF_R, col_count // LEAF_C, LEAF_C, port_count
    )
    blocks = blocks.transpose(1, 3, 0, 2, 4, 5)
    return blocks.reshape(
        row_count // LEAF_R, col_count // LEAF_C, components, LEAF_R * LEAF_C, port_count
    )


def from_leaves(leaves):
    leaf_rows, leaf_cols, components, leaf_cells, port_count = leaves.shape
    blocks = leaves.reshape(leaf_rows, leaf_cols, components, LEAF_R, LEAF_C, port_count)
    blocks = blocks.transpose(2, 0, 3, 1, 4, 5)
    return blocks.reshape(components, leaf_rows * LEAF_R, leaf_cols * LEAF_C, port_count)


def device_grid():
    nx, ny, nz = (lax.axis_size(a) for a in AXES)
    return nx, ny, nz


def pairs_by(fn):
    nx, ny, nz = device_grid()
    out = []
    for x in range(nx):
        for y in range(ny):
            for z in range(nz):
                target = fn(x, y, z)
                if target is None:
                    continue
                tx, ty, tz = target
                if 0 <= tx < nx and 0 <= ty < ny and 0 <= tz < nz:
                    out.append(((x * ny + y) * nz + z, (tx * ny + ty) * nz + tz))
    return out


def send(value, fn):
    return lax.ppermute(value, AXES, pairs_by(fn))


def sideways(x, y, z, dx):
    nz = lax.axis_size("gz")
    if z == nz - 1:
        return (x + dx, y + 1, 0)
    if z == 0:
        return (x + dx, y - 1, nz - 1)
    return None


def stream_window(stream, half):
    gz = lax.axis_index("gz")
    rows, width = stream.shape[0], stream.shape[1]
    hr, hc = LEAF_R + 1, LEAF_C + 1
    mid_w = half + hc
    mid = lax.dynamic_slice_in_dim(stream, gz * (width - mid_w), mid_w, 1)
    side = lax.dynamic_slice_in_dim(stream, gz * (width - hc), hc, 1)
    h_got = send(side, lambda x, y, z: sideways(x, y, z, 0))
    v_top = send(mid[rows - hr :], lambda x, y, z: (x + 1, y, z))
    v_bot = send(mid[:hr], lambda x, y, z: (x - 1, y, z))
    d_top = send(side[rows - hr :], lambda x, y, z: sideways(x, y, z, 1))
    d_bot = send(side[:hr], lambda x, y, z: sideways(x, y, z, -1))
    left = gz == 0

    def join(core, edge):
        return jnp.where(left, jnp.concatenate([edge, core], 1), jnp.concatenate([core, edge], 1))

    return jnp.concatenate([join(v_top, d_top), join(mid, h_got), join(v_bot, d_bot)], 0)


def field_halo(grid_field):
    x_field = grid_field[0]
    y_field = grid_field[1]
    rows = y_field.shape[0]
    cols = x_field.shape[1]

    def step(x, y, z, dc):
        nz = lax.axis_size("gz")
        c = y * nz + z + dc
        return (x, c // nz, c % nz) if c >= 0 else None

    x_left = send(x_field[:, cols - 1 :], lambda x, y, z: step(x, y, z, 1))
    x_right = send(x_field[:, :1], lambda x, y, z: step(x, y, z, -1))
    y_top = send(y_field[rows - 1 :], lambda x, y, z: (x + 1, y, z))
    y_bot = send(y_field[:1], lambda x, y, z: (x - 1, y, z))
    x_pad = jnp.concatenate([x_left, x_field, x_right], 1).astype(jnp.float32)
    y_pad = jnp.concatenate([y_top, y_field, y_bot], 0).astype(jnp.float32)
    return x_pad[:, :-2] - x_pad[:, 2:] + (y_pad[2:] - y_pad[:-2])


def leaf_kernel(
    codes_ref, scale_ref, bord_ref, ind_ref, row_leaf_ref, col_leaf_ref, cpl_ref, cpl_t_ref,
    cur_ref, field_ref, volt_ref, acc_ref,
):
    leaf = pl.program_id(0)
    leaf_cols = bord_ref.shape[1] - 2
    near_count = ind_ref.shape[1]
    components = ind_ref.shape[2]
    cells = ind_ref.shape[3]
    row = leaf // leaf_cols
    col = leaf % leaf_cols

    @pl.when(leaf == 0)
    def _():
        acc_ref[...] = jnp.zeros_like(acc_ref)

    coupling_t = cpl_t_ref[...]
    coupling_t = jnp.where(row_leaf_ref[...] == leaf, coupling_t, jnp.zeros_like(coupling_t))
    coupling = cpl_ref[...]
    coupling = jnp.where(col_leaf_ref[...] == leaf, coupling, jnp.zeros_like(coupling))
    current = cur_ref[...]
    volt = acc_ref[...]
    for c in range(components):
        total = jnp.dot(
            coupling_t[c * cells : (c + 1) * cells], current, preferred_element_type=jnp.float32
        )
        for n in range(near_count):
            code = codes_ref[leaf * near_count + n]
            src_row = jnp.minimum(jnp.maximum(row + code // 3, 0), bord_ref.shape[0] - 1)
            src_col = jnp.minimum(jnp.maximum(col + code % 3, 0), bord_ref.shape[1] - 1)
            part = jnp.dot(
                ind_ref[0, n, c], bord_ref[src_row, src_col, c], preferred_element_type=jnp.float32
            )
            total += part * scale_ref[leaf * near_count + n]
        field_ref[0, c] = total.astype(field_ref.dtype)
        volt += jnp.dot(
            coupling[:, c * cells : (c + 1) * cells],
            bord_ref[row + 1, col + 1, c],
            preferred_element_type=jnp.float32,
        )
    acc_ref[...] = volt

    @pl.when(leaf == pl.num_programs(0) - 1)
    def _():
        volt_ref[...] = volt.astype(volt_ref.dtype)


def leaf_fields(codes, scales, bordered, kernels, slot_leaf, coupling, current):
    leaf_count, near_count, components, cells, _ = kernels.shape
    slot_count, port_count = current.shape
    coupling_t = coupling.T
    row_leaf = slot_leaf.reshape(1, slot_count)
    col_leaf = slot_leaf.reshape(slot_count, 1)
    operands = (bordered, kernels, row_leaf, col_leaf, coupling, coupling_t, current)

    def whole(shape):
        return pl.BlockSpec(shape, lambda l, codes, scales: (0,) * len(shape))

    in_specs = [whole(x.shape) for x in operands]
    in_specs[1] = pl.BlockSpec(
        (1, near_count, components, cells, cells), lambda l, codes, scales: (l, 0, 0, 0, 0)
    )
    grid_spec = pltpu.PrefetchScalarGridSpec(
        num_scalar_prefetch=2,
        grid=(leaf_count,),
        in_specs=in_specs,
        out_specs=[
            pl.BlockSpec((1, components, cells, port_count), lambda l, codes, scales: (l, 0, 0, 0)),
            whole((slot_count, port_count)),
        ],
        scratch_shapes=[pltpu.VMEM((slot_count, port_count), jnp.float32)],
    )
    return pl.pallas_call(
        leaf_kernel,
        grid_spec=grid_spec,
        out_shape=[
            jax.ShapeDtypeStruct((leaf_count, components, cells, port_count), jnp.bfloat16),
            jax.ShapeDtypeStruct((slot_count, port_count), jnp.bfloat16),
        ],
        compiler_params=pltpu.CompilerParams(dimension_semantics=("arbitrary",)),
    )(codes, scales, *operands)


def body(stream, inductance, near_lists, filament_leaf, filament_current, filament_coupling):
    port_count = stream.shape[0]
    leaf_rows = inductance.shape[0]
    leaf_cols = inductance.shape[1]
    near_count = inductance.shape[2]
    leaf_cells = inductance.shape[4]
    leaf_count = leaf_rows * leaf_cols
    half_cols = leaf_cols * LEAF_C
    nx, ny, nz = device_grid()
    gx = lax.axis_index("gx")
    col_index = lax.axis_index("gy") * nz + lax.axis_index("gz")
    owners = nx * ny * nz

    filament_count = filament_leaf.shape[0]
    capacity = max(2, 2 * filament_count // owners)
    slot_count = owners * capacity
    plane_cols = leaf_cols * ny * nz
    leaf_row = filament_leaf // plane_cols
    leaf_col = filament_leaf % plane_cols
    owner_ids = leaf_row // leaf_rows * (ny * nz) + leaf_col // leaf_cols
    local_ids = leaf_row % leaf_rows * leaf_cols + leaf_col % leaf_cols
    index = jnp.arange(filament_count, dtype=jnp.int32)
    earlier = (owner_ids[None, :] == owner_ids[:, None]) & (index[None, :] < index[:, None])
    position = jnp.sum(earlier.astype(jnp.int32), axis=1)
    target_slot = owner_ids * capacity + position
    placement_mask = target_slot[None, :] == jnp.arange(slot_count, dtype=jnp.int32)[:, None]
    placement = placement_mask.astype(jnp.bfloat16)
    row_width = 2 * leaf_cells + port_count
    rows_out = jnp.concatenate(
        [filament_coupling.reshape(filament_count, 2 * leaf_cells), filament_current], 1
    )
    sent = jnp.dot(placement, rows_out, preferred_element_type=jnp.float32).astype(jnp.bfloat16)
    sent_leaf = jnp.dot(
        placement, (local_ids + 1).astype(jnp.bfloat16), preferred_element_type=jnp.float32
    ) - 1.0
    leaf_row_block = jnp.pad(
        sent_leaf.astype(jnp.bfloat16).reshape(owners, 1, capacity),
        ((0, 0), (0, 0), (0, row_width - capacity)),
    )
    payload = jnp.concatenate([sent.reshape(owners, capacity, row_width), leaf_row_block], 1)
    got = lax.all_to_all(payload, AXES, split_axis=0, concat_axis=0, tiled=True)
    got_rows = got[:, :capacity].reshape(slot_count, row_width)
    got_leaf = got[:, capacity, :capacity].reshape(slot_count).astype(jnp.int32)
    got_coupling = got_rows[:, : 2 * leaf_cells]
    got_current = got_rows[:, 2 * leaf_cells :]

    window = stream_window(stream.transpose(1, 2, 0), half_cols)
    currents = plane_curl(window).astype(jnp.bfloat16)
    bordered = to_leaves(currents)
    ring_rows = jnp.arange(leaf_rows + 2, dtype=jnp.int32)
    ring_cols = jnp.arange(leaf_cols + 2, dtype=jnp.int32)
    row_ok = ((ring_rows > 0) | (gx > 0)) & ((ring_rows < leaf_rows + 1) | (gx < nx - 1))
    col_ok = ((ring_cols > 0) | (col_index > 0)) & (
        (ring_cols < leaf_cols + 1) | (col_index < ny * nz - 1)
    )
    src_row = jnp.arange(leaf_rows, dtype=jnp.int32)[:, None, None] + near_lists // 3
    src_col = jnp.arange(leaf_cols, dtype=jnp.int32)[None, :, None] + near_lists % 3
    scales = (row_ok[src_row] & col_ok[src_col]).astype(jnp.float32).reshape(-1)

    kernels = inductance.reshape(leaf_count, near_count, 2, leaf_cells, leaf_cells)
    total_field, induced = leaf_fields(
        near_lists.reshape(-1), scales, bordered, kernels, got_leaf, got_coupling, got_current
    )
    returned = lax.all_to_all(
        induced.reshape(owners, capacity, port_count), AXES, split_axis=0, concat_axis=0, tiled=True
    ).reshape(slot_count, port_count)
    filament_voltage = lax.dot_general(
        placement, returned, (((0,), (0,)), ((), ())), preferred_element_type=jnp.float32
    ).astype(jnp.bfloat16)

    grid_field = from_leaves(total_field.reshape(leaf_rows, leaf_cols, 2, leaf_cells, port_count))
    loop_voltage = field_halo(grid_field).transpose(2, 0, 1)
    return (loop_voltage, filament_voltage)


def solution(mesh):
    return jax.shard_map(
        body,
        mesh=mesh,
        in_specs=(
            P("groups", "gx", "gy"),
            P(("groups", "gx"), ("gy", "gz"), None, None, None, None),
            P(("groups", "gx"), ("gy", "gz"), None),
            P(("groups", "gx", "gy", "gz")),
            P(("groups", "gx", "gy", "gz"), None),
            P(("groups", "gx", "gy", "gz"), None, None),
        ),
        out_specs=(P("groups", "gx", ("gy", "gz")), P(("groups", "gx", "gy", "gz"), None)),
        check_vma=False,
    )
```

```python
import jax
import jax.numpy as jnp
from jax import lax
from jax.experimental import pallas as pl
from jax.experimental.pallas import tpu as pltpu
from jax.sharding import PartitionSpec as P

LEAF_R = 8
LEAF_C = 16
AXES = ("gx", "gy", "gz")


def plane_curl(padded):
    along_y = padded[1:-1, 2:] - padded[1:-1, :-2]
    along_x = padded[:-2, 1:-1] - padded[2:, 1:-1]
    return jnp.stack([along_y, along_x])


def to_leaves(grid_values):
    components, row_count, col_count, port_count = grid_values.shape
    blocks = grid_values.reshape(
        components, row_count // LEAF_R, LEAF_R, col_count // LEAF_C, LEAF_C, port_count
    )
    blocks = blocks.transpose(1, 3, 0, 2, 4, 5)
    return blocks.reshape(
        row_count // LEAF_R, col_count // LEAF_C, components, LEAF_R * LEAF_C, port_count
    )


def from_leaves(leaves):
    leaf_rows, leaf_cols, components, leaf_cells, port_count = leaves.shape
    blocks = leaves.reshape(leaf_rows, leaf_cols, components, LEAF_R, LEAF_C, port_count)
    blocks = blocks.transpose(2, 0, 3, 1, 4, 5)
    return blocks.reshape(components, leaf_rows * LEAF_R, leaf_cols * LEAF_C, port_count)


def device_grid():
    nx, ny, nz = (lax.axis_size(a) for a in AXES)
    return nx, ny, nz


def pairs_by(fn):
    nx, ny, nz = device_grid()
    out = []
    for x in range(nx):
        for y in range(ny):
            for z in range(nz):
                target = fn(x, y, z)
                if target is None:
                    continue
                tx, ty, tz = target
                if 0 <= tx < nx and 0 <= ty < ny and 0 <= tz < nz:
                    out.append(((x * ny + y) * nz + z, (tx * ny + ty) * nz + tz))
    return out


def send(value, fn):
    return lax.ppermute(value, AXES, pairs_by(fn))


def sideways(x, y, z, dx):
    nz = lax.axis_size("gz")
    if z == nz - 1:
        return (x + dx, y + 1, 0)
    if z == 0:
        return (x + dx, y - 1, nz - 1)
    return None


def stream_window(stream, half):
    gz = lax.axis_index("gz")
    rows, width = stream.shape[0], stream.shape[1]
    hr, hc = LEAF_R + 1, LEAF_C + 1
    mid_w = half + hc
    mid = lax.dynamic_slice_in_dim(stream, gz * (width - mid_w), mid_w, 1)
    side = lax.dynamic_slice_in_dim(stream, gz * (width - hc), hc, 1)
    h_got = send(side, lambda x, y, z: sideways(x, y, z, 0))
    v_top = send(mid[rows - hr :], lambda x, y, z: (x + 1, y, z))
    v_bot = send(mid[:hr], lambda x, y, z: (x - 1, y, z))
    d_top = send(side[rows - hr :], lambda x, y, z: sideways(x, y, z, 1))
    d_bot = send(side[:hr], lambda x, y, z: sideways(x, y, z, -1))
    left = gz == 0

    def join(core, edge):
        return jnp.where(left, jnp.concatenate([edge, core], 1), jnp.concatenate([core, edge], 1))

    return jnp.concatenate([join(v_top, d_top), join(mid, h_got), join(v_bot, d_bot)], 0)


def field_halo(grid_field):
    x_field = grid_field[0]
    y_field = grid_field[1]
    rows = y_field.shape[0]
    cols = x_field.shape[1]

    def step(x, y, z, dc):
        nz = lax.axis_size("gz")
        c = y * nz + z + dc
        return (x, c // nz, c % nz) if c >= 0 else None

    x_left = send(x_field[:, cols - 1 :], lambda x, y, z: step(x, y, z, 1))
    x_right = send(x_field[:, :1], lambda x, y, z: step(x, y, z, -1))
    y_top = send(y_field[rows - 1 :], lambda x, y, z: (x + 1, y, z))
    y_bot = send(y_field[:1], lambda x, y, z: (x - 1, y, z))
    x_pad = jnp.concatenate([x_left, x_field, x_right], 1).astype(jnp.float32)
    y_pad = jnp.concatenate([y_top, y_field, y_bot], 0).astype(jnp.float32)
    return x_pad[:, :-2] - x_pad[:, 2:] + (y_pad[2:] - y_pad[:-2])


def leaf_kernel(
    codes_ref, scale_ref, bord_ref, ind_ref, row_leaf_ref, col_leaf_ref, cpl_ref, cpl_t_ref,
    cur_ref, field_ref, volt_ref, acc_ref,
):
    leaf = pl.program_id(0)
    leaf_cols = bord_ref.shape[1] - 2
    near_count = ind_ref.shape[1]
    components = ind_ref.shape[2]
    cells = ind_ref.shape[3]
    row = leaf // leaf_cols
    col = leaf % leaf_cols

    @pl.when(leaf == 0)
    def _():
        acc_ref[...] = jnp.zeros_like(acc_ref)

    coupling_t = cpl_t_ref[...]
    coupling_t = jnp.where(row_leaf_ref[...] == leaf, coupling_t, jnp.zeros_like(coupling_t))
    coupling = cpl_ref[...]
    coupling = jnp.where(col_leaf_ref[...] == leaf, coupling, jnp.zeros_like(coupling))
    filament = jnp.dot(coupling_t, cur_ref[...], preferred_element_type=jnp.float32)
    sources = []
    for n in range(near_count):
        code = codes_ref[leaf * near_count + n]
        src_row = jnp.minimum(jnp.maximum(row + code // 3, 0), bord_ref.shape[0] - 1)
        src_col = jnp.minimum(jnp.maximum(col + code % 3, 0), bord_ref.shape[1] - 1)
        keep = scale_ref[leaf * near_count + n] > 0
        tile = bord_ref[src_row, src_col]
        sources.append(jnp.where(keep, tile, jnp.zeros_like(tile)))
    for c in range(components):
        weights = jnp.concatenate([ind_ref[0, n, c] for n in range(near_count)], axis=1)
        stacked = jnp.concatenate([s[c] for s in sources], axis=0)
        total = filament[c * cells : (c + 1) * cells] + jnp.dot(
            weights, stacked, preferred_element_type=jnp.float32
        )
        field_ref[0, c] = total.astype(field_ref.dtype)
    own = bord_ref[row + 1, col + 1].reshape(components * cells, -1)
    volt = acc_ref[...] + jnp.dot(coupling, own, preferred_element_type=jnp.float32)
    acc_ref[...] = volt

    @pl.when(leaf == pl.num_programs(0) - 1)
    def _():
        volt_ref[...] = volt.astype(volt_ref.dtype)


def leaf_fields(codes, scales, bordered, kernels, slot_leaf, coupling, current):
    leaf_count, near_count, components, cells, _ = kernels.shape
    slot_count, port_count = current.shape
    coupling_t = coupling.T
    row_leaf = slot_leaf.reshape(1, slot_count)
    col_leaf = slot_leaf.reshape(slot_count, 1)
    operands = (bordered, kernels, row_leaf, col_leaf, coupling, coupling_t, current)

    def whole(shape):
        return pl.BlockSpec(shape, lambda l, codes, scales: (0,) * len(shape))

    in_specs = [whole(x.shape) for x in operands]
    in_specs[1] = pl.BlockSpec(
        (1, near_count, components, cells, cells), lambda l, codes, scales: (l, 0, 0, 0, 0)
    )
    grid_spec = pltpu.PrefetchScalarGridSpec(
        num_scalar_prefetch=2,
        grid=(leaf_count,),
        in_specs=in_specs,
        out_specs=[
            pl.BlockSpec((1, components, cells, port_count), lambda l, codes, scales: (l, 0, 0, 0)),
            whole((slot_count, port_count)),
        ],
        scratch_shapes=[pltpu.VMEM((slot_count, port_count), jnp.float32)],
    )
    return pl.pallas_call(
        leaf_kernel,
        grid_spec=grid_spec,
        out_shape=[
            jax.ShapeDtypeStruct((leaf_count, components, cells, port_count), jnp.bfloat16),
            jax.ShapeDtypeStruct((slot_count, port_count), jnp.bfloat16),
        ],
        compiler_params=pltpu.CompilerParams(dimension_semantics=("arbitrary",)),
    )(codes, scales, *operands)


def body(stream, inductance, near_lists, filament_leaf, filament_current, filament_coupling):
    port_count = stream.shape[0]
    leaf_rows = inductance.shape[0]
    leaf_cols = inductance.shape[1]
    near_count = inductance.shape[2]
    leaf_cells = inductance.shape[4]
    leaf_count = leaf_rows * leaf_cols
    half_cols = leaf_cols * LEAF_C
    nx, ny, nz = device_grid()
    gx = lax.axis_index("gx")
    col_index = lax.axis_index("gy") * nz + lax.axis_index("gz")
    owners = nx * ny * nz

    filament_count = filament_leaf.shape[0]
    capacity = max(2, 2 * filament_count // owners)
    slot_count = owners * capacity
    plane_cols = leaf_cols * ny * nz
    leaf_row = filament_leaf // plane_cols
    leaf_col = filament_leaf % plane_cols
    owner_ids = leaf_row // leaf_rows * (ny * nz) + leaf_col // leaf_cols
    local_ids = leaf_row % leaf_rows * leaf_cols + leaf_col % leaf_cols
    index = jnp.arange(filament_count, dtype=jnp.int32)
    earlier = (owner_ids[None, :] == owner_ids[:, None]) & (index[None, :] < index[:, None])
    position = jnp.sum(earlier.astype(jnp.int32), axis=1)
    target_slot = owner_ids * capacity + position
    placement_mask = target_slot[None, :] == jnp.arange(slot_count, dtype=jnp.int32)[:, None]
    placement = placement_mask.astype(jnp.bfloat16)
    row_width = 2 * leaf_cells + port_count
    rows_out = jnp.concatenate(
        [filament_coupling.reshape(filament_count, 2 * leaf_cells), filament_current], 1
    )
    sent = jnp.dot(placement, rows_out, preferred_element_type=jnp.float32).astype(jnp.bfloat16)
    sent_leaf = jnp.dot(
        placement, (local_ids + 1).astype(jnp.bfloat16), preferred_element_type=jnp.float32
    ) - 1.0
    leaf_row_block = jnp.pad(
        sent_leaf.astype(jnp.bfloat16).reshape(owners, 1, capacity),
        ((0, 0), (0, 0), (0, row_width - capacity)),
    )
    payload = jnp.concatenate([sent.reshape(owners, capacity, row_width), leaf_row_block], 1)
    got = lax.all_to_all(payload, AXES, split_axis=0, concat_axis=0, tiled=True)
    got_rows = got[:, :capacity].reshape(slot_count, row_width)
    got_leaf = got[:, capacity, :capacity].reshape(slot_count).astype(jnp.int32)
    got_coupling = got_rows[:, : 2 * leaf_cells]
    got_current = got_rows[:, 2 * leaf_cells :]

    window = stream_window(stream.transpose(1, 2, 0), half_cols)
    currents = plane_curl(window).astype(jnp.bfloat16)
    bordered = to_leaves(currents)
    ring_rows = jnp.arange(leaf_rows + 2, dtype=jnp.int32)
    ring_cols = jnp.arange(leaf_cols + 2, dtype=jnp.int32)
    row_ok = ((ring_rows > 0) | (gx > 0)) & ((ring_rows < leaf_rows + 1) | (gx < nx - 1))
    col_ok = ((ring_cols > 0) | (col_index > 0)) & (
        (ring_cols < leaf_cols + 1) | (col_index < ny * nz - 1)
    )
    src_row = jnp.arange(leaf_rows, dtype=jnp.int32)[:, None, None] + near_lists // 3
    src_col = jnp.arange(leaf_cols, dtype=jnp.int32)[None, :, None] + near_lists % 3
    scales = (row_ok[src_row] & col_ok[src_col]).astype(jnp.float32).reshape(-1)

    kernels = inductance.reshape(leaf_count, near_count, 2, leaf_cells, leaf_cells)
    total_field, induced = leaf_fields(
        near_lists.reshape(-1), scales, bordered, kernels, got_leaf, got_coupling, got_current
    )
    returned = lax.all_to_all(
        induced.reshape(owners, capacity, port_count), AXES, split_axis=0, concat_axis=0, tiled=True
    ).reshape(slot_count, port_count)
    filament_voltage = lax.dot_general(
        placement, returned, (((0,), (0,)), ((), ())), preferred_element_type=jnp.float32
    ).astype(jnp.bfloat16)

    grid_field = from_leaves(total_field.reshape(leaf_rows, leaf_cols, 2, leaf_cells, port_count))
    loop_voltage = field_halo(grid_field).transpose(2, 0, 1)
    return (loop_voltage, filament_voltage)


def solution(mesh):
    return jax.shard_map(
        body,
        mesh=mesh,
        in_specs=(
            P("groups", "gx", "gy"),
            P(("groups", "gx"), ("gy", "gz"), None, None, None, None),
            P(("groups", "gx"), ("gy", "gz"), None),
            P(("groups", "gx", "gy", "gz")),
            P(("groups", "gx", "gy", "gz"), None),
            P(("groups", "gx", "gy", "gz"), None, None),
        ),
        out_specs=(P("groups", "gx", ("gy", "gz")), P(("groups", "gx", "gy", "gz"), None)),
        check_vma=False,
    )
```

```python
import jax
import jax.numpy as jnp
from jax import lax
from jax.experimental import pallas as pl
from jax.experimental.pallas import tpu as pltpu
from jax.sharding import PartitionSpec as P

LEAF_R = 8
LEAF_C = 16
AXES = ("gx", "gy", "gz")


def plane_curl(padded):
    along_y = padded[1:-1, 2:] - padded[1:-1, :-2]
    along_x = padded[:-2, 1:-1] - padded[2:, 1:-1]
    return jnp.stack([along_y, along_x])


def to_leaves(grid_values):
    components, row_count, col_count, port_count = grid_values.shape
    blocks = grid_values.reshape(
        components, row_count // LEAF_R, LEAF_R, col_count // LEAF_C, LEAF_C, port_count
    )
    blocks = blocks.transpose(1, 3, 0, 2, 4, 5)
    return blocks.reshape(
        row_count // LEAF_R, col_count // LEAF_C, components, LEAF_R * LEAF_C, port_count
    )


def from_leaves(leaves):
    leaf_rows, leaf_cols, components, leaf_cells, port_count = leaves.shape
    blocks = leaves.reshape(leaf_rows, leaf_cols, components, LEAF_R, LEAF_C, port_count)
    blocks = blocks.transpose(2, 0, 3, 1, 4, 5)
    return blocks.reshape(components, leaf_rows * LEAF_R, leaf_cols * LEAF_C, port_count)


def device_grid():
    nx, ny, nz = (lax.axis_size(a) for a in AXES)
    return nx, ny, nz


def pairs_by(fn):
    nx, ny, nz = device_grid()
    out = []
    for x in range(nx):
        for y in range(ny):
            for z in range(nz):
                target = fn(x, y, z)
                if target is None:
                    continue
                tx, ty, tz = target
                if 0 <= tx < nx and 0 <= ty < ny and 0 <= tz < nz:
                    out.append(((x * ny + y) * nz + z, (tx * ny + ty) * nz + tz))
    return out


def send(value, fn):
    return lax.ppermute(value, AXES, pairs_by(fn))


def sideways(x, y, z, dx):
    nz = lax.axis_size("gz")
    if z == nz - 1:
        return (x + dx, y + 1, 0)
    if z == 0:
        return (x + dx, y - 1, nz - 1)
    return None


def stream_window(stream, half):
    gz = lax.axis_index("gz")
    rows, width = stream.shape[0], stream.shape[1]
    hr, hc = LEAF_R + 1, LEAF_C + 1
    mid_w = half + hc
    mid = lax.dynamic_slice_in_dim(stream, gz * (width - mid_w), mid_w, 1)
    side = lax.dynamic_slice_in_dim(stream, gz * (width - hc), hc, 1)
    h_got = send(side, lambda x, y, z: sideways(x, y, z, 0))
    v_top = send(mid[rows - hr :], lambda x, y, z: (x + 1, y, z))
    v_bot = send(mid[:hr], lambda x, y, z: (x - 1, y, z))
    d_top = send(side[rows - hr :], lambda x, y, z: sideways(x, y, z, 1))
    d_bot = send(side[:hr], lambda x, y, z: sideways(x, y, z, -1))
    left = gz == 0

    def join(core, edge):
        return jnp.where(left, jnp.concatenate([edge, core], 1), jnp.concatenate([core, edge], 1))

    return jnp.concatenate([join(v_top, d_top), join(mid, h_got), join(v_bot, d_bot)], 0)


def field_halo(grid_field):
    x_field = grid_field[0]
    y_field = grid_field[1]
    rows = y_field.shape[0]
    cols = x_field.shape[1]

    def step(x, y, z, dc):
        nz = lax.axis_size("gz")
        c = y * nz + z + dc
        return (x, c // nz, c % nz) if c >= 0 else None

    x_left = send(x_field[:, cols - 1 :], lambda x, y, z: step(x, y, z, 1))
    x_right = send(x_field[:, :1], lambda x, y, z: step(x, y, z, -1))
    y_top = send(y_field[rows - 1 :], lambda x, y, z: (x + 1, y, z))
    y_bot = send(y_field[:1], lambda x, y, z: (x - 1, y, z))
    x_pad = jnp.concatenate([x_left, x_field, x_right], 1).astype(jnp.float32)
    y_pad = jnp.concatenate([y_top, y_field, y_bot], 0).astype(jnp.float32)
    return x_pad[:, :-2] - x_pad[:, 2:] + (y_pad[2:] - y_pad[:-2])


def leaf_kernel(
    codes_ref, scale_ref, bord_hbm, ind_hbm, row_leaf_ref, cpl_t_hbm, cur_hbm,
    field_ref, volt_ref, bord_ref, ind_ref, cpl_t_ref, cur_ref, acc_ref, sems, ind_sems,
):
    leaf_count = ind_ref.shape[0]
    leaf_cols = bord_ref.shape[1] - 2
    near_count = ind_ref.shape[1]
    cells = ind_ref.shape[3]
    first = [
        pltpu.make_async_copy(bord_hbm, bord_ref, sems.at[0]),
        pltpu.make_async_copy(cpl_t_hbm, cpl_t_ref, sems.at[1]),
        pltpu.make_async_copy(cur_hbm, cur_ref, sems.at[2]),
    ]
    for copy in first:
        copy.start()
    for l in range(leaf_count):
        pltpu.make_async_copy(ind_hbm.at[l], ind_ref.at[l], ind_sems.at[l]).start()
    acc_ref[...] = jnp.zeros_like(acc_ref)
    for copy in first:
        copy.wait()

    def one_leaf(leaf, carry):
        pltpu.make_async_copy(ind_hbm.at[leaf], ind_ref.at[leaf], ind_sems.at[leaf]).wait()
        row = leaf // leaf_cols
        col = leaf % leaf_cols
        coupling_t = cpl_t_ref[...]
        coupling_t = jnp.where(row_leaf_ref[...] == leaf, coupling_t, jnp.zeros_like(coupling_t))
        filament = jnp.dot(coupling_t, cur_ref[...], preferred_element_type=jnp.float32)
        sources = []
        for n in range(near_count):
            code = codes_ref[leaf * near_count + n]
            src_row = jnp.minimum(jnp.maximum(row + code // 3, 0), bord_ref.shape[0] - 1)
            src_col = jnp.minimum(jnp.maximum(col + code % 3, 0), bord_ref.shape[1] - 1)
            keep = scale_ref[leaf * near_count + n] > 0
            tile = bord_ref[src_row, src_col]
            sources.append(jnp.where(keep, tile, jnp.zeros_like(tile)))
        for c in range(2):
            weights = jnp.concatenate([ind_ref[leaf, n, c] for n in range(near_count)], axis=1)
            stacked = jnp.concatenate([s[c] for s in sources], axis=0)
            total = filament[c * cells : (c + 1) * cells] + jnp.dot(
                weights, stacked, preferred_element_type=jnp.float32
            )
            field_ref[leaf, c] = total.astype(field_ref.dtype)
        own = bord_ref[row + 1, col + 1].reshape(2 * cells, -1)
        acc_ref[...] += lax.dot_general(
            own, coupling_t, (((0,), (0,)), ((), ())), preferred_element_type=jnp.float32
        )
        return carry

    lax.fori_loop(0, leaf_count, one_leaf, 0)
    volt_ref[...] = acc_ref[...].astype(volt_ref.dtype)


def leaf_fields(codes, scales, bordered, kernels, slot_leaf, coupling, current):
    leaf_count, near_count, components, cells, _ = kernels.shape
    slot_count, port_count = current.shape
    coupling_t = coupling.T
    row_leaf = slot_leaf.reshape(1, slot_count)
    smem = pl.BlockSpec(memory_space=pltpu.SMEM)
    hbm = pl.BlockSpec(memory_space=pl.ANY)
    vmem = pl.BlockSpec(memory_space=pltpu.VMEM)
    return pl.pallas_call(
        leaf_kernel,
        in_specs=[smem, smem, hbm, hbm, vmem, hbm, hbm],
        out_specs=[vmem, vmem],
        out_shape=[
            jax.ShapeDtypeStruct((leaf_count, components, cells, port_count), jnp.bfloat16),
            jax.ShapeDtypeStruct((port_count, slot_count), jnp.bfloat16),
        ],
        scratch_shapes=[
            pltpu.VMEM(bordered.shape, bordered.dtype),
            pltpu.VMEM(kernels.shape, kernels.dtype),
            pltpu.VMEM(coupling_t.shape, coupling_t.dtype),
            pltpu.VMEM(current.shape, current.dtype),
            pltpu.VMEM((port_count, slot_count), jnp.float32),
            pltpu.SemaphoreType.DMA((3,)),
            pltpu.SemaphoreType.DMA((leaf_count,)),
        ],
    )(codes, scales, bordered, kernels, row_leaf, coupling_t, current)


def body(stream, inductance, near_lists, filament_leaf, filament_current, filament_coupling):
    port_count = stream.shape[0]
    leaf_rows = inductance.shape[0]
    leaf_cols = inductance.shape[1]
    near_count = inductance.shape[2]
    leaf_cells = inductance.shape[4]
    leaf_count = leaf_rows * leaf_cols
    half_cols = leaf_cols * LEAF_C
    nx, ny, nz = device_grid()
    gx = lax.axis_index("gx")
    col_index = lax.axis_index("gy") * nz + lax.axis_index("gz")
    owners = nx * ny * nz

    filament_count = filament_leaf.shape[0]
    capacity = max(2, 2 * filament_count // owners)
    slot_count = owners * capacity
    plane_cols = leaf_cols * ny * nz
    leaf_row = filament_leaf // plane_cols
    leaf_col = filament_leaf % plane_cols
    owner_ids = leaf_row // leaf_rows * (ny * nz) + leaf_col // leaf_cols
    local_ids = leaf_row % leaf_rows * leaf_cols + leaf_col % leaf_cols
    index = jnp.arange(filament_count, dtype=jnp.int32)
    earlier = (owner_ids[None, :] == owner_ids[:, None]) & (index[None, :] < index[:, None])
    position = jnp.sum(earlier.astype(jnp.int32), axis=1)
    target_slot = owner_ids * capacity + position
    placement_mask = target_slot[None, :] == jnp.arange(slot_count, dtype=jnp.int32)[:, None]
    placement = placement_mask.astype(jnp.bfloat16)
    row_width = 2 * leaf_cells + port_count
    rows_out = jnp.concatenate(
        [filament_coupling.reshape(filament_count, 2 * leaf_cells), filament_current], 1
    )
    sent = jnp.dot(placement, rows_out, preferred_element_type=jnp.float32).astype(jnp.bfloat16)
    sent_leaf = jnp.dot(
        placement, (local_ids + 1).astype(jnp.bfloat16), preferred_element_type=jnp.float32
    ) - 1.0
    leaf_row_block = jnp.pad(
        sent_leaf.astype(jnp.bfloat16).reshape(owners, 1, capacity),
        ((0, 0), (0, 0), (0, row_width - capacity)),
    )
    payload = jnp.concatenate([sent.reshape(owners, capacity, row_width), leaf_row_block], 1)
    got = lax.all_to_all(payload, AXES, split_axis=0, concat_axis=0, tiled=True)
    got_rows = got[:, :capacity].reshape(slot_count, row_width)
    got_leaf = got[:, capacity, :capacity].reshape(slot_count).astype(jnp.int32)
    got_coupling = got_rows[:, : 2 * leaf_cells]
    got_current = got_rows[:, 2 * leaf_cells :]

    window = stream_window(stream.transpose(1, 2, 0), half_cols)
    currents = plane_curl(window).astype(jnp.bfloat16)
    bordered = to_leaves(currents)
    ring_rows = jnp.arange(leaf_rows + 2, dtype=jnp.int32)
    ring_cols = jnp.arange(leaf_cols + 2, dtype=jnp.int32)
    row_ok = ((ring_rows > 0) | (gx > 0)) & ((ring_rows < leaf_rows + 1) | (gx < nx - 1))
    col_ok = ((ring_cols > 0) | (col_index > 0)) & (
        (ring_cols < leaf_cols + 1) | (col_index < ny * nz - 1)
    )
    src_row = jnp.arange(leaf_rows, dtype=jnp.int32)[:, None, None] + near_lists // 3
    src_col = jnp.arange(leaf_cols, dtype=jnp.int32)[None, :, None] + near_lists % 3
    scales = (row_ok[src_row] & col_ok[src_col]).astype(jnp.float32).reshape(-1)

    kernels = inductance.reshape(leaf_count, near_count, 2, leaf_cells, leaf_cells)
    total_field, induced = leaf_fields(
        near_lists.reshape(-1), scales, bordered, kernels, got_leaf, got_coupling, got_current
    )
    returned = lax.all_to_all(
        induced.reshape(port_count, owners, capacity), AXES, split_axis=1, concat_axis=1, tiled=True
    ).reshape(port_count, slot_count)
    filament_voltage = lax.dot_general(
        placement, returned, (((0,), (1,)), ((), ())), preferred_element_type=jnp.float32
    ).astype(jnp.bfloat16)

    grid_field = from_leaves(total_field.reshape(leaf_rows, leaf_cols, 2, leaf_cells, port_count))
    loop_voltage = field_halo(grid_field).transpose(2, 0, 1)
    return (loop_voltage, filament_voltage)


def solution(mesh):
    return jax.shard_map(
        body,
        mesh=mesh,
        in_specs=(
            P("groups", "gx", "gy"),
            P(("groups", "gx"), ("gy", "gz"), None, None, None, None),
            P(("groups", "gx"), ("gy", "gz"), None),
            P(("groups", "gx", "gy", "gz")),
            P(("groups", "gx", "gy", "gz"), None),
            P(("groups", "gx", "gy", "gz"), None, None),
        ),
        out_specs=(P("groups", "gx", ("gy", "gz")), P(("groups", "gx", "gy", "gz"), None)),
        check_vma=False,
    )
```

```python
import jax
import jax.numpy as jnp
from jax import lax
from jax.experimental import pallas as pl
from jax.experimental.pallas import tpu as pltpu
from jax.sharding import PartitionSpec as P

LEAF_R = 8
LEAF_C = 16
AXES = ("gx", "gy", "gz")


def plane_curl(padded):
    along_y = padded[1:-1, 2:] - padded[1:-1, :-2]
    along_x = padded[:-2, 1:-1] - padded[2:, 1:-1]
    return jnp.stack([along_y, along_x])


def to_leaves(grid_values):
    components, row_count, col_count, port_count = grid_values.shape
    blocks = grid_values.reshape(
        components, row_count // LEAF_R, LEAF_R, col_count // LEAF_C, LEAF_C, port_count
    )
    blocks = blocks.transpose(1, 3, 0, 2, 4, 5)
    return blocks.reshape(
        row_count // LEAF_R, col_count // LEAF_C, components, LEAF_R * LEAF_C, port_count
    )


def from_leaves(leaves):
    leaf_rows, leaf_cols, components, leaf_cells, port_count = leaves.shape
    blocks = leaves.reshape(leaf_rows, leaf_cols, components, LEAF_R, LEAF_C, port_count)
    blocks = blocks.transpose(2, 0, 3, 1, 4, 5)
    return blocks.reshape(components, leaf_rows * LEAF_R, leaf_cols * LEAF_C, port_count)


def device_grid():
    nx, ny, nz = (lax.axis_size(a) for a in AXES)
    return nx, ny, nz


def pairs_by(fn):
    nx, ny, nz = device_grid()
    out = []
    for x in range(nx):
        for y in range(ny):
            for z in range(nz):
                target = fn(x, y, z)
                if target is None:
                    continue
                tx, ty, tz = target
                if 0 <= tx < nx and 0 <= ty < ny and 0 <= tz < nz:
                    out.append(((x * ny + y) * nz + z, (tx * ny + ty) * nz + tz))
    return out


def send(value, fn):
    return lax.ppermute(value, AXES, pairs_by(fn))


def sideways(x, y, z, dx):
    nz = lax.axis_size("gz")
    if z == nz - 1:
        return (x + dx, y + 1, 0)
    if z == 0:
        return (x + dx, y - 1, nz - 1)
    return None


def stream_window(stream, half):
    gz = lax.axis_index("gz")
    rows, width = stream.shape[0], stream.shape[1]
    hr, hc = LEAF_R + 1, LEAF_C + 1
    mid_w = half + hc
    mid = lax.dynamic_slice_in_dim(stream, gz * (width - mid_w), mid_w, 1)
    side = lax.dynamic_slice_in_dim(stream, gz * (width - hc), hc, 1)
    h_got = send(side, lambda x, y, z: sideways(x, y, z, 0))
    v_top = send(mid[rows - hr :], lambda x, y, z: (x + 1, y, z))
    v_bot = send(mid[:hr], lambda x, y, z: (x - 1, y, z))
    d_top = send(side[rows - hr :], lambda x, y, z: sideways(x, y, z, 1))
    d_bot = send(side[:hr], lambda x, y, z: sideways(x, y, z, -1))

    core = jnp.concatenate([v_top, mid, v_bot], 0)
    edge = jnp.concatenate([d_top, h_got, d_bot], 0)
    both = jnp.concatenate([edge, core, edge], 1)
    return lax.dynamic_slice_in_dim(both, gz * hc, mid_w + hc, 1)


def field_halo(grid_field):
    x_field = grid_field[0]
    y_field = grid_field[1]
    rows = y_field.shape[0]
    cols = x_field.shape[1]

    def step(x, y, z, dc):
        nz = lax.axis_size("gz")
        c = y * nz + z + dc
        return (x, c // nz, c % nz) if c >= 0 else None

    x_left = send(x_field[:, cols - 1 :], lambda x, y, z: step(x, y, z, 1))
    x_right = send(x_field[:, :1], lambda x, y, z: step(x, y, z, -1))
    y_top = send(y_field[rows - 1 :], lambda x, y, z: (x + 1, y, z))
    y_bot = send(y_field[:1], lambda x, y, z: (x - 1, y, z))
    x_pad = jnp.concatenate([x_left, x_field, x_right], 1).astype(jnp.float32)
    y_pad = jnp.concatenate([y_top, y_field, y_bot], 0).astype(jnp.float32)
    return x_pad[:, :-2] - x_pad[:, 2:] + (y_pad[2:] - y_pad[:-2])


def leaf_kernel(
    codes_ref, scale_ref, bord_hbm, ind_hbm, row_leaf_ref, cpl_t_hbm, cur_hbm,
    field_ref, volt_ref, bord_ref, ind_ref, cpl_t_ref, cur_ref, acc_ref, sems, ind_sems,
):
    leaf_count = ind_ref.shape[0]
    leaf_cols = bord_ref.shape[1] - 2
    near_count = ind_ref.shape[1]
    cells = ind_ref.shape[3]
    first = [
        pltpu.make_async_copy(bord_hbm, bord_ref, sems.at[0]),
        pltpu.make_async_copy(cpl_t_hbm, cpl_t_ref, sems.at[1]),
        pltpu.make_async_copy(cur_hbm, cur_ref, sems.at[2]),
    ]
    for copy in first:
        copy.start()
    for l in range(leaf_count):
        pltpu.make_async_copy(ind_hbm.at[l], ind_ref.at[l], ind_sems.at[l]).start()
    acc_ref[...] = jnp.zeros_like(acc_ref)
    for copy in first:
        copy.wait()

    def one_leaf(leaf, carry):
        pltpu.make_async_copy(ind_hbm.at[leaf], ind_ref.at[leaf], ind_sems.at[leaf]).wait()
        row = leaf // leaf_cols
        col = leaf % leaf_cols
        coupling_t = cpl_t_ref[...]
        coupling_t = jnp.where(row_leaf_ref[...] == leaf, coupling_t, jnp.zeros_like(coupling_t))
        filament = jnp.dot(coupling_t, cur_ref[...], preferred_element_type=jnp.float32)
        sources = []
        for n in range(near_count):
            code = codes_ref[leaf, n]
            src_row = jnp.minimum(jnp.maximum(row + code // 3, 0), bord_ref.shape[0] - 1)
            src_col = jnp.minimum(jnp.maximum(col + code % 3, 0), bord_ref.shape[1] - 1)
            keep = scale_ref[leaf, n] > 0
            tile = bord_ref[src_row, src_col]
            sources.append(jnp.where(keep, tile, jnp.zeros_like(tile)))
        for c in range(2):
            weights = jnp.concatenate([ind_ref[leaf, n, c] for n in range(near_count)], axis=1)
            stacked = jnp.concatenate([s[c] for s in sources], axis=0)
            total = filament[c * cells : (c + 1) * cells] + jnp.dot(
                weights, stacked, preferred_element_type=jnp.float32
            )
            field_ref[leaf, c] = total.astype(field_ref.dtype)
        own = bord_ref[row + 1, col + 1].reshape(2 * cells, -1)
        acc_ref[...] += lax.dot_general(
            own, coupling_t, (((0,), (0,)), ((), ())), preferred_element_type=jnp.float32
        )
        return carry

    lax.fori_loop(0, leaf_count, one_leaf, 0)
    volt_ref[...] = acc_ref[...].T.astype(volt_ref.dtype)


def leaf_fields(codes, scales, bordered, kernels, slot_leaf, coupling, current):
    leaf_count, near_count, components, cells, _ = kernels.shape
    slot_count, port_count = current.shape
    coupling_t = coupling.T
    row_leaf = slot_leaf.reshape(1, slot_count)
    smem = pl.BlockSpec(memory_space=pltpu.SMEM)
    hbm = pl.BlockSpec(memory_space=pl.ANY)
    vmem = pl.BlockSpec(memory_space=pltpu.VMEM)
    return pl.pallas_call(
        leaf_kernel,
        in_specs=[smem, smem, hbm, hbm, vmem, hbm, hbm],
        out_specs=[vmem, vmem],
        out_shape=[
            jax.ShapeDtypeStruct((leaf_count, components, cells, port_count), jnp.bfloat16),
            jax.ShapeDtypeStruct((slot_count, port_count), jnp.bfloat16),
        ],
        scratch_shapes=[
            pltpu.VMEM(bordered.shape, bordered.dtype),
            pltpu.VMEM(kernels.shape, kernels.dtype),
            pltpu.VMEM(coupling_t.shape, coupling_t.dtype),
            pltpu.VMEM(current.shape, current.dtype),
            pltpu.VMEM((port_count, slot_count), jnp.float32),
            pltpu.SemaphoreType.DMA((3,)),
            pltpu.SemaphoreType.DMA((leaf_count,)),
        ],
    )(codes, scales, bordered, kernels, row_leaf, coupling_t, current)


def body(stream, inductance, near_lists, filament_leaf, filament_current, filament_coupling):
    port_count = stream.shape[0]
    leaf_rows = inductance.shape[0]
    leaf_cols = inductance.shape[1]
    near_count = inductance.shape[2]
    leaf_cells = inductance.shape[4]
    leaf_count = leaf_rows * leaf_cols
    half_cols = leaf_cols * LEAF_C
    nx, ny, nz = device_grid()
    gx = lax.axis_index("gx")
    col_index = lax.axis_index("gy") * nz + lax.axis_index("gz")
    owners = nx * ny * nz

    filament_count = filament_leaf.shape[0]
    capacity = max(2, 2 * filament_count // owners)
    slot_count = owners * capacity
    plane_cols = leaf_cols * ny * nz
    leaf_row = filament_leaf // plane_cols
    leaf_col = filament_leaf % plane_cols
    owner_ids = leaf_row // leaf_rows * (ny * nz) + leaf_col // leaf_cols
    local_ids = leaf_row % leaf_rows * leaf_cols + leaf_col % leaf_cols
    index = jnp.arange(filament_count, dtype=jnp.int32)
    earlier = (owner_ids[None, :] == owner_ids[:, None]) & (index[None, :] < index[:, None])
    position = jnp.sum(earlier.astype(jnp.int32), axis=1)
    target_slot = owner_ids * capacity + position
    placement_mask = target_slot[None, :] == jnp.arange(slot_count, dtype=jnp.int32)[:, None]
    placement = placement_mask.astype(jnp.bfloat16)
    row_width = 2 * leaf_cells + port_count
    rows_out = jnp.concatenate(
        [filament_coupling.reshape(filament_count, 2 * leaf_cells), filament_current], 1
    )
    sent = jnp.dot(placement, rows_out, preferred_element_type=jnp.float32).astype(jnp.bfloat16)
    sent_leaf = jnp.dot(
        placement, (local_ids + 1).astype(jnp.bfloat16), preferred_element_type=jnp.float32
    ) - 1.0
    leaf_row_block = jnp.pad(
        sent_leaf.astype(jnp.bfloat16).reshape(owners, 1, capacity),
        ((0, 0), (0, 0), (0, row_width - capacity)),
    )
    payload = jnp.concatenate([sent.reshape(owners, capacity, row_width), leaf_row_block], 1)
    got = lax.all_to_all(payload, AXES, split_axis=0, concat_axis=0, tiled=True)
    got_rows = got[:, :capacity].reshape(slot_count, row_width)
    got_leaf = got[:, capacity, :capacity].reshape(slot_count).astype(jnp.int32)
    got_coupling = got_rows[:, : 2 * leaf_cells]
    got_current = got_rows[:, 2 * leaf_cells :]

    window = stream_window(stream.transpose(1, 2, 0), half_cols)
    currents = plane_curl(window).astype(jnp.bfloat16)
    bordered = to_leaves(currents)
    src_row = jnp.arange(leaf_rows, dtype=jnp.int32)[:, None, None] + near_lists // 3
    src_col = jnp.arange(leaf_cols, dtype=jnp.int32)[None, :, None] + near_lists % 3
    row_ok = ((src_row > 0) | (gx > 0)) & ((src_row < leaf_rows + 1) | (gx < nx - 1))
    col_ok = ((src_col > 0) | (col_index > 0)) & (
        (src_col < leaf_cols + 1) | (col_index < ny * nz - 1)
    )
    scales = (row_ok & col_ok).astype(jnp.int32).reshape(leaf_count, near_count)

    kernels = inductance.reshape(leaf_count, near_count, 2, leaf_cells, leaf_cells)
    codes = near_lists.reshape(leaf_count, near_count)
    total_field, induced = leaf_fields(
        codes, scales, bordered, kernels, got_leaf, got_coupling, got_current
    )
    returned = lax.all_to_all(
        induced.reshape(owners, capacity, port_count), AXES, split_axis=0, concat_axis=0, tiled=True
    ).reshape(slot_count, port_count)
    filament_voltage = lax.dot_general(
        placement, returned, (((0,), (0,)), ((), ())), preferred_element_type=jnp.float32
    ).astype(jnp.bfloat16)

    grid_field = from_leaves(total_field.reshape(leaf_rows, leaf_cols, 2, leaf_cells, port_count))
    loop_voltage = field_halo(grid_field).transpose(2, 0, 1)
    return (loop_voltage, filament_voltage)


def solution(mesh):
    return jax.shard_map(
        body,
        mesh=mesh,
        in_specs=(
            P("groups", "gx", "gy"),
            P(("groups", "gx"), ("gy", "gz"), None, None, None, None),
            P(("groups", "gx"), ("gy", "gz"), None),
            P(("groups", "gx", "gy", "gz")),
            P(("groups", "gx", "gy", "gz"), None),
            P(("groups", "gx", "gy", "gz"), None, None),
        ),
        out_specs=(P("groups", "gx", ("gy", "gz")), P(("groups", "gx", "gy", "gz"), None)),
        check_vma=False,
    )
```

```python
import jax
import jax.numpy as jnp
from jax import lax
from jax.experimental import pallas as pl
from jax.experimental.pallas import tpu as pltpu
from jax.sharding import PartitionSpec as P

LEAF_R = 8
LEAF_C = 16
AXES = ("gx", "gy", "gz")


def plane_curl(padded):
    along_y = padded[1:-1, 2:] - padded[1:-1, :-2]
    along_x = padded[:-2, 1:-1] - padded[2:, 1:-1]
    return jnp.stack([along_y, along_x])


def to_leaves(grid_values):
    components, row_count, col_count, port_count = grid_values.shape
    blocks = grid_values.reshape(
        components, row_count // LEAF_R, LEAF_R, col_count // LEAF_C, LEAF_C, port_count
    )
    blocks = blocks.transpose(1, 3, 0, 2, 4, 5)
    return blocks.reshape(
        row_count // LEAF_R, col_count // LEAF_C, components, LEAF_R * LEAF_C, port_count
    )


def from_leaves(leaves):
    leaf_rows, leaf_cols, components, leaf_cells, port_count = leaves.shape
    blocks = leaves.reshape(leaf_rows, leaf_cols, components, LEAF_R, LEAF_C, port_count)
    blocks = blocks.transpose(2, 0, 3, 1, 4, 5)
    return blocks.reshape(components, leaf_rows * LEAF_R, leaf_cols * LEAF_C, port_count)


def device_grid():
    nx, ny, nz = (lax.axis_size(a) for a in AXES)
    return nx, ny, nz


def pairs_by(fn):
    nx, ny, nz = device_grid()
    out = []
    for x in range(nx):
        for y in range(ny):
            for z in range(nz):
                target = fn(x, y, z)
                if target is None:
                    continue
                tx, ty, tz = target
                if 0 <= tx < nx and 0 <= ty < ny and 0 <= tz < nz:
                    out.append(((x * ny + y) * nz + z, (tx * ny + ty) * nz + tz))
    return out


def send(value, fn):
    return lax.ppermute(value, AXES, pairs_by(fn))


def sideways(x, y, z, dx):
    nz = lax.axis_size("gz")
    if z == nz - 1:
        return (x + dx, y + 1, 0)
    if z == 0:
        return (x + dx, y - 1, nz - 1)
    return None


def stream_window(stream, half, ready):
    gz = lax.axis_index("gz")
    rows, width = stream.shape[0], stream.shape[1]
    hr, hc = LEAF_R + 1, LEAF_C + 1
    mid_w = half + hc
    mid = lax.dynamic_slice_in_dim(stream, gz * (width - mid_w), mid_w, 1)
    side = lax.dynamic_slice_in_dim(stream, gz * (width - hc), hc, 1)
    h_got = send(side, lambda x, y, z: sideways(x, y, z, 0))
    v_top = send(mid[rows - hr :], lambda x, y, z: (x + 1, y, z))
    v_bot = send(mid[:hr], lambda x, y, z: (x - 1, y, z))
    d_top = send(side[rows - hr :], lambda x, y, z: sideways(x, y, z, 1))
    d_bot = send(side[:hr], lambda x, y, z: sideways(x, y, z, -1))

    (v_top, v_bot, d_top, d_bot, h_got), ready = lax.optimization_barrier(
        ((v_top, v_bot, d_top, d_bot, h_got), ready)
    )
    core = jnp.concatenate([v_top, mid, v_bot], 0)
    edge = jnp.concatenate([d_top, h_got, d_bot], 0)
    both = jnp.concatenate([edge, core, edge], 1)
    return lax.dynamic_slice_in_dim(both, gz * hc, mid_w + hc, 1), ready


def field_halo(grid_field):
    x_field = grid_field[0]
    y_field = grid_field[1]
    rows = y_field.shape[0]
    cols = x_field.shape[1]

    def step(x, y, z, dc):
        nz = lax.axis_size("gz")
        c = y * nz + z + dc
        return (x, c // nz, c % nz) if c >= 0 else None

    x_left = send(x_field[:, cols - 1 :], lambda x, y, z: step(x, y, z, 1))
    x_right = send(x_field[:, :1], lambda x, y, z: step(x, y, z, -1))
    y_top = send(y_field[rows - 1 :], lambda x, y, z: (x + 1, y, z))
    y_bot = send(y_field[:1], lambda x, y, z: (x - 1, y, z))
    x_pad = jnp.concatenate([x_left, x_field, x_right], 1).astype(jnp.float32)
    y_pad = jnp.concatenate([y_top, y_field, y_bot], 0).astype(jnp.float32)
    return x_pad[:, :-2] - x_pad[:, 2:] + (y_pad[2:] - y_pad[:-2])


def leaf_kernel(
    codes_ref, scale_ref, bord_hbm, ind_hbm, row_leaf_ref, cpl_t_hbm, cur_hbm,
    field_ref, volt_ref, bord_ref, ind_ref, cpl_t_ref, cur_ref, acc_ref, sems, ind_sems,
):
    leaf_count = ind_ref.shape[0]
    leaf_cols = bord_ref.shape[1] - 2
    near_count = ind_ref.shape[1]
    cells = ind_ref.shape[3]
    first = [
        pltpu.make_async_copy(bord_hbm, bord_ref, sems.at[0]),
        pltpu.make_async_copy(cpl_t_hbm, cpl_t_ref, sems.at[1]),
        pltpu.make_async_copy(cur_hbm, cur_ref, sems.at[2]),
    ]
    for copy in first:
        copy.start()
    for l in range(leaf_count):
        pltpu.make_async_copy(ind_hbm.at[l], ind_ref.at[l], ind_sems.at[l]).start()
    acc_ref[...] = jnp.zeros_like(acc_ref)
    for copy in first:
        copy.wait()

    def one_leaf(leaf, carry):
        pltpu.make_async_copy(ind_hbm.at[leaf], ind_ref.at[leaf], ind_sems.at[leaf]).wait()
        row = leaf // leaf_cols
        col = leaf % leaf_cols
        coupling_t = cpl_t_ref[...]
        coupling_t = jnp.where(row_leaf_ref[...] == leaf, coupling_t, jnp.zeros_like(coupling_t))
        filament = jnp.dot(coupling_t, cur_ref[...], preferred_element_type=jnp.float32)
        sources = []
        for n in range(near_count):
            code = codes_ref[leaf, n]
            src_row = jnp.minimum(jnp.maximum(row + code // 3, 0), bord_ref.shape[0] - 1)
            src_col = jnp.minimum(jnp.maximum(col + code % 3, 0), bord_ref.shape[1] - 1)
            keep = scale_ref[leaf, n] > 0
            tile = bord_ref[src_row, src_col]
            sources.append(jnp.where(keep, tile, jnp.zeros_like(tile)))
        for c in range(2):
            weights = jnp.concatenate([ind_ref[leaf, n, c] for n in range(near_count)], axis=1)
            stacked = jnp.concatenate([s[c] for s in sources], axis=0)
            total = filament[c * cells : (c + 1) * cells] + jnp.dot(
                weights, stacked, preferred_element_type=jnp.float32
            )
            field_ref[leaf, c] = total.astype(field_ref.dtype)
        own = bord_ref[row + 1, col + 1].reshape(2 * cells, -1)
        acc_ref[...] += lax.dot_general(
            own, coupling_t, (((0,), (0,)), ((), ())), preferred_element_type=jnp.float32
        )
        return carry

    lax.fori_loop(0, leaf_count, one_leaf, 0)
    volt_ref[...] = acc_ref[...].T.astype(volt_ref.dtype)


def leaf_fields(codes, scales, bordered, kernels, row_leaf, coupling_t, current):
    leaf_count, near_count, components, cells, _ = kernels.shape
    slot_count, port_count = current.shape
    smem = pl.BlockSpec(memory_space=pltpu.SMEM)
    hbm = pl.BlockSpec(memory_space=pl.ANY)
    vmem = pl.BlockSpec(memory_space=pltpu.VMEM)
    return pl.pallas_call(
        leaf_kernel,
        in_specs=[smem, smem, hbm, hbm, vmem, hbm, hbm],
        out_specs=[vmem, vmem],
        out_shape=[
            jax.ShapeDtypeStruct((leaf_count, components, cells, port_count), jnp.bfloat16),
            jax.ShapeDtypeStruct((slot_count, port_count), jnp.bfloat16),
        ],
        scratch_shapes=[
            pltpu.VMEM(bordered.shape, bordered.dtype),
            pltpu.VMEM(kernels.shape, kernels.dtype),
            pltpu.VMEM(coupling_t.shape, coupling_t.dtype),
            pltpu.VMEM(current.shape, current.dtype),
            pltpu.VMEM((port_count, slot_count), jnp.float32),
            pltpu.SemaphoreType.DMA((3,)),
            pltpu.SemaphoreType.DMA((leaf_count,)),
        ],
    )(codes, scales, bordered, kernels, row_leaf, coupling_t, current)


def body(stream, inductance, near_lists, filament_leaf, filament_current, filament_coupling):
    port_count = stream.shape[0]
    leaf_rows = inductance.shape[0]
    leaf_cols = inductance.shape[1]
    near_count = inductance.shape[2]
    leaf_cells = inductance.shape[4]
    leaf_count = leaf_rows * leaf_cols
    half_cols = leaf_cols * LEAF_C
    nx, ny, nz = device_grid()
    gx = lax.axis_index("gx")
    col_index = lax.axis_index("gy") * nz + lax.axis_index("gz")
    owners = nx * ny * nz

    filament_count = filament_leaf.shape[0]
    capacity = max(2, 2 * filament_count // owners)
    slot_count = owners * capacity
    plane_cols = leaf_cols * ny * nz
    leaf_row = filament_leaf // plane_cols
    leaf_col = filament_leaf % plane_cols
    owner_ids = leaf_row // leaf_rows * (ny * nz) + leaf_col // leaf_cols
    local_ids = leaf_row % leaf_rows * leaf_cols + leaf_col % leaf_cols
    index = jnp.arange(filament_count, dtype=jnp.int32)
    earlier = (owner_ids[None, :] == owner_ids[:, None]) & (index[None, :] < index[:, None])
    position = jnp.sum(earlier.astype(jnp.int32), axis=1)
    target_slot = owner_ids * capacity + position
    placement_mask = target_slot[None, :] == jnp.arange(slot_count, dtype=jnp.int32)[:, None]
    placement = placement_mask.astype(jnp.bfloat16)
    row_width = 2 * leaf_cells + port_count
    rows_out = jnp.concatenate(
        [filament_coupling.reshape(filament_count, 2 * leaf_cells), filament_current], 1
    )
    sent = jnp.dot(placement, rows_out, preferred_element_type=jnp.float32).astype(jnp.bfloat16)
    sent_leaf = jnp.dot(
        placement, (local_ids + 1).astype(jnp.bfloat16), preferred_element_type=jnp.float32
    ) - 1.0
    leaf_row_block = jnp.pad(
        sent_leaf.astype(jnp.bfloat16).reshape(owners, 1, capacity),
        ((0, 0), (0, 0), (0, row_width - capacity)),
    )
    payload = jnp.concatenate([sent.reshape(owners, capacity, row_width), leaf_row_block], 1)
    got = lax.all_to_all(payload, AXES, split_axis=0, concat_axis=0, tiled=True)
    got_rows = got[:, :capacity].reshape(slot_count, row_width)
    got_leaf = got[:, capacity, :capacity].reshape(slot_count).astype(jnp.int32)
    got_coupling_t = got_rows[:, : 2 * leaf_cells].T
    got_current = got_rows[:, 2 * leaf_cells :]
    got_leaf = got_leaf.reshape(1, slot_count)

    window, (got_leaf, got_coupling_t, got_current) = stream_window(
        stream.transpose(1, 2, 0), half_cols, (got_leaf, got_coupling_t, got_current)
    )
    currents = plane_curl(window).astype(jnp.bfloat16)
    bordered = to_leaves(currents)
    src_row = jnp.arange(leaf_rows, dtype=jnp.int32)[:, None, None] + near_lists // 3
    src_col = jnp.arange(leaf_cols, dtype=jnp.int32)[None, :, None] + near_lists % 3
    row_ok = ((src_row > 0) | (gx > 0)) & ((src_row < leaf_rows + 1) | (gx < nx - 1))
    col_ok = ((src_col > 0) | (col_index > 0)) & (
        (src_col < leaf_cols + 1) | (col_index < ny * nz - 1)
    )
    scales = (row_ok & col_ok).astype(jnp.int32).reshape(leaf_count, near_count)

    kernels = inductance.reshape(leaf_count, near_count, 2, leaf_cells, leaf_cells)
    codes = near_lists.reshape(leaf_count, near_count)
    total_field, induced = leaf_fields(
        codes, scales, bordered, kernels, got_leaf, got_coupling_t, got_current
    )
    returned = lax.all_to_all(
        induced.reshape(owners, capacity, port_count), AXES, split_axis=0, concat_axis=0, tiled=True
    ).reshape(slot_count, port_count)
    filament_voltage = lax.dot_general(
        placement, returned, (((0,), (0,)), ((), ())), preferred_element_type=jnp.float32
    ).astype(jnp.bfloat16)

    grid_field = from_leaves(total_field.reshape(leaf_rows, leaf_cols, 2, leaf_cells, port_count))
    loop_voltage = field_halo(grid_field).transpose(2, 0, 1)
    return (loop_voltage, filament_voltage)


def solution(mesh):
    return jax.shard_map(
        body,
        mesh=mesh,
        in_specs=(
            P("groups", "gx", "gy"),
            P(("groups", "gx"), ("gy", "gz"), None, None, None, None),
            P(("groups", "gx"), ("gy", "gz"), None),
            P(("groups", "gx", "gy", "gz")),
            P(("groups", "gx", "gy", "gz"), None),
            P(("groups", "gx", "gy", "gz"), None, None),
        ),
        out_specs=(P("groups", "gx", ("gy", "gz")), P(("groups", "gx", "gy", "gz"), None)),
        check_vma=False,
    )
```

```python
import jax
import jax.numpy as jnp
from jax import lax
from jax.experimental import pallas as pl
from jax.experimental.pallas import tpu as pltpu
from jax.sharding import PartitionSpec as P

LEAF_R = 8
LEAF_C = 16
AXES = ("gx", "gy", "gz")


def plane_curl(padded):
    along_y = padded[1:-1, 2:] - padded[1:-1, :-2]
    along_x = padded[:-2, 1:-1] - padded[2:, 1:-1]
    return jnp.stack([along_y, along_x])


def to_leaves(grid_values):
    components, row_count, col_count, port_count = grid_values.shape
    blocks = grid_values.reshape(
        components, row_count // LEAF_R, LEAF_R, col_count // LEAF_C, LEAF_C, port_count
    )
    blocks = blocks.transpose(1, 3, 0, 2, 4, 5)
    return blocks.reshape(
        row_count // LEAF_R, col_count // LEAF_C, components, LEAF_R * LEAF_C, port_count
    )


def from_leaves(leaves):
    leaf_rows, leaf_cols, components, leaf_cells, port_count = leaves.shape
    blocks = leaves.reshape(leaf_rows, leaf_cols, components, LEAF_R, LEAF_C, port_count)
    blocks = blocks.transpose(2, 0, 3, 1, 4, 5)
    return blocks.reshape(components, leaf_rows * LEAF_R, leaf_cols * LEAF_C, port_count)


def device_grid():
    nx, ny, nz = (lax.axis_size(a) for a in AXES)
    return nx, ny, nz


def pairs_by(fn):
    nx, ny, nz = device_grid()
    out = []
    for x in range(nx):
        for y in range(ny):
            for z in range(nz):
                target = fn(x, y, z)
                if target is None:
                    continue
                tx, ty, tz = target
                if 0 <= tx < nx and 0 <= ty < ny and 0 <= tz < nz:
                    out.append(((x * ny + y) * nz + z, (tx * ny + ty) * nz + tz))
    return out


def send(value, fn):
    return lax.ppermute(value, AXES, pairs_by(fn))


def sideways(x, y, z, dx):
    nz = lax.axis_size("gz")
    if z == nz - 1:
        return (x + dx, y + 1, 0)
    if z == 0:
        return (x + dx, y - 1, nz - 1)
    return None


def stream_window(stream, half, ready):
    gz = lax.axis_index("gz")
    rows, width = stream.shape[0], stream.shape[1]
    hr, hc = LEAF_R + 1, LEAF_C + 1
    mid_w = half + hc
    mid = lax.dynamic_slice_in_dim(stream, gz * (width - mid_w), mid_w, 1)
    side = lax.dynamic_slice_in_dim(stream, gz * (width - hc), hc, 1)
    h_got = send(side, lambda x, y, z: sideways(x, y, z, 0))
    v_top = send(mid[rows - hr :], lambda x, y, z: (x + 1, y, z))
    v_bot = send(mid[:hr], lambda x, y, z: (x - 1, y, z))
    d_top = send(side[rows - hr :], lambda x, y, z: sideways(x, y, z, 1))
    d_bot = send(side[:hr], lambda x, y, z: sideways(x, y, z, -1))

    (v_top, v_bot, d_top, d_bot, h_got), ready = lax.optimization_barrier(
        ((v_top, v_bot, d_top, d_bot, h_got), ready)
    )
    core = jnp.concatenate([v_top, mid, v_bot], 0)
    edge = jnp.concatenate([d_top, h_got, d_bot], 0)
    both = jnp.concatenate([edge, core, edge], 1)
    return lax.dynamic_slice_in_dim(both, gz * hc, mid_w + hc, 1), ready


def field_halo(grid_field):
    x_field = grid_field[0]
    y_field = grid_field[1]
    rows = y_field.shape[0]
    cols = x_field.shape[1]

    def step(x, y, z, dc):
        nz = lax.axis_size("gz")
        c = y * nz + z + dc
        return (x, c // nz, c % nz) if c >= 0 else None

    x_left = send(x_field[:, cols - 1 :], lambda x, y, z: step(x, y, z, 1))
    x_right = send(x_field[:, :1], lambda x, y, z: step(x, y, z, -1))
    y_top = send(y_field[rows - 1 :], lambda x, y, z: (x + 1, y, z))
    y_bot = send(y_field[:1], lambda x, y, z: (x - 1, y, z))
    x_pad = jnp.concatenate([x_left, x_field, x_right], 1).astype(jnp.float32)
    y_pad = jnp.concatenate([y_top, y_field, y_bot], 0).astype(jnp.float32)
    return x_pad[:, :-2] - x_pad[:, 2:] + (y_pad[2:] - y_pad[:-2])


def leaf_kernel(
    codes_ref, scale_ref, bord_hbm, ind_hbm, row_leaf_ref, cpl_t_hbm, cur_hbm,
    field_ref, volt_ref, bord_ref, ind_ref, cpl_t_ref, cur_ref, acc_ref, sems, ind_sems,
):
    leaf_count = ind_ref.shape[0]
    leaf_cols = bord_ref.shape[1] - 2
    near_count = ind_ref.shape[1]
    cells = ind_ref.shape[3]
    first = [
        pltpu.make_async_copy(bord_hbm, bord_ref, sems.at[0]),
        pltpu.make_async_copy(cpl_t_hbm, cpl_t_ref, sems.at[1]),
        pltpu.make_async_copy(cur_hbm, cur_ref, sems.at[2]),
    ]
    for copy in first:
        copy.start()
    for l in range(leaf_count):
        pltpu.make_async_copy(ind_hbm.at[l], ind_ref.at[l], ind_sems.at[l]).start()
    acc_ref[...] = jnp.zeros_like(acc_ref)
    for copy in first:
        copy.wait()

    def one_leaf(leaf, carry):
        pltpu.make_async_copy(ind_hbm.at[leaf], ind_ref.at[leaf], ind_sems.at[leaf]).wait()
        row = leaf // leaf_cols
        col = leaf % leaf_cols
        coupling_t = cpl_t_ref[...]
        coupling_t = jnp.where(row_leaf_ref[...] == leaf, coupling_t, jnp.zeros_like(coupling_t))
        filament = jnp.dot(coupling_t, cur_ref[...], preferred_element_type=jnp.float32)
        sources = []
        for n in range(near_count):
            code = codes_ref[leaf, n]
            src_row = jnp.minimum(jnp.maximum(row + code // 3, 0), bord_ref.shape[0] - 1)
            src_col = jnp.minimum(jnp.maximum(col + code % 3, 0), bord_ref.shape[1] - 1)
            keep = scale_ref[leaf, n] > 0
            tile = bord_ref[src_row, src_col]
            sources.append(jnp.where(keep, tile, jnp.zeros_like(tile)))
        for c in range(2):
            weights = jnp.concatenate([ind_ref[leaf, n, c] for n in range(near_count)], axis=1)
            stacked = jnp.concatenate([s[c] for s in sources], axis=0)
            total = filament[c * cells : (c + 1) * cells] + jnp.dot(
                weights, stacked, preferred_element_type=jnp.float32
            )
            field_ref[c, pl.ds(row * LEAF_R, LEAF_R), pl.ds(pl.multiple_of(col * LEAF_C, LEAF_C), LEAF_C)] = (
                total.reshape(LEAF_R, LEAF_C, -1).astype(field_ref.dtype)
            )
        own = bord_ref[row + 1, col + 1].reshape(2 * cells, -1)
        acc_ref[...] += lax.dot_general(
            own, coupling_t, (((0,), (0,)), ((), ())), preferred_element_type=jnp.float32
        )
        return carry

    lax.fori_loop(0, leaf_count, one_leaf, 0)
    volt_ref[...] = acc_ref[...].T.astype(volt_ref.dtype)


def leaf_fields(codes, scales, bordered, kernels, row_leaf, coupling_t, current):
    leaf_count, near_count, components, cells, _ = kernels.shape
    leaf_rows = bordered.shape[0] - 2
    leaf_cols = bordered.shape[1] - 2
    slot_count, port_count = current.shape
    smem = pl.BlockSpec(memory_space=pltpu.SMEM)
    hbm = pl.BlockSpec(memory_space=pl.ANY)
    vmem = pl.BlockSpec(memory_space=pltpu.VMEM)
    return pl.pallas_call(
        leaf_kernel,
        in_specs=[smem, smem, hbm, hbm, vmem, hbm, hbm],
        out_specs=[vmem, vmem],
        out_shape=[
            jax.ShapeDtypeStruct(
                (components, leaf_rows * LEAF_R, leaf_cols * LEAF_C, port_count), jnp.bfloat16
            ),
            jax.ShapeDtypeStruct((slot_count, port_count), jnp.bfloat16),
        ],
        scratch_shapes=[
            pltpu.VMEM(bordered.shape, bordered.dtype),
            pltpu.VMEM(kernels.shape, kernels.dtype),
            pltpu.VMEM(coupling_t.shape, coupling_t.dtype),
            pltpu.VMEM(current.shape, current.dtype),
            pltpu.VMEM((port_count, slot_count), jnp.float32),
            pltpu.SemaphoreType.DMA((3,)),
            pltpu.SemaphoreType.DMA((leaf_count,)),
        ],
    )(codes, scales, bordered, kernels, row_leaf, coupling_t, current)


def body(stream, inductance, near_lists, filament_leaf, filament_current, filament_coupling):
    port_count = stream.shape[0]
    leaf_rows = inductance.shape[0]
    leaf_cols = inductance.shape[1]
    near_count = inductance.shape[2]
    leaf_cells = inductance.shape[4]
    leaf_count = leaf_rows * leaf_cols
    half_cols = leaf_cols * LEAF_C
    nx, ny, nz = device_grid()
    gx = lax.axis_index("gx")
    col_index = lax.axis_index("gy") * nz + lax.axis_index("gz")
    owners = nx * ny * nz

    filament_count = filament_leaf.shape[0]
    capacity = max(2, 2 * filament_count // owners)
    slot_count = owners * capacity
    plane_cols = leaf_cols * ny * nz
    leaf_row = filament_leaf // plane_cols
    leaf_col = filament_leaf % plane_cols
    owner_ids = leaf_row // leaf_rows * (ny * nz) + leaf_col // leaf_cols
    local_ids = leaf_row % leaf_rows * leaf_cols + leaf_col % leaf_cols
    index = jnp.arange(filament_count, dtype=jnp.int32)
    earlier = (owner_ids[None, :] == owner_ids[:, None]) & (index[None, :] < index[:, None])
    position = jnp.sum(earlier.astype(jnp.int32), axis=1)
    target_slot = owner_ids * capacity + position
    placement_mask = target_slot[None, :] == jnp.arange(slot_count, dtype=jnp.int32)[:, None]
    placement = placement_mask.astype(jnp.bfloat16)
    row_width = 2 * leaf_cells + port_count
    rows_out = jnp.concatenate(
        [filament_coupling.reshape(filament_count, 2 * leaf_cells), filament_current], 1
    )
    sent = jnp.dot(placement, rows_out, preferred_element_type=jnp.float32).astype(jnp.bfloat16)
    sent_leaf = jnp.dot(
        placement, (local_ids + 1).astype(jnp.bfloat16), preferred_element_type=jnp.float32
    ) - 1.0
    leaf_row_block = jnp.pad(
        sent_leaf.astype(jnp.bfloat16).reshape(owners, 1, capacity),
        ((0, 0), (0, 0), (0, row_width - capacity)),
    )
    payload = jnp.concatenate([sent.reshape(owners, capacity, row_width), leaf_row_block], 1)
    got = lax.all_to_all(payload, AXES, split_axis=0, concat_axis=0, tiled=True)
    got_rows = got[:, :capacity].reshape(slot_count, row_width)
    got_leaf = got[:, capacity, :capacity].reshape(slot_count).astype(jnp.int32)
    got_coupling_t = got_rows[:, : 2 * leaf_cells].T
    got_current = got_rows[:, 2 * leaf_cells :]
    got_leaf = got_leaf.reshape(1, slot_count)

    window, (got_leaf, got_coupling_t, got_current) = stream_window(
        stream.transpose(1, 2, 0), half_cols, (got_leaf, got_coupling_t, got_current)
    )
    currents = plane_curl(window).astype(jnp.bfloat16)
    bordered = to_leaves(currents)
    src_row = jnp.arange(leaf_rows, dtype=jnp.int32)[:, None, None] + near_lists // 3
    src_col = jnp.arange(leaf_cols, dtype=jnp.int32)[None, :, None] + near_lists % 3
    row_ok = ((src_row > 0) | (gx > 0)) & ((src_row < leaf_rows + 1) | (gx < nx - 1))
    col_ok = ((src_col > 0) | (col_index > 0)) & (
        (src_col < leaf_cols + 1) | (col_index < ny * nz - 1)
    )
    scales = (row_ok & col_ok).astype(jnp.int32).reshape(leaf_count, near_count)

    kernels = inductance.reshape(leaf_count, near_count, 2, leaf_cells, leaf_cells)
    codes = near_lists.reshape(leaf_count, near_count)
    total_field, induced = leaf_fields(
        codes, scales, bordered, kernels, got_leaf, got_coupling_t, got_current
    )
    returned = lax.all_to_all(
        induced.reshape(owners, capacity, port_count), AXES, split_axis=0, concat_axis=0, tiled=True
    ).reshape(slot_count, port_count)
    filament_voltage = lax.dot_general(
        placement, returned, (((0,), (0,)), ((), ())), preferred_element_type=jnp.float32
    ).astype(jnp.bfloat16)

    loop_voltage = field_halo(total_field).transpose(2, 0, 1)
    return (loop_voltage, filament_voltage)


def solution(mesh):
    return jax.shard_map(
        body,
        mesh=mesh,
        in_specs=(
            P("groups", "gx", "gy"),
            P(("groups", "gx"), ("gy", "gz"), None, None, None, None),
            P(("groups", "gx"), ("gy", "gz"), None),
            P(("groups", "gx", "gy", "gz")),
            P(("groups", "gx", "gy", "gz"), None),
            P(("groups", "gx", "gy", "gz"), None, None),
        ),
        out_specs=(P("groups", "gx", ("gy", "gz")), P(("groups", "gx", "gy", "gz"), None)),
        check_vma=False,
    )
```

```python
import jax
import jax.numpy as jnp
from jax import lax
from jax.experimental import pallas as pl
from jax.experimental.pallas import tpu as pltpu
from jax.sharding import PartitionSpec as P

LEAF_R = 8
LEAF_C = 16
AXES = ("gx", "gy", "gz")


def plane_curl(padded):
    along_y = padded[1:-1, 2:] - padded[1:-1, :-2]
    along_x = padded[:-2, 1:-1] - padded[2:, 1:-1]
    return jnp.stack([along_y, along_x])


def to_leaves(grid_values):
    components, row_count, col_count, port_count = grid_values.shape
    blocks = grid_values.reshape(
        components, row_count // LEAF_R, LEAF_R, col_count // LEAF_C, LEAF_C, port_count
    )
    blocks = blocks.transpose(1, 3, 0, 2, 4, 5)
    return blocks.reshape(
        row_count // LEAF_R, col_count // LEAF_C, components, LEAF_R * LEAF_C, port_count
    )


def from_leaves(leaves):
    leaf_rows, leaf_cols, components, leaf_cells, port_count = leaves.shape
    blocks = leaves.reshape(leaf_rows, leaf_cols, components, LEAF_R, LEAF_C, port_count)
    blocks = blocks.transpose(2, 0, 3, 1, 4, 5)
    return blocks.reshape(components, leaf_rows * LEAF_R, leaf_cols * LEAF_C, port_count)


def device_grid():
    nx, ny, nz = (lax.axis_size(a) for a in AXES)
    return nx, ny, nz


def pairs_by(fn):
    nx, ny, nz = device_grid()
    out = []
    for x in range(nx):
        for y in range(ny):
            for z in range(nz):
                target = fn(x, y, z)
                if target is None:
                    continue
                tx, ty, tz = target
                if 0 <= tx < nx and 0 <= ty < ny and 0 <= tz < nz:
                    out.append(((x * ny + y) * nz + z, (tx * ny + ty) * nz + tz))
    return out


def send(value, fn):
    return lax.ppermute(value, AXES, pairs_by(fn))


def sideways(x, y, z, dx):
    nz = lax.axis_size("gz")
    if z == nz - 1:
        return (x + dx, y + 1, 0)
    if z == 0:
        return (x + dx, y - 1, nz - 1)
    return None


def stream_window(stream, half, ready):
    gz = lax.axis_index("gz")
    rows, width = stream.shape[0], stream.shape[1]
    hr, hc = LEAF_R + 1, LEAF_C + 1
    mid_w = half + hc
    mid = lax.dynamic_slice_in_dim(stream, gz * (width - mid_w), mid_w, 1)
    side = lax.dynamic_slice_in_dim(stream, gz * (width - hc), hc, 1)
    h_got = send(side, lambda x, y, z: sideways(x, y, z, 0))
    v_top = send(mid[rows - hr :], lambda x, y, z: (x + 1, y, z))
    v_bot = send(mid[:hr], lambda x, y, z: (x - 1, y, z))
    d_top = send(side[rows - hr :], lambda x, y, z: sideways(x, y, z, 1))
    d_bot = send(side[:hr], lambda x, y, z: sideways(x, y, z, -1))

    (v_top, v_bot, d_top, d_bot, h_got), ready = lax.optimization_barrier(
        ((v_top, v_bot, d_top, d_bot, h_got), ready)
    )
    core = jnp.concatenate([v_top, mid, v_bot], 0)
    edge = jnp.concatenate([d_top, h_got, d_bot], 0)
    both = jnp.concatenate([edge, core, edge], 1)
    return lax.dynamic_slice_in_dim(both, gz * hc, mid_w + hc, 1), ready


def field_halo(grid_field):
    x_field = grid_field[0]
    y_field = grid_field[1]
    rows = y_field.shape[0]
    cols = x_field.shape[1]

    def step(x, y, z, dc):
        nz = lax.axis_size("gz")
        c = y * nz + z + dc
        return (x, c // nz, c % nz) if c >= 0 else None

    x_left = send(x_field[:, cols - 1 :], lambda x, y, z: step(x, y, z, 1))
    x_right = send(x_field[:, :1], lambda x, y, z: step(x, y, z, -1))
    y_top = send(y_field[rows - 1 :], lambda x, y, z: (x + 1, y, z))
    y_bot = send(y_field[:1], lambda x, y, z: (x - 1, y, z))
    x_pad = jnp.concatenate([x_left, x_field, x_right], 1).astype(jnp.float32)
    y_pad = jnp.concatenate([y_top, y_field, y_bot], 0).astype(jnp.float32)
    return x_pad[:, :-2] - x_pad[:, 2:] + (y_pad[2:] - y_pad[:-2])


def leaf_kernel(
    codes_ref, scale_ref, bord_hbm, ind_hbm, row_leaf_ref, cpl_t_hbm, cur_hbm,
    field_ref, volt_ref, bord_ref, ind_ref, cpl_t_ref, cur_ref, acc_ref, sems, ind_sems,
):
    leaf_count = ind_ref.shape[0]
    leaf_rows = bord_ref.shape[1] // LEAF_R - 2
    leaf_cols = bord_ref.shape[2] // LEAF_C - 2
    near_count = ind_ref.shape[1]
    cells = ind_ref.shape[3]

    def tile(r, q):
        rows = pl.ds(r * LEAF_R, LEAF_R)
        cols = pl.ds(pl.multiple_of(q * LEAF_C, LEAF_C), LEAF_C)
        return bord_ref[:, rows, cols, :].reshape(2, cells, -1)

    first = [
        pltpu.make_async_copy(bord_hbm, bord_ref, sems.at[0]),
        pltpu.make_async_copy(cpl_t_hbm, cpl_t_ref, sems.at[1]),
        pltpu.make_async_copy(cur_hbm, cur_ref, sems.at[2]),
    ]
    for copy in first:
        copy.start()
    for l in range(leaf_count):
        pltpu.make_async_copy(ind_hbm.at[l], ind_ref.at[l], ind_sems.at[l]).start()
    acc_ref[...] = jnp.zeros_like(acc_ref)
    for copy in first:
        copy.wait()

    def one_leaf(leaf, carry):
        pltpu.make_async_copy(ind_hbm.at[leaf], ind_ref.at[leaf], ind_sems.at[leaf]).wait()
        row = leaf // leaf_cols
        col = leaf % leaf_cols
        coupling_t = cpl_t_ref[...]
        coupling_t = jnp.where(row_leaf_ref[...] == leaf, coupling_t, jnp.zeros_like(coupling_t))
        filament = jnp.dot(coupling_t, cur_ref[...], preferred_element_type=jnp.float32)
        sources = []
        for n in range(near_count):
            code = codes_ref[leaf, n]
            src_row = jnp.minimum(jnp.maximum(row + code // 3, 0), leaf_rows + 1)
            src_col = jnp.minimum(jnp.maximum(col + code % 3, 0), leaf_cols + 1)
            keep = scale_ref[leaf, n] > 0
            block = tile(src_row, src_col)
            sources.append(jnp.where(keep, block, jnp.zeros_like(block)))
        for c in range(2):
            weights = jnp.concatenate([ind_ref[leaf, n, c] for n in range(near_count)], axis=1)
            stacked = jnp.concatenate([s[c] for s in sources], axis=0)
            total = filament[c * cells : (c + 1) * cells] + jnp.dot(
                weights, stacked, preferred_element_type=jnp.float32
            )
            field_ref[c, pl.ds(row * LEAF_R, LEAF_R), pl.ds(pl.multiple_of(col * LEAF_C, LEAF_C), LEAF_C)] = (
                total.reshape(LEAF_R, LEAF_C, -1).astype(field_ref.dtype)
            )
        own = tile(row + 1, col + 1).reshape(2 * cells, -1)
        acc_ref[...] += lax.dot_general(
            own, coupling_t, (((0,), (0,)), ((), ())), preferred_element_type=jnp.float32
        )
        return carry

    lax.fori_loop(0, leaf_count, one_leaf, 0)
    volt_ref[...] = acc_ref[...].T.astype(volt_ref.dtype)


def leaf_fields(codes, scales, bordered, kernels, row_leaf, coupling_t, current):
    leaf_count, near_count, components, cells, _ = kernels.shape
    leaf_rows = bordered.shape[1] // LEAF_R - 2
    leaf_cols = bordered.shape[2] // LEAF_C - 2
    slot_count, port_count = current.shape
    smem = pl.BlockSpec(memory_space=pltpu.SMEM)
    hbm = pl.BlockSpec(memory_space=pl.ANY)
    vmem = pl.BlockSpec(memory_space=pltpu.VMEM)
    return pl.pallas_call(
        leaf_kernel,
        in_specs=[smem, smem, hbm, hbm, vmem, hbm, hbm],
        out_specs=[vmem, vmem],
        out_shape=[
            jax.ShapeDtypeStruct(
                (components, leaf_rows * LEAF_R, leaf_cols * LEAF_C, port_count), jnp.bfloat16
            ),
            jax.ShapeDtypeStruct((slot_count, port_count), jnp.bfloat16),
        ],
        scratch_shapes=[
            pltpu.VMEM(bordered.shape, bordered.dtype),
            pltpu.VMEM(kernels.shape, kernels.dtype),
            pltpu.VMEM(coupling_t.shape, coupling_t.dtype),
            pltpu.VMEM(current.shape, current.dtype),
            pltpu.VMEM((port_count, slot_count), jnp.float32),
            pltpu.SemaphoreType.DMA((3,)),
            pltpu.SemaphoreType.DMA((leaf_count,)),
        ],
    )(codes, scales, bordered, kernels, row_leaf, coupling_t, current)


def body(stream, inductance, near_lists, filament_leaf, filament_current, filament_coupling):
    port_count = stream.shape[0]
    leaf_rows = inductance.shape[0]
    leaf_cols = inductance.shape[1]
    near_count = inductance.shape[2]
    leaf_cells = inductance.shape[4]
    leaf_count = leaf_rows * leaf_cols
    half_cols = leaf_cols * LEAF_C
    nx, ny, nz = device_grid()
    gx = lax.axis_index("gx")
    col_index = lax.axis_index("gy") * nz + lax.axis_index("gz")
    owners = nx * ny * nz

    filament_count = filament_leaf.shape[0]
    capacity = max(2, 2 * filament_count // owners)
    slot_count = owners * capacity
    plane_cols = leaf_cols * ny * nz
    leaf_row = filament_leaf // plane_cols
    leaf_col = filament_leaf % plane_cols
    owner_ids = leaf_row // leaf_rows * (ny * nz) + leaf_col // leaf_cols
    local_ids = leaf_row % leaf_rows * leaf_cols + leaf_col % leaf_cols
    index = jnp.arange(filament_count, dtype=jnp.int32)
    earlier = (owner_ids[None, :] == owner_ids[:, None]) & (index[None, :] < index[:, None])
    position = jnp.sum(earlier.astype(jnp.int32), axis=1)
    target_slot = owner_ids * capacity + position
    placement_mask = target_slot[None, :] == jnp.arange(slot_count, dtype=jnp.int32)[:, None]
    placement = placement_mask.astype(jnp.bfloat16)
    row_width = 2 * leaf_cells + port_count
    rows_out = jnp.concatenate(
        [filament_coupling.reshape(filament_count, 2 * leaf_cells), filament_current], 1
    )
    sent = jnp.dot(placement, rows_out, preferred_element_type=jnp.float32).astype(jnp.bfloat16)
    sent_leaf = jnp.dot(
        placement, (local_ids + 1).astype(jnp.bfloat16), preferred_element_type=jnp.float32
    ) - 1.0
    leaf_row_block = jnp.pad(
        sent_leaf.astype(jnp.bfloat16).reshape(owners, 1, capacity),
        ((0, 0), (0, 0), (0, row_width - capacity)),
    )
    payload = jnp.concatenate([sent.reshape(owners, capacity, row_width), leaf_row_block], 1)
    got = lax.all_to_all(payload, AXES, split_axis=0, concat_axis=0, tiled=True)
    got_rows = got[:, :capacity].reshape(slot_count, row_width)
    got_leaf = got[:, capacity, :capacity].reshape(slot_count).astype(jnp.int32)
    got_coupling_t = got_rows[:, : 2 * leaf_cells].T
    got_current = got_rows[:, 2 * leaf_cells :]
    got_leaf = got_leaf.reshape(1, slot_count)

    window, (got_leaf, got_coupling_t, got_current) = stream_window(
        stream.transpose(1, 2, 0), half_cols, (got_leaf, got_coupling_t, got_current)
    )
    bordered = plane_curl(window).astype(jnp.bfloat16)
    src_row = jnp.arange(leaf_rows, dtype=jnp.int32)[:, None, None] + near_lists // 3
    src_col = jnp.arange(leaf_cols, dtype=jnp.int32)[None, :, None] + near_lists % 3
    row_ok = ((src_row > 0) | (gx > 0)) & ((src_row < leaf_rows + 1) | (gx < nx - 1))
    col_ok = ((src_col > 0) | (col_index > 0)) & (
        (src_col < leaf_cols + 1) | (col_index < ny * nz - 1)
    )
    scales = (row_ok & col_ok).astype(jnp.int32).reshape(leaf_count, near_count)

    kernels = inductance.reshape(leaf_count, near_count, 2, leaf_cells, leaf_cells)
    codes = near_lists.reshape(leaf_count, near_count)
    total_field, induced = leaf_fields(
        codes, scales, bordered, kernels, got_leaf, got_coupling_t, got_current
    )
    returned = lax.all_to_all(
        induced.reshape(owners, capacity, port_count), AXES, split_axis=0, concat_axis=0, tiled=True
    ).reshape(slot_count, port_count)
    filament_voltage = lax.dot_general(
        placement, returned, (((0,), (0,)), ((), ())), preferred_element_type=jnp.float32
    ).astype(jnp.bfloat16)

    loop_voltage = field_halo(total_field).transpose(2, 0, 1)
    return (loop_voltage, filament_voltage)


def solution(mesh):
    return jax.shard_map(
        body,
        mesh=mesh,
        in_specs=(
            P("groups", "gx", "gy"),
            P(("groups", "gx"), ("gy", "gz"), None, None, None, None),
            P(("groups", "gx"), ("gy", "gz"), None),
            P(("groups", "gx", "gy", "gz")),
            P(("groups", "gx", "gy", "gz"), None),
            P(("groups", "gx", "gy", "gz"), None, None),
        ),
        out_specs=(P("groups", "gx", ("gy", "gz")), P(("groups", "gx", "gy", "gz"), None)),
        check_vma=False,
    )
```

```python
import jax
import jax.numpy as jnp
from jax import lax
from jax.experimental import pallas as pl
from jax.experimental.pallas import tpu as pltpu
from jax.sharding import PartitionSpec as P

LEAF_R = 8
LEAF_C = 16
AXES = ("gx", "gy", "gz")


def plane_curl(padded):
    along_y = padded[1:-1, 2:] - padded[1:-1, :-2]
    along_x = padded[:-2, 1:-1] - padded[2:, 1:-1]
    return jnp.stack([along_y, along_x])


def to_leaves(grid_values):
    components, row_count, col_count, port_count = grid_values.shape
    blocks = grid_values.reshape(
        components, row_count // LEAF_R, LEAF_R, col_count // LEAF_C, LEAF_C, port_count
    )
    blocks = blocks.transpose(1, 3, 0, 2, 4, 5)
    return blocks.reshape(
        row_count // LEAF_R, col_count // LEAF_C, components, LEAF_R * LEAF_C, port_count
    )


def from_leaves(leaves):
    leaf_rows, leaf_cols, components, leaf_cells, port_count = leaves.shape
    blocks = leaves.reshape(leaf_rows, leaf_cols, components, LEAF_R, LEAF_C, port_count)
    blocks = blocks.transpose(2, 0, 3, 1, 4, 5)
    return blocks.reshape(components, leaf_rows * LEAF_R, leaf_cols * LEAF_C, port_count)


def device_grid():
    nx, ny, nz = (lax.axis_size(a) for a in AXES)
    return nx, ny, nz


def pairs_by(fn):
    nx, ny, nz = device_grid()
    out = []
    for x in range(nx):
        for y in range(ny):
            for z in range(nz):
                target = fn(x, y, z)
                if target is None:
                    continue
                tx, ty, tz = target
                if 0 <= tx < nx and 0 <= ty < ny and 0 <= tz < nz:
                    out.append(((x * ny + y) * nz + z, (tx * ny + ty) * nz + tz))
    return out


def send(value, fn):
    return lax.ppermute(value, AXES, pairs_by(fn))


def sideways(x, y, z, dx):
    nz = lax.axis_size("gz")
    if z == nz - 1:
        return (x + dx, y + 1, 0)
    if z == 0:
        return (x + dx, y - 1, nz - 1)
    return None


def stream_window(stream, half, ready):
    gz = lax.axis_index("gz")
    rows, width = stream.shape[0], stream.shape[1]
    hr, hc = LEAF_R + 1, LEAF_C + 1
    mid_w = half + hc
    mid = lax.dynamic_slice_in_dim(stream, gz * (width - mid_w), mid_w, 1)
    side = lax.dynamic_slice_in_dim(stream, gz * (width - hc), hc, 1)
    h_got = send(side, lambda x, y, z: sideways(x, y, z, 0))
    wide = lax.dynamic_slice_in_dim(
        jnp.concatenate([h_got, mid, h_got], 1), gz * hc, mid_w + hc, 1
    )
    v_top = send(wide[rows - hr :], lambda x, y, z: (x + 1, y, z))
    v_bot = send(wide[:hr], lambda x, y, z: (x - 1, y, z))
    (v_top, v_bot), ready = lax.optimization_barrier(((v_top, v_bot), ready))
    return jnp.concatenate([v_top, wide, v_bot], 0), ready


def field_halo(grid_field):
    x_field = grid_field[0]
    y_field = grid_field[1]
    rows = y_field.shape[0]
    cols = x_field.shape[1]

    def step(x, y, z, dc):
        nz = lax.axis_size("gz")
        c = y * nz + z + dc
        return (x, c // nz, c % nz) if c >= 0 else None

    x_left = send(x_field[:, cols - 1 :], lambda x, y, z: step(x, y, z, 1))
    x_right = send(x_field[:, :1], lambda x, y, z: step(x, y, z, -1))
    y_top = send(y_field[rows - 1 :], lambda x, y, z: (x + 1, y, z))
    y_bot = send(y_field[:1], lambda x, y, z: (x - 1, y, z))
    x_pad = jnp.concatenate([x_left, x_field, x_right], 1).astype(jnp.float32)
    y_pad = jnp.concatenate([y_top, y_field, y_bot], 0).astype(jnp.float32)
    return x_pad[:, :-2] - x_pad[:, 2:] + (y_pad[2:] - y_pad[:-2])


def leaf_kernel(
    codes_ref, scale_ref, bord_hbm, ind_hbm, row_leaf_ref, cpl_t_hbm, cur_hbm,
    field_ref, volt_ref, bord_ref, ind_ref, cpl_t_ref, cur_ref, acc_ref, sems, ind_sems,
):
    leaf_count = ind_ref.shape[0]
    leaf_cols = bord_ref.shape[1] - 2
    near_count = ind_ref.shape[1]
    cells = ind_ref.shape[3]
    first = [
        pltpu.make_async_copy(bord_hbm, bord_ref, sems.at[0]),
        pltpu.make_async_copy(cpl_t_hbm, cpl_t_ref, sems.at[1]),
        pltpu.make_async_copy(cur_hbm, cur_ref, sems.at[2]),
    ]
    for copy in first:
        copy.start()
    for l in range(leaf_count):
        pltpu.make_async_copy(ind_hbm.at[l], ind_ref.at[l], ind_sems.at[l]).start()
    acc_ref[...] = jnp.zeros_like(acc_ref)
    for copy in first:
        copy.wait()

    def one_leaf(leaf, carry):
        pltpu.make_async_copy(ind_hbm.at[leaf], ind_ref.at[leaf], ind_sems.at[leaf]).wait()
        row = leaf // leaf_cols
        col = leaf % leaf_cols
        coupling_t = cpl_t_ref[...]
        coupling_t = jnp.where(row_leaf_ref[...] == leaf, coupling_t, jnp.zeros_like(coupling_t))
        filament = jnp.dot(coupling_t, cur_ref[...], preferred_element_type=jnp.float32)
        sources = []
        for n in range(near_count):
            code = codes_ref[leaf, n]
            src_row = jnp.minimum(jnp.maximum(row + code // 3, 0), bord_ref.shape[0] - 1)
            src_col = jnp.minimum(jnp.maximum(col + code % 3, 0), bord_ref.shape[1] - 1)
            keep = scale_ref[leaf, n] > 0
            tile = bord_ref[src_row, src_col]
            sources.append(jnp.where(keep, tile, jnp.zeros_like(tile)))
        for c in range(2):
            weights = jnp.concatenate([ind_ref[leaf, n, c] for n in range(near_count)], axis=1)
            stacked = jnp.concatenate([s[c] for s in sources], axis=0)
            total = filament[c * cells : (c + 1) * cells] + jnp.dot(
                weights, stacked, preferred_element_type=jnp.float32
            )
            field_ref[c, pl.ds(row * LEAF_R, LEAF_R), pl.ds(pl.multiple_of(col * LEAF_C, LEAF_C), LEAF_C)] = (
                total.reshape(LEAF_R, LEAF_C, -1).astype(field_ref.dtype)
            )
        own = bord_ref[row + 1, col + 1].reshape(2 * cells, -1)
        acc_ref[...] += lax.dot_general(
            own, coupling_t, (((0,), (0,)), ((), ())), preferred_element_type=jnp.float32
        )
        return carry

    lax.fori_loop(0, leaf_count, one_leaf, 0)
    volt_ref[...] = acc_ref[...].T.astype(volt_ref.dtype)


def leaf_fields(codes, scales, bordered, kernels, row_leaf, coupling_t, current):
    leaf_count, near_count, components, cells, _ = kernels.shape
    leaf_rows = bordered.shape[0] - 2
    leaf_cols = bordered.shape[1] - 2
    slot_count, port_count = current.shape
    smem = pl.BlockSpec(memory_space=pltpu.SMEM)
    hbm = pl.BlockSpec(memory_space=pl.ANY)
    vmem = pl.BlockSpec(memory_space=pltpu.VMEM)
    return pl.pallas_call(
        leaf_kernel,
        in_specs=[smem, smem, hbm, hbm, vmem, hbm, hbm],
        out_specs=[vmem, vmem],
        out_shape=[
            jax.ShapeDtypeStruct(
                (components, leaf_rows * LEAF_R, leaf_cols * LEAF_C, port_count), jnp.bfloat16
            ),
            jax.ShapeDtypeStruct((slot_count, port_count), jnp.bfloat16),
        ],
        scratch_shapes=[
            pltpu.VMEM(bordered.shape, bordered.dtype),
            pltpu.VMEM(kernels.shape, kernels.dtype),
            pltpu.VMEM(coupling_t.shape, coupling_t.dtype),
            pltpu.VMEM(current.shape, current.dtype),
            pltpu.VMEM((port_count, slot_count), jnp.float32),
            pltpu.SemaphoreType.DMA((3,)),
            pltpu.SemaphoreType.DMA((leaf_count,)),
        ],
    )(codes, scales, bordered, kernels, row_leaf, coupling_t, current)


def body(stream, inductance, near_lists, filament_leaf, filament_current, filament_coupling):
    port_count = stream.shape[0]
    leaf_rows = inductance.shape[0]
    leaf_cols = inductance.shape[1]
    near_count = inductance.shape[2]
    leaf_cells = inductance.shape[4]
    leaf_count = leaf_rows * leaf_cols
    half_cols = leaf_cols * LEAF_C
    nx, ny, nz = device_grid()
    gx = lax.axis_index("gx")
    col_index = lax.axis_index("gy") * nz + lax.axis_index("gz")
    owners = nx * ny * nz

    filament_count = filament_leaf.shape[0]
    capacity = max(2, 2 * filament_count // owners)
    slot_count = owners * capacity
    plane_cols = leaf_cols * ny * nz
    leaf_row = filament_leaf // plane_cols
    leaf_col = filament_leaf % plane_cols
    owner_ids = leaf_row // leaf_rows * (ny * nz) + leaf_col // leaf_cols
    local_ids = leaf_row % leaf_rows * leaf_cols + leaf_col % leaf_cols
    index = jnp.arange(filament_count, dtype=jnp.int32)
    earlier = (owner_ids[None, :] == owner_ids[:, None]) & (index[None, :] < index[:, None])
    position = jnp.sum(earlier.astype(jnp.int32), axis=1)
    target_slot = owner_ids * capacity + position
    placement_mask = target_slot[None, :] == jnp.arange(slot_count, dtype=jnp.int32)[:, None]
    placement = placement_mask.astype(jnp.bfloat16)
    row_width = 2 * leaf_cells + port_count
    rows_out = jnp.concatenate(
        [filament_coupling.reshape(filament_count, 2 * leaf_cells), filament_current], 1
    )
    sent = jnp.dot(placement, rows_out, preferred_element_type=jnp.float32).astype(jnp.bfloat16)
    sent_leaf = jnp.dot(
        placement, (local_ids + 1).astype(jnp.bfloat16), preferred_element_type=jnp.float32
    ) - 1.0
    leaf_row_block = jnp.pad(
        sent_leaf.astype(jnp.bfloat16).reshape(owners, 1, capacity),
        ((0, 0), (0, 0), (0, row_width - capacity)),
    )
    payload = jnp.concatenate([sent.reshape(owners, capacity, row_width), leaf_row_block], 1)
    got = lax.all_to_all(payload, AXES, split_axis=0, concat_axis=0, tiled=True)
    got_rows = got[:, :capacity].reshape(slot_count, row_width)
    got_leaf = got[:, capacity, :capacity].reshape(slot_count).astype(jnp.int32)
    got_coupling_t = got_rows[:, : 2 * leaf_cells].T
    got_current = got_rows[:, 2 * leaf_cells :]
    got_leaf = got_leaf.reshape(1, slot_count)

    window, (got_leaf, got_coupling_t, got_current) = stream_window(
        stream.transpose(1, 2, 0), half_cols, (got_leaf, got_coupling_t, got_current)
    )
    currents = plane_curl(window).astype(jnp.bfloat16)
    bordered = to_leaves(currents)
    src_row = jnp.arange(leaf_rows, dtype=jnp.int32)[:, None, None] + near_lists // 3
    src_col = jnp.arange(leaf_cols, dtype=jnp.int32)[None, :, None] + near_lists % 3
    row_ok = ((src_row > 0) | (gx > 0)) & ((src_row < leaf_rows + 1) | (gx < nx - 1))
    col_ok = ((src_col > 0) | (col_index > 0)) & (
        (src_col < leaf_cols + 1) | (col_index < ny * nz - 1)
    )
    scales = (row_ok & col_ok).astype(jnp.int32).reshape(leaf_count, near_count)

    kernels = inductance.reshape(leaf_count, near_count, 2, leaf_cells, leaf_cells)
    codes = near_lists.reshape(leaf_count, near_count)
    total_field, induced = leaf_fields(
        codes, scales, bordered, kernels, got_leaf, got_coupling_t, got_current
    )
    returned = lax.all_to_all(
        induced.reshape(owners, capacity, port_count), AXES, split_axis=0, concat_axis=0, tiled=True
    ).reshape(slot_count, port_count)
    filament_voltage = lax.dot_general(
        placement, returned, (((0,), (0,)), ((), ())), preferred_element_type=jnp.float32
    ).astype(jnp.bfloat16)

    loop_voltage = field_halo(total_field).transpose(2, 0, 1)
    return (loop_voltage, filament_voltage)


def solution(mesh):
    return jax.shard_map(
        body,
        mesh=mesh,
        in_specs=(
            P("groups", "gx", "gy"),
            P(("groups", "gx"), ("gy", "gz"), None, None, None, None),
            P(("groups", "gx"), ("gy", "gz"), None),
            P(("groups", "gx", "gy", "gz")),
            P(("groups", "gx", "gy", "gz"), None),
            P(("groups", "gx", "gy", "gz"), None, None),
        ),
        out_specs=(P("groups", "gx", ("gy", "gz")), P(("groups", "gx", "gy", "gz"), None)),
        check_vma=False,
    )
```

```python
import jax
import jax.numpy as jnp
from jax import lax
from jax.experimental import pallas as pl
from jax.experimental.pallas import tpu as pltpu
from jax.sharding import PartitionSpec as P

LEAF_R = 8
LEAF_C = 16
AXES = ("gx", "gy", "gz")


def plane_curl(padded):
    along_y = padded[1:-1, 2:] - padded[1:-1, :-2]
    along_x = padded[:-2, 1:-1] - padded[2:, 1:-1]
    return jnp.stack([along_y, along_x])


def to_leaves(grid_values):
    components, row_count, col_count, port_count = grid_values.shape
    blocks = grid_values.reshape(
        components, row_count // LEAF_R, LEAF_R, col_count // LEAF_C, LEAF_C, port_count
    )
    blocks = blocks.transpose(1, 3, 0, 2, 4, 5)
    return blocks.reshape(
        row_count // LEAF_R, col_count // LEAF_C, components, LEAF_R * LEAF_C, port_count
    )


def from_leaves(leaves):
    leaf_rows, leaf_cols, components, leaf_cells, port_count = leaves.shape
    blocks = leaves.reshape(leaf_rows, leaf_cols, components, LEAF_R, LEAF_C, port_count)
    blocks = blocks.transpose(2, 0, 3, 1, 4, 5)
    return blocks.reshape(components, leaf_rows * LEAF_R, leaf_cols * LEAF_C, port_count)


def device_grid():
    nx, ny, nz = (lax.axis_size(a) for a in AXES)
    return nx, ny, nz


def pairs_by(fn):
    nx, ny, nz = device_grid()
    out = []
    for x in range(nx):
        for y in range(ny):
            for z in range(nz):
                target = fn(x, y, z)
                if target is None:
                    continue
                tx, ty, tz = target
                if 0 <= tx < nx and 0 <= ty < ny and 0 <= tz < nz:
                    out.append(((x * ny + y) * nz + z, (tx * ny + ty) * nz + tz))
    return out


def send(value, fn):
    return lax.ppermute(value, AXES, pairs_by(fn))


def sideways(x, y, z, dx):
    nz = lax.axis_size("gz")
    if z == nz - 1:
        return (x + dx, y + 1, 0)
    if z == 0:
        return (x + dx, y - 1, nz - 1)
    return None


def stream_window(stream, half, ready):
    gz = lax.axis_index("gz")
    rows, width = stream.shape[0], stream.shape[1]
    hr, hc = LEAF_R + 1, LEAF_C + 1
    mid_w = half + hc
    mid = lax.dynamic_slice_in_dim(stream, gz * (width - mid_w), mid_w, 1)
    side = lax.dynamic_slice_in_dim(stream, gz * (width - hc), hc, 1)
    h_got = send(side, lambda x, y, z: sideways(x, y, z, 0))
    wide = lax.dynamic_slice_in_dim(
        jnp.concatenate([h_got, mid, h_got], 1), gz * hc, mid_w + hc, 1
    )
    v_top = send(wide[rows - hr :], lambda x, y, z: (x + 1, y, z))
    v_bot = send(wide[:hr], lambda x, y, z: (x - 1, y, z))
    (v_top, v_bot), ready = lax.optimization_barrier(((v_top, v_bot), ready))
    return jnp.concatenate([v_top, wide, v_bot], 0), ready


def field_halo(grid_field):
    x_field = grid_field[0]
    y_field = grid_field[1]
    rows = y_field.shape[0]
    cols = x_field.shape[1]

    def step(x, y, z, dc):
        nz = lax.axis_size("gz")
        c = y * nz + z + dc
        return (x, c // nz, c % nz) if c >= 0 else None

    x_left = send(x_field[:, cols - 1 :], lambda x, y, z: step(x, y, z, 1))
    x_right = send(x_field[:, :1], lambda x, y, z: step(x, y, z, -1))
    y_top = send(y_field[rows - 1 :], lambda x, y, z: (x + 1, y, z))
    y_bot = send(y_field[:1], lambda x, y, z: (x - 1, y, z))
    x_pad = jnp.concatenate([x_left, x_field, x_right], 1).astype(jnp.float32)
    y_pad = jnp.concatenate([y_top, y_field, y_bot], 0).astype(jnp.float32)
    return x_pad[:, :-2] - x_pad[:, 2:] + (y_pad[2:] - y_pad[:-2])


def leaf_kernel(
    codes_ref, scale_ref, bord_hbm, ind_hbm, row_leaf_ref, cpl_t_hbm, cur_hbm,
    field_ref, bord_ref, ind_ref, cpl_t_ref, cur_ref, sems, ind_sems,
):
    leaf_count = ind_ref.shape[0]
    leaf_cols = bord_ref.shape[1] - 2
    near_count = ind_ref.shape[1]
    cells = ind_ref.shape[3]
    first = [
        pltpu.make_async_copy(bord_hbm, bord_ref, sems.at[0]),
        pltpu.make_async_copy(cpl_t_hbm, cpl_t_ref, sems.at[1]),
        pltpu.make_async_copy(cur_hbm, cur_ref, sems.at[2]),
    ]
    for copy in first:
        copy.start()
    for l in range(leaf_count):
        pltpu.make_async_copy(ind_hbm.at[l], ind_ref.at[l], ind_sems.at[l]).start()
    for copy in first:
        copy.wait()

    def one_leaf(leaf, carry):
        pltpu.make_async_copy(ind_hbm.at[leaf], ind_ref.at[leaf], ind_sems.at[leaf]).wait()
        row = leaf // leaf_cols
        col = leaf % leaf_cols
        coupling_t = cpl_t_ref[...]
        coupling_t = jnp.where(row_leaf_ref[...] == leaf, coupling_t, jnp.zeros_like(coupling_t))
        filament = jnp.dot(coupling_t, cur_ref[...], preferred_element_type=jnp.float32)
        sources = []
        for n in range(near_count):
            code = codes_ref[leaf, n]
            src_row = jnp.minimum(jnp.maximum(row + code // 3, 0), bord_ref.shape[0] - 1)
            src_col = jnp.minimum(jnp.maximum(col + code % 3, 0), bord_ref.shape[1] - 1)
            keep = scale_ref[leaf, n] > 0
            tile = bord_ref[src_row, src_col]
            sources.append(jnp.where(keep, tile, jnp.zeros_like(tile)))
        for c in range(2):
            weights = jnp.concatenate([ind_ref[leaf, n, c] for n in range(near_count)], axis=1)
            stacked = jnp.concatenate([s[c] for s in sources], axis=0)
            total = filament[c * cells : (c + 1) * cells] + jnp.dot(
                weights, stacked, preferred_element_type=jnp.float32
            )
            field_ref[c, pl.ds(row * LEAF_R, LEAF_R), pl.ds(pl.multiple_of(col * LEAF_C, LEAF_C), LEAF_C)] = (
                total.reshape(LEAF_R, LEAF_C, -1).astype(field_ref.dtype)
            )
        return carry

    lax.fori_loop(0, leaf_count, one_leaf, 0)


def induced_kernel(bord_ref, row_leaf_ref, cpl_t_ref, volt_ref, acc_ref):
    leaf_rows = bord_ref.shape[0] - 2
    leaf_cols = bord_ref.shape[1] - 2
    cells = bord_ref.shape[3]
    acc_ref[...] = jnp.zeros_like(acc_ref)

    def one_leaf(leaf, carry):
        row = leaf // leaf_cols
        col = leaf % leaf_cols
        coupling_t = cpl_t_ref[...]
        coupling_t = jnp.where(row_leaf_ref[...] == leaf, coupling_t, jnp.zeros_like(coupling_t))
        own = bord_ref[row + 1, col + 1].reshape(2 * cells, -1)
        acc_ref[...] += lax.dot_general(
            own, coupling_t, (((0,), (0,)), ((), ())), preferred_element_type=jnp.float32
        )
        return carry

    lax.fori_loop(0, leaf_rows * leaf_cols, one_leaf, 0)
    volt_ref[...] = acc_ref[...].T.astype(volt_ref.dtype)


def leaf_fields(codes, scales, bordered, kernels, row_leaf, coupling_t, current):
    leaf_count, near_count, components, cells, _ = kernels.shape
    leaf_rows = bordered.shape[0] - 2
    leaf_cols = bordered.shape[1] - 2
    slot_count, port_count = current.shape
    smem = pl.BlockSpec(memory_space=pltpu.SMEM)
    hbm = pl.BlockSpec(memory_space=pl.ANY)
    vmem = pl.BlockSpec(memory_space=pltpu.VMEM)
    field = pl.pallas_call(
        leaf_kernel,
        in_specs=[smem, smem, hbm, hbm, vmem, hbm, hbm],
        out_specs=vmem,
        out_shape=jax.ShapeDtypeStruct(
            (components, leaf_rows * LEAF_R, leaf_cols * LEAF_C, port_count), jnp.bfloat16
        ),
        scratch_shapes=[
            pltpu.VMEM(bordered.shape, bordered.dtype),
            pltpu.VMEM(kernels.shape, kernels.dtype),
            pltpu.VMEM(coupling_t.shape, coupling_t.dtype),
            pltpu.VMEM(current.shape, current.dtype),
            pltpu.SemaphoreType.DMA((3,)),
            pltpu.SemaphoreType.DMA((leaf_count,)),
        ],
    )(codes, scales, bordered, kernels, row_leaf, coupling_t, current)
    field, bordered = lax.optimization_barrier((field, bordered))
    volt = pl.pallas_call(
        induced_kernel,
        in_specs=[vmem, vmem, vmem],
        out_specs=vmem,
        out_shape=jax.ShapeDtypeStruct((slot_count, port_count), jnp.bfloat16),
        scratch_shapes=[pltpu.VMEM((port_count, slot_count), jnp.float32)],
    )(bordered, row_leaf, coupling_t)
    return field, volt


def body(stream, inductance, near_lists, filament_leaf, filament_current, filament_coupling):
    port_count = stream.shape[0]
    leaf_rows = inductance.shape[0]
    leaf_cols = inductance.shape[1]
    near_count = inductance.shape[2]
    leaf_cells = inductance.shape[4]
    leaf_count = leaf_rows * leaf_cols
    half_cols = leaf_cols * LEAF_C
    nx, ny, nz = device_grid()
    gx = lax.axis_index("gx")
    col_index = lax.axis_index("gy") * nz + lax.axis_index("gz")
    owners = nx * ny * nz

    filament_count = filament_leaf.shape[0]
    capacity = max(2, 2 * filament_count // owners)
    slot_count = owners * capacity
    plane_cols = leaf_cols * ny * nz
    leaf_row = filament_leaf // plane_cols
    leaf_col = filament_leaf % plane_cols
    owner_ids = leaf_row // leaf_rows * (ny * nz) + leaf_col // leaf_cols
    local_ids = leaf_row % leaf_rows * leaf_cols + leaf_col % leaf_cols
    index = jnp.arange(filament_count, dtype=jnp.int32)
    earlier = (owner_ids[None, :] == owner_ids[:, None]) & (index[None, :] < index[:, None])
    position = jnp.sum(earlier.astype(jnp.int32), axis=1)
    target_slot = owner_ids * capacity + position
    placement_mask = target_slot[None, :] == jnp.arange(slot_count, dtype=jnp.int32)[:, None]
    placement = placement_mask.astype(jnp.bfloat16)
    row_width = 2 * leaf_cells + port_count
    rows_out = jnp.concatenate(
        [filament_coupling.reshape(filament_count, 2 * leaf_cells), filament_current], 1
    )
    sent = jnp.dot(placement, rows_out, preferred_element_type=jnp.float32).astype(jnp.bfloat16)
    sent_leaf = jnp.dot(
        placement, (local_ids + 1).astype(jnp.bfloat16), preferred_element_type=jnp.float32
    ) - 1.0
    leaf_row_block = jnp.pad(
        sent_leaf.astype(jnp.bfloat16).reshape(owners, 1, capacity),
        ((0, 0), (0, 0), (0, row_width - capacity)),
    )
    payload = jnp.concatenate([sent.reshape(owners, capacity, row_width), leaf_row_block], 1)
    got = lax.all_to_all(payload, AXES, split_axis=0, concat_axis=0, tiled=True)
    got_rows = got[:, :capacity].reshape(slot_count, row_width)
    got_leaf = got[:, capacity, :capacity].reshape(slot_count).astype(jnp.int32)
    got_coupling_t = got_rows[:, : 2 * leaf_cells].T
    got_current = got_rows[:, 2 * leaf_cells :]
    got_leaf = got_leaf.reshape(1, slot_count)

    window, (got_leaf, got_coupling_t, got_current) = stream_window(
        stream.transpose(1, 2, 0), half_cols, (got_leaf, got_coupling_t, got_current)
    )
    currents = plane_curl(window).astype(jnp.bfloat16)
    bordered = to_leaves(currents)
    src_row = jnp.arange(leaf_rows, dtype=jnp.int32)[:, None, None] + near_lists // 3
    src_col = jnp.arange(leaf_cols, dtype=jnp.int32)[None, :, None] + near_lists % 3
    row_ok = ((src_row > 0) | (gx > 0)) & ((src_row < leaf_rows + 1) | (gx < nx - 1))
    col_ok = ((src_col > 0) | (col_index > 0)) & (
        (src_col < leaf_cols + 1) | (col_index < ny * nz - 1)
    )
    scales = (row_ok & col_ok).astype(jnp.int32).reshape(leaf_count, near_count)

    kernels = inductance.reshape(leaf_count, near_count, 2, leaf_cells, leaf_cells)
    codes = near_lists.reshape(leaf_count, near_count)
    total_field, induced = leaf_fields(
        codes, scales, bordered, kernels, got_leaf, got_coupling_t, got_current
    )
    returned = lax.all_to_all(
        induced.reshape(owners, capacity, port_count), AXES, split_axis=0, concat_axis=0, tiled=True
    ).reshape(slot_count, port_count)
    filament_voltage = lax.dot_general(
        placement, returned, (((0,), (0,)), ((), ())), preferred_element_type=jnp.float32
    ).astype(jnp.bfloat16)

    loop_voltage = field_halo(total_field).transpose(2, 0, 1)
    return (loop_voltage, filament_voltage)


def solution(mesh):
    return jax.shard_map(
        body,
        mesh=mesh,
        in_specs=(
            P("groups", "gx", "gy"),
            P(("groups", "gx"), ("gy", "gz"), None, None, None, None),
            P(("groups", "gx"), ("gy", "gz"), None),
            P(("groups", "gx", "gy", "gz")),
            P(("groups", "gx", "gy", "gz"), None),
            P(("groups", "gx", "gy", "gz"), None, None),
        ),
        out_specs=(P("groups", "gx", ("gy", "gz")), P(("groups", "gx", "gy", "gz"), None)),
        check_vma=False,
    )
```

```python
import jax
import jax.numpy as jnp
from jax import lax
from jax.experimental import pallas as pl
from jax.experimental.pallas import tpu as pltpu
from jax.sharding import PartitionSpec as P

LEAF_R = 8
LEAF_C = 16
AXES = ("gx", "gy", "gz")


def plane_curl(padded):
    along_y = padded[1:-1, 2:] - padded[1:-1, :-2]
    along_x = padded[:-2, 1:-1] - padded[2:, 1:-1]
    return jnp.stack([along_y, along_x])


def to_leaves(grid_values):
    components, row_count, col_count, port_count = grid_values.shape
    blocks = grid_values.reshape(
        components, row_count // LEAF_R, LEAF_R, col_count // LEAF_C, LEAF_C, port_count
    )
    blocks = blocks.transpose(1, 3, 0, 2, 4, 5)
    return blocks.reshape(
        row_count // LEAF_R, col_count // LEAF_C, components, LEAF_R * LEAF_C, port_count
    )


def from_leaves(leaves):
    leaf_rows, leaf_cols, components, leaf_cells, port_count = leaves.shape
    blocks = leaves.reshape(leaf_rows, leaf_cols, components, LEAF_R, LEAF_C, port_count)
    blocks = blocks.transpose(2, 0, 3, 1, 4, 5)
    return blocks.reshape(components, leaf_rows * LEAF_R, leaf_cols * LEAF_C, port_count)


def device_grid():
    nx, ny, nz = (lax.axis_size(a) for a in AXES)
    return nx, ny, nz


def pairs_by(fn):
    nx, ny, nz = device_grid()
    out = []
    for x in range(nx):
        for y in range(ny):
            for z in range(nz):
                target = fn(x, y, z)
                if target is None:
                    continue
                tx, ty, tz = target
                if 0 <= tx < nx and 0 <= ty < ny and 0 <= tz < nz:
                    out.append(((x * ny + y) * nz + z, (tx * ny + ty) * nz + tz))
    return out


def send(value, fn):
    return lax.ppermute(value, AXES, pairs_by(fn))


def sideways(x, y, z, dx):
    nz = lax.axis_size("gz")
    if z == nz - 1:
        return (x + dx, y + 1, 0)
    if z == 0:
        return (x + dx, y - 1, nz - 1)
    return None


def stream_window(stream, half, ready):
    gz = lax.axis_index("gz")
    rows, width = stream.shape[0], stream.shape[1]
    hr, hc = LEAF_R + 1, LEAF_C + 1
    mid_w = half + hc
    mid = lax.dynamic_slice_in_dim(stream, gz * (width - mid_w), mid_w, 1)
    side = lax.dynamic_slice_in_dim(stream, gz * (width - hc), hc, 1)
    h_got = send(side, lambda x, y, z: sideways(x, y, z, 0))
    wide = lax.dynamic_slice_in_dim(
        jnp.concatenate([h_got, mid, h_got], 1), gz * hc, mid_w + hc, 1
    )
    v_top = send(wide[rows - hr :], lambda x, y, z: (x + 1, y, z))
    v_bot = send(wide[:hr], lambda x, y, z: (x - 1, y, z))
    (v_top, v_bot), ready = lax.optimization_barrier(((v_top, v_bot), ready))
    return jnp.concatenate([v_top, wide, v_bot], 0), ready


def field_halo(grid_field):
    x_field = grid_field[0]
    y_field = grid_field[1]
    rows = y_field.shape[0]
    cols = x_field.shape[1]

    def step(x, y, z, dc):
        nz = lax.axis_size("gz")
        c = y * nz + z + dc
        return (x, c // nz, c % nz) if c >= 0 else None

    x_left = send(x_field[:, cols - 1 :], lambda x, y, z: step(x, y, z, 1))
    x_right = send(x_field[:, :1], lambda x, y, z: step(x, y, z, -1))
    y_top = send(y_field[rows - 1 :], lambda x, y, z: (x + 1, y, z))
    y_bot = send(y_field[:1], lambda x, y, z: (x - 1, y, z))
    x_pad = jnp.concatenate([x_left, x_field, x_right], 1).astype(jnp.float32)
    y_pad = jnp.concatenate([y_top, y_field, y_bot], 0).astype(jnp.float32)
    return x_pad[:, :-2] - x_pad[:, 2:] + (y_pad[2:] - y_pad[:-2])


def filament_kernel(row_leaf_ref, cpl_t_ref, cur_ref, fil_ref):
    def one_leaf(leaf, carry):
        coupling_t = cpl_t_ref[...]
        coupling_t = jnp.where(row_leaf_ref[...] == leaf, coupling_t, jnp.zeros_like(coupling_t))
        fil_ref[leaf] = jnp.dot(coupling_t, cur_ref[...], preferred_element_type=jnp.float32)
        return carry

    lax.fori_loop(0, fil_ref.shape[0], one_leaf, 0)


def filament_field(row_leaf, coupling_t, current, leaf_count):
    vmem = pl.BlockSpec(memory_space=pltpu.VMEM)
    return pl.pallas_call(
        filament_kernel,
        in_specs=[vmem, vmem, vmem],
        out_specs=vmem,
        out_shape=jax.ShapeDtypeStruct(
            (leaf_count, coupling_t.shape[0], current.shape[1]), jnp.float32
        ),
    )(row_leaf, coupling_t, current)


def leaf_kernel(
    codes_ref, scale_ref, bord_hbm, ind_hbm, fil_hbm,
    field_ref, bord_ref, ind_ref, fil_ref, sems, ind_sems,
):
    leaf_count = ind_ref.shape[0]
    leaf_cols = bord_ref.shape[1] - 2
    near_count = ind_ref.shape[1]
    cells = ind_ref.shape[3]
    first = [
        pltpu.make_async_copy(bord_hbm, bord_ref, sems.at[0]),
        pltpu.make_async_copy(fil_hbm, fil_ref, sems.at[1]),
    ]
    for copy in first:
        copy.start()
    for l in range(leaf_count):
        pltpu.make_async_copy(ind_hbm.at[l], ind_ref.at[l], ind_sems.at[l]).start()
    for copy in first:
        copy.wait()

    def one_leaf(leaf, carry):
        pltpu.make_async_copy(ind_hbm.at[leaf], ind_ref.at[leaf], ind_sems.at[leaf]).wait()
        row = leaf // leaf_cols
        col = leaf % leaf_cols
        filament = fil_ref[leaf]
        sources = []
        for n in range(near_count):
            code = codes_ref[leaf, n]
            src_row = jnp.minimum(jnp.maximum(row + code // 3, 0), bord_ref.shape[0] - 1)
            src_col = jnp.minimum(jnp.maximum(col + code % 3, 0), bord_ref.shape[1] - 1)
            keep = scale_ref[leaf, n] > 0
            tile = bord_ref[src_row, src_col]
            sources.append(jnp.where(keep, tile, jnp.zeros_like(tile)))
        for c in range(2):
            weights = jnp.concatenate([ind_ref[leaf, n, c] for n in range(near_count)], axis=1)
            stacked = jnp.concatenate([s[c] for s in sources], axis=0)
            total = filament[c * cells : (c + 1) * cells] + jnp.dot(
                weights, stacked, preferred_element_type=jnp.float32
            )
            field_ref[c, pl.ds(row * LEAF_R, LEAF_R), pl.ds(pl.multiple_of(col * LEAF_C, LEAF_C), LEAF_C)] = (
                total.reshape(LEAF_R, LEAF_C, -1).astype(field_ref.dtype)
            )
        return carry

    lax.fori_loop(0, leaf_count, one_leaf, 0)


def induced_kernel(bord_ref, row_leaf_ref, cpl_t_ref, volt_ref, acc_ref):
    leaf_rows = bord_ref.shape[0] - 2
    leaf_cols = bord_ref.shape[1] - 2
    cells = bord_ref.shape[3]
    acc_ref[...] = jnp.zeros_like(acc_ref)

    def one_leaf(leaf, carry):
        row = leaf // leaf_cols
        col = leaf % leaf_cols
        coupling_t = cpl_t_ref[...]
        coupling_t = jnp.where(row_leaf_ref[...] == leaf, coupling_t, jnp.zeros_like(coupling_t))
        own = bord_ref[row + 1, col + 1].reshape(2 * cells, -1)
        acc_ref[...] += lax.dot_general(
            own, coupling_t, (((0,), (0,)), ((), ())), preferred_element_type=jnp.float32
        )
        return carry

    lax.fori_loop(0, leaf_rows * leaf_cols, one_leaf, 0)
    volt_ref[...] = acc_ref[...].T.astype(volt_ref.dtype)


def leaf_fields(codes, scales, bordered, kernels, filament, row_leaf, coupling_t):
    leaf_count, near_count, components, cells, _ = kernels.shape
    leaf_rows = bordered.shape[0] - 2
    leaf_cols = bordered.shape[1] - 2
    port_count = bordered.shape[-1]
    slot_count = coupling_t.shape[1]
    smem = pl.BlockSpec(memory_space=pltpu.SMEM)
    hbm = pl.BlockSpec(memory_space=pl.ANY)
    vmem = pl.BlockSpec(memory_space=pltpu.VMEM)
    field = pl.pallas_call(
        leaf_kernel,
        in_specs=[smem, smem, hbm, hbm, hbm],
        out_specs=vmem,
        out_shape=jax.ShapeDtypeStruct(
            (components, leaf_rows * LEAF_R, leaf_cols * LEAF_C, port_count), jnp.bfloat16
        ),
        scratch_shapes=[
            pltpu.VMEM(bordered.shape, bordered.dtype),
            pltpu.VMEM(kernels.shape, kernels.dtype),
            pltpu.VMEM(filament.shape, filament.dtype),
            pltpu.SemaphoreType.DMA((2,)),
            pltpu.SemaphoreType.DMA((leaf_count,)),
        ],
    )(codes, scales, bordered, kernels, filament)
    field, bordered = lax.optimization_barrier((field, bordered))
    volt = pl.pallas_call(
        induced_kernel,
        in_specs=[vmem, vmem, vmem],
        out_specs=vmem,
        out_shape=jax.ShapeDtypeStruct((slot_count, port_count), jnp.bfloat16),
        scratch_shapes=[pltpu.VMEM((port_count, slot_count), jnp.float32)],
    )(bordered, row_leaf, coupling_t)
    return field, volt


def body(stream, inductance, near_lists, filament_leaf, filament_current, filament_coupling):
    port_count = stream.shape[0]
    leaf_rows = inductance.shape[0]
    leaf_cols = inductance.shape[1]
    near_count = inductance.shape[2]
    leaf_cells = inductance.shape[4]
    leaf_count = leaf_rows * leaf_cols
    half_cols = leaf_cols * LEAF_C
    nx, ny, nz = device_grid()
    gx = lax.axis_index("gx")
    col_index = lax.axis_index("gy") * nz + lax.axis_index("gz")
    owners = nx * ny * nz

    filament_count = filament_leaf.shape[0]
    capacity = max(2, 2 * filament_count // owners)
    slot_count = owners * capacity
    plane_cols = leaf_cols * ny * nz
    leaf_row = filament_leaf // plane_cols
    leaf_col = filament_leaf % plane_cols
    owner_ids = leaf_row // leaf_rows * (ny * nz) + leaf_col // leaf_cols
    local_ids = leaf_row % leaf_rows * leaf_cols + leaf_col % leaf_cols
    index = jnp.arange(filament_count, dtype=jnp.int32)
    earlier = (owner_ids[None, :] == owner_ids[:, None]) & (index[None, :] < index[:, None])
    position = jnp.sum(earlier.astype(jnp.int32), axis=1)
    target_slot = owner_ids * capacity + position
    placement_mask = target_slot[None, :] == jnp.arange(slot_count, dtype=jnp.int32)[:, None]
    placement = placement_mask.astype(jnp.bfloat16)
    row_width = 2 * leaf_cells + port_count
    rows_out = jnp.concatenate(
        [filament_coupling.reshape(filament_count, 2 * leaf_cells), filament_current], 1
    )
    sent = jnp.dot(placement, rows_out, preferred_element_type=jnp.float32).astype(jnp.bfloat16)
    sent_leaf = jnp.dot(
        placement, (local_ids + 1).astype(jnp.bfloat16), preferred_element_type=jnp.float32
    ) - 1.0
    leaf_row_block = jnp.pad(
        sent_leaf.astype(jnp.bfloat16).reshape(owners, 1, capacity),
        ((0, 0), (0, 0), (0, row_width - capacity)),
    )
    payload = jnp.concatenate([sent.reshape(owners, capacity, row_width), leaf_row_block], 1)
    got = lax.all_to_all(payload, AXES, split_axis=0, concat_axis=0, tiled=True)
    got_rows = got[:, :capacity].reshape(slot_count, row_width)
    got_leaf = got[:, capacity, :capacity].reshape(slot_count).astype(jnp.int32)
    got_coupling_t = got_rows[:, : 2 * leaf_cells].T
    got_current = got_rows[:, 2 * leaf_cells :]
    got_leaf = got_leaf.reshape(1, slot_count)
    filament = filament_field(got_leaf, got_coupling_t, got_current, leaf_count)

    window, (got_leaf, got_coupling_t, filament) = stream_window(
        stream.transpose(1, 2, 0), half_cols, (got_leaf, got_coupling_t, filament)
    )
    currents = plane_curl(window).astype(jnp.bfloat16)
    bordered = to_leaves(currents)
    src_row = jnp.arange(leaf_rows, dtype=jnp.int32)[:, None, None] + near_lists // 3
    src_col = jnp.arange(leaf_cols, dtype=jnp.int32)[None, :, None] + near_lists % 3
    row_ok = ((src_row > 0) | (gx > 0)) & ((src_row < leaf_rows + 1) | (gx < nx - 1))
    col_ok = ((src_col > 0) | (col_index > 0)) & (
        (src_col < leaf_cols + 1) | (col_index < ny * nz - 1)
    )
    scales = (row_ok & col_ok).astype(jnp.int32).reshape(leaf_count, near_count)

    kernels = inductance.reshape(leaf_count, near_count, 2, leaf_cells, leaf_cells)
    codes = near_lists.reshape(leaf_count, near_count)
    total_field, induced = leaf_fields(
        codes, scales, bordered, kernels, filament, got_leaf, got_coupling_t
    )
    returned = lax.all_to_all(
        induced.reshape(owners, capacity, port_count), AXES, split_axis=0, concat_axis=0, tiled=True
    ).reshape(slot_count, port_count)
    filament_voltage = lax.dot_general(
        placement, returned, (((0,), (0,)), ((), ())), preferred_element_type=jnp.float32
    ).astype(jnp.bfloat16)

    loop_voltage = field_halo(total_field).transpose(2, 0, 1)
    return (loop_voltage, filament_voltage)


def solution(mesh):
    return jax.shard_map(
        body,
        mesh=mesh,
        in_specs=(
            P("groups", "gx", "gy"),
            P(("groups", "gx"), ("gy", "gz"), None, None, None, None),
            P(("groups", "gx"), ("gy", "gz"), None),
            P(("groups", "gx", "gy", "gz")),
            P(("groups", "gx", "gy", "gz"), None),
            P(("groups", "gx", "gy", "gz"), None, None),
        ),
        out_specs=(P("groups", "gx", ("gy", "gz")), P(("groups", "gx", "gy", "gz"), None)),
        check_vma=False,
    )
```

```python
import jax
import jax.numpy as jnp
from jax import lax
from jax.experimental import pallas as pl
from jax.experimental.pallas import tpu as pltpu
from jax.sharding import PartitionSpec as P

LEAF_R = 8
LEAF_C = 16
AXES = ("gx", "gy", "gz")


def plane_curl(padded):
    along_y = padded[1:-1, 2:] - padded[1:-1, :-2]
    along_x = padded[:-2, 1:-1] - padded[2:, 1:-1]
    return jnp.stack([along_y, along_x])


def to_leaves(grid_values):
    components, row_count, col_count, port_count = grid_values.shape
    blocks = grid_values.reshape(
        components, row_count // LEAF_R, LEAF_R, col_count // LEAF_C, LEAF_C, port_count
    )
    blocks = blocks.transpose(1, 3, 0, 2, 4, 5)
    return blocks.reshape(
        row_count // LEAF_R, col_count // LEAF_C, components, LEAF_R * LEAF_C, port_count
    )


def from_leaves(leaves):
    leaf_rows, leaf_cols, components, leaf_cells, port_count = leaves.shape
    blocks = leaves.reshape(leaf_rows, leaf_cols, components, LEAF_R, LEAF_C, port_count)
    blocks = blocks.transpose(2, 0, 3, 1, 4, 5)
    return blocks.reshape(components, leaf_rows * LEAF_R, leaf_cols * LEAF_C, port_count)


def device_grid():
    nx, ny, nz = (lax.axis_size(a) for a in AXES)
    return nx, ny, nz


def pairs_by(fn):
    nx, ny, nz = device_grid()
    out = []
    for x in range(nx):
        for y in range(ny):
            for z in range(nz):
                target = fn(x, y, z)
                if target is None:
                    continue
                tx, ty, tz = target
                if 0 <= tx < nx and 0 <= ty < ny and 0 <= tz < nz:
                    out.append(((x * ny + y) * nz + z, (tx * ny + ty) * nz + tz))
    return out


def send(value, fn):
    return lax.ppermute(value, AXES, pairs_by(fn))


def sideways(x, y, z, dx):
    nz = lax.axis_size("gz")
    if z == nz - 1:
        return (x + dx, y + 1, 0)
    if z == 0:
        return (x + dx, y - 1, nz - 1)
    return None


def stream_window(stream, half, ready):
    gz = lax.axis_index("gz")
    rows, width = stream.shape[0], stream.shape[1]
    hr, hc = LEAF_R + 1, LEAF_C + 1
    mid_w = half + hc
    mid = lax.dynamic_slice_in_dim(stream, gz * (width - mid_w), mid_w, 1)
    side = lax.dynamic_slice_in_dim(stream, gz * (width - hc), hc, 1)
    h_got = send(side, lambda x, y, z: sideways(x, y, z, 0))
    wide = lax.dynamic_slice_in_dim(
        jnp.concatenate([h_got, mid, h_got], 1), gz * hc, mid_w + hc, 1
    )
    v_top = send(wide[rows - hr :], lambda x, y, z: (x + 1, y, z))
    v_bot = send(wide[:hr], lambda x, y, z: (x - 1, y, z))
    (v_top, v_bot), ready = lax.optimization_barrier(((v_top, v_bot), ready))
    return jnp.concatenate([v_top, wide, v_bot], 0), ready


def field_halo(grid_field):
    x_field = grid_field[0]
    y_field = grid_field[1]
    rows = y_field.shape[0]
    cols = x_field.shape[1]

    def step(x, y, z, dc):
        nz = lax.axis_size("gz")
        c = y * nz + z + dc
        return (x, c // nz, c % nz) if c >= 0 else None

    x_left = send(x_field[:, cols - 1 :], lambda x, y, z: step(x, y, z, 1))
    x_right = send(x_field[:, :1], lambda x, y, z: step(x, y, z, -1))
    y_top = send(y_field[rows - 1 :], lambda x, y, z: (x + 1, y, z))
    y_bot = send(y_field[:1], lambda x, y, z: (x - 1, y, z))
    x_pad = jnp.concatenate([x_left, x_field, x_right], 1).astype(jnp.float32)
    y_pad = jnp.concatenate([y_top, y_field, y_bot], 0).astype(jnp.float32)
    return x_pad[:, :-2] - x_pad[:, 2:] + (y_pad[2:] - y_pad[:-2])


def filament_kernel(row_leaf_ref, cpl_t_ref, cur_ref, fil_ref):
    def one_leaf(leaf, carry):
        coupling_t = cpl_t_ref[...]
        coupling_t = jnp.where(row_leaf_ref[...] == leaf, coupling_t, jnp.zeros_like(coupling_t))
        fil_ref[leaf] = jnp.dot(coupling_t, cur_ref[...], preferred_element_type=jnp.float32)
        return carry

    lax.fori_loop(0, fil_ref.shape[0], one_leaf, 0)


def filament_field(row_leaf, coupling_t, current, leaf_count):
    vmem = pl.BlockSpec(memory_space=pltpu.VMEM)
    return pl.pallas_call(
        filament_kernel,
        in_specs=[vmem, vmem, vmem],
        out_specs=vmem,
        out_shape=jax.ShapeDtypeStruct(
            (leaf_count, coupling_t.shape[0], current.shape[1]), jnp.float32
        ),
    )(row_leaf, coupling_t, current)


def leaf_kernel(
    codes_ref, scale_ref, bord_hbm, ind_hbm, fil_hbm,
    field_ref, bord_ref, ind_ref, fil_ref, sems, ind_sems,
):
    leaf_count = ind_ref.shape[0]
    leaf_cols = bord_ref.shape[1] - 2
    near_count = ind_ref.shape[1]
    cells = ind_ref.shape[3]
    first = [
        pltpu.make_async_copy(bord_hbm, bord_ref, sems.at[0]),
        pltpu.make_async_copy(fil_hbm, fil_ref, sems.at[1]),
    ]
    for copy in first:
        copy.start()
    for l in range(leaf_count):
        pltpu.make_async_copy(ind_hbm.at[l], ind_ref.at[l], ind_sems.at[l]).start()
    for copy in first:
        copy.wait()

    def one_leaf(leaf, carry):
        pltpu.make_async_copy(ind_hbm.at[leaf], ind_ref.at[leaf], ind_sems.at[leaf]).wait()
        row = leaf // leaf_cols
        col = leaf % leaf_cols
        filament = fil_ref[leaf]
        sources = []
        for n in range(near_count):
            code = codes_ref[leaf, n]
            src_row = jnp.minimum(jnp.maximum(row + code // 3, 0), bord_ref.shape[0] - 1)
            src_col = jnp.minimum(jnp.maximum(col + code % 3, 0), bord_ref.shape[1] - 1)
            keep = scale_ref[leaf, n] > 0
            tile = bord_ref[src_row, src_col]
            sources.append(jnp.where(keep, tile, jnp.zeros_like(tile)))
        for c in range(2):
            weights = jnp.concatenate([ind_ref[leaf, n, c] for n in range(near_count)], axis=1)
            stacked = jnp.concatenate([s[c] for s in sources], axis=0)
            total = filament[c * cells : (c + 1) * cells] + jnp.dot(
                weights, stacked, preferred_element_type=jnp.float32
            )
            field_ref[c, pl.ds(row * LEAF_R, LEAF_R), pl.ds(pl.multiple_of(col * LEAF_C, LEAF_C), LEAF_C)] = (
                total.reshape(LEAF_R, LEAF_C, -1).astype(field_ref.dtype)
            )
        return carry

    lax.fori_loop(0, leaf_count, one_leaf, 0)


def induced_kernel(bord_hbm, row_leaf_ref, cpl_t_ref, volt_ref, own_ref, acc_ref, sems):
    leaf_rows = own_ref.shape[0]
    leaf_cols = own_ref.shape[1] - 2
    cells = own_ref.shape[3]
    copies = [
        pltpu.make_async_copy(bord_hbm.at[r + 1], own_ref.at[r], sems.at[r]) for r in range(leaf_rows)
    ]
    for copy in copies:
        copy.start()
    acc_ref[...] = jnp.zeros_like(acc_ref)

    def one_leaf(row, col):
        coupling_t = cpl_t_ref[...]
        leaf = row * leaf_cols + col
        coupling_t = jnp.where(row_leaf_ref[...] == leaf, coupling_t, jnp.zeros_like(coupling_t))
        own = own_ref[row, col + 1].reshape(2 * cells, -1)
        acc_ref[...] += lax.dot_general(
            own, coupling_t, (((0,), (0,)), ((), ())), preferred_element_type=jnp.float32
        )

    for r in range(leaf_rows):
        copies[r].wait()
        lax.fori_loop(0, leaf_cols, lambda col, carry: (one_leaf(r, col), carry)[1], 0)
    volt_ref[...] = acc_ref[...].T.astype(volt_ref.dtype)


def leaf_fields(codes, scales, bordered, kernels, filament, row_leaf, coupling_t):
    leaf_count, near_count, components, cells, _ = kernels.shape
    leaf_rows = bordered.shape[0] - 2
    leaf_cols = bordered.shape[1] - 2
    port_count = bordered.shape[-1]
    slot_count = coupling_t.shape[1]
    smem = pl.BlockSpec(memory_space=pltpu.SMEM)
    hbm = pl.BlockSpec(memory_space=pl.ANY)
    vmem = pl.BlockSpec(memory_space=pltpu.VMEM)
    field = pl.pallas_call(
        leaf_kernel,
        in_specs=[smem, smem, hbm, hbm, hbm],
        out_specs=vmem,
        out_shape=jax.ShapeDtypeStruct(
            (components, leaf_rows * LEAF_R, leaf_cols * LEAF_C, port_count), jnp.bfloat16
        ),
        scratch_shapes=[
            pltpu.VMEM(bordered.shape, bordered.dtype),
            pltpu.VMEM(kernels.shape, kernels.dtype),
            pltpu.VMEM(filament.shape, filament.dtype),
            pltpu.SemaphoreType.DMA((2,)),
            pltpu.SemaphoreType.DMA((leaf_count,)),
        ],
    )(codes, scales, bordered, kernels, filament)
    field, bordered = lax.optimization_barrier((field, bordered))
    volt = pl.pallas_call(
        induced_kernel,
        in_specs=[hbm, vmem, vmem],
        out_specs=vmem,
        out_shape=jax.ShapeDtypeStruct((slot_count, port_count), jnp.bfloat16),
        scratch_shapes=[
            pltpu.VMEM((leaf_rows,) + bordered.shape[1:], bordered.dtype),
            pltpu.VMEM((port_count, slot_count), jnp.float32),
            pltpu.SemaphoreType.DMA((leaf_rows,)),
        ],
    )(bordered, row_leaf, coupling_t)
    return field, volt


def body(stream, inductance, near_lists, filament_leaf, filament_current, filament_coupling):
    port_count = stream.shape[0]
    leaf_rows = inductance.shape[0]
    leaf_cols = inductance.shape[1]
    near_count = inductance.shape[2]
    leaf_cells = inductance.shape[4]
    leaf_count = leaf_rows * leaf_cols
    half_cols = leaf_cols * LEAF_C
    nx, ny, nz = device_grid()
    gx = lax.axis_index("gx")
    col_index = lax.axis_index("gy") * nz + lax.axis_index("gz")
    owners = nx * ny * nz

    filament_count = filament_leaf.shape[0]
    capacity = max(2, 2 * filament_count // owners)
    slot_count = owners * capacity
    plane_cols = leaf_cols * ny * nz
    leaf_row = filament_leaf // plane_cols
    leaf_col = filament_leaf % plane_cols
    owner_ids = leaf_row // leaf_rows * (ny * nz) + leaf_col // leaf_cols
    local_ids = leaf_row % leaf_rows * leaf_cols + leaf_col % leaf_cols
    index = jnp.arange(filament_count, dtype=jnp.int32)
    earlier = (owner_ids[None, :] == owner_ids[:, None]) & (index[None, :] < index[:, None])
    position = jnp.sum(earlier.astype(jnp.int32), axis=1)
    target_slot = owner_ids * capacity + position
    placement_mask = target_slot[None, :] == jnp.arange(slot_count, dtype=jnp.int32)[:, None]
    placement = placement_mask.astype(jnp.bfloat16)
    row_width = 2 * leaf_cells + port_count
    rows_out = jnp.concatenate(
        [filament_coupling.reshape(filament_count, 2 * leaf_cells), filament_current], 1
    )
    sent = jnp.dot(placement, rows_out, preferred_element_type=jnp.float32).astype(jnp.bfloat16)
    sent_leaf = jnp.dot(
        placement, (local_ids + 1).astype(jnp.bfloat16), preferred_element_type=jnp.float32
    ) - 1.0
    leaf_row_block = jnp.pad(
        sent_leaf.astype(jnp.bfloat16).reshape(owners, 1, capacity),
        ((0, 0), (0, 0), (0, row_width - capacity)),
    )
    payload = jnp.concatenate([sent.reshape(owners, capacity, row_width), leaf_row_block], 1)
    got = lax.all_to_all(payload, AXES, split_axis=0, concat_axis=0, tiled=True)
    got_rows = got[:, :capacity].reshape(slot_count, row_width)
    got_leaf = got[:, capacity, :capacity].reshape(slot_count).astype(jnp.int32)
    got_coupling_t = got_rows[:, : 2 * leaf_cells].T
    got_current = got_rows[:, 2 * leaf_cells :]
    got_leaf = got_leaf.reshape(1, slot_count)
    filament = filament_field(got_leaf, got_coupling_t, got_current, leaf_count)

    window, (got_leaf, got_coupling_t, filament) = stream_window(
        stream.transpose(1, 2, 0), half_cols, (got_leaf, got_coupling_t, filament)
    )
    currents = plane_curl(window).astype(jnp.bfloat16)
    bordered = to_leaves(currents)
    src_row = jnp.arange(leaf_rows, dtype=jnp.int32)[:, None, None] + near_lists // 3
    src_col = jnp.arange(leaf_cols, dtype=jnp.int32)[None, :, None] + near_lists % 3
    row_ok = ((src_row > 0) | (gx > 0)) & ((src_row < leaf_rows + 1) | (gx < nx - 1))
    col_ok = ((src_col > 0) | (col_index > 0)) & (
        (src_col < leaf_cols + 1) | (col_index < ny * nz - 1)
    )
    scales = (row_ok & col_ok).astype(jnp.int32).reshape(leaf_count, near_count)

    kernels = inductance.reshape(leaf_count, near_count, 2, leaf_cells, leaf_cells)
    codes = near_lists.reshape(leaf_count, near_count)
    total_field, induced = leaf_fields(
        codes, scales, bordered, kernels, filament, got_leaf, got_coupling_t
    )
    returned = lax.all_to_all(
        induced.reshape(owners, capacity, port_count), AXES, split_axis=0, concat_axis=0, tiled=True
    ).reshape(slot_count, port_count)
    filament_voltage = lax.dot_general(
        placement, returned, (((0,), (0,)), ((), ())), preferred_element_type=jnp.float32
    ).astype(jnp.bfloat16)

    loop_voltage = field_halo(total_field).transpose(2, 0, 1)
    return (loop_voltage, filament_voltage)


def solution(mesh):
    return jax.shard_map(
        body,
        mesh=mesh,
        in_specs=(
            P("groups", "gx", "gy"),
            P(("groups", "gx"), ("gy", "gz"), None, None, None, None),
            P(("groups", "gx"), ("gy", "gz"), None),
            P(("groups", "gx", "gy", "gz")),
            P(("groups", "gx", "gy", "gz"), None),
            P(("groups", "gx", "gy", "gz"), None, None),
        ),
        out_specs=(P("groups", "gx", ("gy", "gz")), P(("groups", "gx", "gy", "gz"), None)),
        check_vma=False,
    )
```

```python
import jax
import jax.numpy as jnp
from jax import lax
from jax.experimental import pallas as pl
from jax.experimental.pallas import tpu as pltpu
from jax.sharding import PartitionSpec as P

LEAF_R = 8
LEAF_C = 16
AXES = ("gx", "gy", "gz")


def plane_curl(padded):
    along_y = padded[1:-1, 2:] - padded[1:-1, :-2]
    along_x = padded[:-2, 1:-1] - padded[2:, 1:-1]
    return jnp.stack([along_y, along_x])


def to_leaves(grid_values):
    components, row_count, col_count, port_count = grid_values.shape
    blocks = grid_values.reshape(
        components, row_count // LEAF_R, LEAF_R, col_count // LEAF_C, LEAF_C, port_count
    )
    blocks = blocks.transpose(1, 3, 0, 2, 4, 5)
    return blocks.reshape(
        row_count // LEAF_R, col_count // LEAF_C, components, LEAF_R * LEAF_C, port_count
    )


def from_leaves(leaves):
    leaf_rows, leaf_cols, components, leaf_cells, port_count = leaves.shape
    blocks = leaves.reshape(leaf_rows, leaf_cols, components, LEAF_R, LEAF_C, port_count)
    blocks = blocks.transpose(2, 0, 3, 1, 4, 5)
    return blocks.reshape(components, leaf_rows * LEAF_R, leaf_cols * LEAF_C, port_count)


def device_grid():
    nx, ny, nz = (lax.axis_size(a) for a in AXES)
    return nx, ny, nz


def pairs_by(fn):
    nx, ny, nz = device_grid()
    out = []
    for x in range(nx):
        for y in range(ny):
            for z in range(nz):
                target = fn(x, y, z)
                if target is None:
                    continue
                tx, ty, tz = target
                if 0 <= tx < nx and 0 <= ty < ny and 0 <= tz < nz:
                    out.append(((x * ny + y) * nz + z, (tx * ny + ty) * nz + tz))
    return out


def send(value, fn):
    return lax.ppermute(value, AXES, pairs_by(fn))


def sideways(x, y, z, dx):
    nz = lax.axis_size("gz")
    if z == nz - 1:
        return (x + dx, y + 1, 0)
    if z == 0:
        return (x + dx, y - 1, nz - 1)
    return None


def stream_window(stream, half, ready):
    gz = lax.axis_index("gz")
    rows, width = stream.shape[0], stream.shape[1]
    hr, hc = LEAF_R + 1, LEAF_C + 1
    mid_w = half + hc
    mid = lax.dynamic_slice_in_dim(stream, gz * (width - mid_w), mid_w, 1)
    side = lax.dynamic_slice_in_dim(stream, gz * (width - hc), hc, 1)
    h_got = send(side, lambda x, y, z: sideways(x, y, z, 0))
    wide = lax.dynamic_slice_in_dim(
        jnp.concatenate([h_got, mid, h_got], 1), gz * hc, mid_w + hc, 1
    )
    v_top = send(wide[rows - hr :], lambda x, y, z: (x + 1, y, z))
    v_bot = send(wide[:hr], lambda x, y, z: (x - 1, y, z))
    (v_top, v_bot), ready = lax.optimization_barrier(((v_top, v_bot), ready))
    return jnp.concatenate([v_top, wide, v_bot], 0), ready


def field_halo(grid_field):
    x_field = grid_field[0]
    y_field = grid_field[1]
    rows = y_field.shape[0]
    cols = x_field.shape[1]

    def step(x, y, z, dc):
        nz = lax.axis_size("gz")
        c = y * nz + z + dc
        return (x, c // nz, c % nz) if c >= 0 else None

    x_left = send(x_field[:, cols - 1 :], lambda x, y, z: step(x, y, z, 1))
    x_right = send(x_field[:, :1], lambda x, y, z: step(x, y, z, -1))
    y_top = send(y_field[rows - 1 :], lambda x, y, z: (x + 1, y, z))
    y_bot = send(y_field[:1], lambda x, y, z: (x - 1, y, z))
    x_pad = jnp.concatenate([x_left, x_field, x_right], 1).astype(jnp.float32)
    y_pad = jnp.concatenate([y_top, y_field, y_bot], 0).astype(jnp.float32)
    return x_pad[:, :-2] - x_pad[:, 2:] + (y_pad[2:] - y_pad[:-2])


def filament_kernel(row_leaf_ref, cpl_t_ref, cur_ref, fil_ref):
    def one_leaf(leaf, carry):
        coupling_t = cpl_t_ref[...]
        coupling_t = jnp.where(row_leaf_ref[...] == leaf, coupling_t, jnp.zeros_like(coupling_t))
        fil_ref[leaf] = jnp.dot(coupling_t, cur_ref[...], preferred_element_type=jnp.float32)
        return carry

    lax.fori_loop(0, fil_ref.shape[0], one_leaf, 0)


def filament_field(row_leaf, coupling_t, current, leaf_count):
    vmem = pl.BlockSpec(memory_space=pltpu.VMEM)
    return pl.pallas_call(
        filament_kernel,
        in_specs=[vmem, vmem, vmem],
        out_specs=vmem,
        out_shape=jax.ShapeDtypeStruct(
            (leaf_count, coupling_t.shape[0], current.shape[1]), jnp.float32
        ),
    )(row_leaf, coupling_t, current)


def leaf_kernel(
    codes_ref, scale_ref, bord_hbm, ind_hbm, fil_hbm,
    field_ref, bord_ref, ind_ref, fil_ref, sems, ind_sems,
):
    leaf_count = ind_ref.shape[0]
    leaf_cols = bord_ref.shape[1] - 2
    near_count = ind_ref.shape[1]
    cells = ind_ref.shape[3]
    first = [
        pltpu.make_async_copy(bord_hbm, bord_ref, sems.at[0]),
        pltpu.make_async_copy(fil_hbm, fil_ref, sems.at[1]),
    ]
    for copy in first:
        copy.start()
    for l in range(leaf_count):
        pltpu.make_async_copy(ind_hbm.at[l], ind_ref.at[l], ind_sems.at[l]).start()
    for copy in first:
        copy.wait()

    def one_leaf(leaf, carry):
        pltpu.make_async_copy(ind_hbm.at[leaf], ind_ref.at[leaf], ind_sems.at[leaf]).wait()
        row = leaf // leaf_cols
        col = leaf % leaf_cols
        filament = fil_ref[leaf]
        sources = []
        for n in range(near_count):
            code = codes_ref[leaf, n]
            src_row = jnp.minimum(jnp.maximum(row + code // 3, 0), bord_ref.shape[0] - 1)
            src_col = jnp.minimum(jnp.maximum(col + code % 3, 0), bord_ref.shape[1] - 1)
            keep = scale_ref[leaf, n] > 0
            tile = bord_ref[src_row, src_col]
            sources.append(jnp.where(keep, tile, jnp.zeros_like(tile)))
        for c in range(2):
            weights = jnp.concatenate([ind_ref[leaf, n, c] for n in range(near_count)], axis=1)
            stacked = jnp.concatenate([s[c] for s in sources], axis=0)
            total = filament[c * cells : (c + 1) * cells] + jnp.dot(
                weights, stacked, preferred_element_type=jnp.float32
            )
            field_ref[c, pl.ds(row * LEAF_R, LEAF_R), pl.ds(pl.multiple_of(col * LEAF_C, LEAF_C), LEAF_C)] = (
                total.reshape(LEAF_R, LEAF_C, -1).astype(field_ref.dtype)
            )
        return carry

    lax.fori_loop(0, leaf_count, one_leaf, 0)


def induced_kernel(bord_hbm, col_leaf_ref, cpl_ref, volt_ref, own_ref, acc_ref, sems):
    leaf_rows = own_ref.shape[0]
    leaf_cols = own_ref.shape[1] - 2
    cells = own_ref.shape[3]
    copies = [
        pltpu.make_async_copy(bord_hbm.at[r + 1], own_ref.at[r], sems.at[r]) for r in range(leaf_rows)
    ]
    for copy in copies:
        copy.start()
    acc_ref[...] = jnp.zeros_like(acc_ref)

    def one_leaf(row, col):
        coupling = cpl_ref[...]
        leaf = row * leaf_cols + col
        coupling = jnp.where(col_leaf_ref[...] == leaf, coupling, jnp.zeros_like(coupling))
        own = own_ref[row, col + 1].reshape(2 * cells, -1)
        acc_ref[...] += jnp.dot(coupling, own, preferred_element_type=jnp.float32)

    for r in range(leaf_rows):
        copies[r].wait()
        lax.fori_loop(0, leaf_cols, lambda col, carry: (one_leaf(r, col), carry)[1], 0)
    volt_ref[...] = acc_ref[...].astype(volt_ref.dtype)


def leaf_fields(codes, scales, bordered, kernels, filament, col_leaf, coupling):
    leaf_count, near_count, components, cells, _ = kernels.shape
    leaf_rows = bordered.shape[0] - 2
    leaf_cols = bordered.shape[1] - 2
    port_count = bordered.shape[-1]
    slot_count = coupling.shape[0]
    smem = pl.BlockSpec(memory_space=pltpu.SMEM)
    hbm = pl.BlockSpec(memory_space=pl.ANY)
    vmem = pl.BlockSpec(memory_space=pltpu.VMEM)
    field = pl.pallas_call(
        leaf_kernel,
        in_specs=[smem, smem, hbm, hbm, hbm],
        out_specs=vmem,
        out_shape=jax.ShapeDtypeStruct(
            (components, leaf_rows * LEAF_R, leaf_cols * LEAF_C, port_count), jnp.bfloat16
        ),
        scratch_shapes=[
            pltpu.VMEM(bordered.shape, bordered.dtype),
            pltpu.VMEM(kernels.shape, kernels.dtype),
            pltpu.VMEM(filament.shape, filament.dtype),
            pltpu.SemaphoreType.DMA((2,)),
            pltpu.SemaphoreType.DMA((leaf_count,)),
        ],
    )(codes, scales, bordered, kernels, filament)
    field, bordered = lax.optimization_barrier((field, bordered))
    volt = pl.pallas_call(
        induced_kernel,
        in_specs=[hbm, vmem, vmem],
        out_specs=vmem,
        out_shape=jax.ShapeDtypeStruct((slot_count, port_count), jnp.bfloat16),
        scratch_shapes=[
            pltpu.VMEM((leaf_rows,) + bordered.shape[1:], bordered.dtype),
            pltpu.VMEM((slot_count, port_count), jnp.float32),
            pltpu.SemaphoreType.DMA((leaf_rows,)),
        ],
    )(bordered, col_leaf, coupling)
    return field, volt


def body(stream, inductance, near_lists, filament_leaf, filament_current, filament_coupling):
    port_count = stream.shape[0]
    leaf_rows = inductance.shape[0]
    leaf_cols = inductance.shape[1]
    near_count = inductance.shape[2]
    leaf_cells = inductance.shape[4]
    leaf_count = leaf_rows * leaf_cols
    half_cols = leaf_cols * LEAF_C
    nx, ny, nz = device_grid()
    gx = lax.axis_index("gx")
    col_index = lax.axis_index("gy") * nz + lax.axis_index("gz")
    owners = nx * ny * nz

    filament_count = filament_leaf.shape[0]
    capacity = max(2, 2 * filament_count // owners)
    slot_count = owners * capacity
    plane_cols = leaf_cols * ny * nz
    leaf_row = filament_leaf // plane_cols
    leaf_col = filament_leaf % plane_cols
    owner_ids = leaf_row // leaf_rows * (ny * nz) + leaf_col // leaf_cols
    local_ids = leaf_row % leaf_rows * leaf_cols + leaf_col % leaf_cols
    index = jnp.arange(filament_count, dtype=jnp.int32)
    earlier = (owner_ids[None, :] == owner_ids[:, None]) & (index[None, :] < index[:, None])
    position = jnp.sum(earlier.astype(jnp.int32), axis=1)
    target_slot = owner_ids * capacity + position
    placement_mask = target_slot[None, :] == jnp.arange(slot_count, dtype=jnp.int32)[:, None]
    placement = placement_mask.astype(jnp.bfloat16)
    row_width = 2 * leaf_cells + port_count
    rows_out = jnp.concatenate(
        [filament_coupling.reshape(filament_count, 2 * leaf_cells), filament_current], 1
    )
    sent = jnp.dot(placement, rows_out, preferred_element_type=jnp.float32).astype(jnp.bfloat16)
    sent_leaf = jnp.dot(
        placement, (local_ids + 1).astype(jnp.bfloat16), preferred_element_type=jnp.float32
    ) - 1.0
    leaf_row_block = jnp.pad(
        sent_leaf.astype(jnp.bfloat16).reshape(owners, 1, capacity),
        ((0, 0), (0, 0), (0, row_width - capacity)),
    )
    payload = jnp.concatenate([sent.reshape(owners, capacity, row_width), leaf_row_block], 1)
    got = lax.all_to_all(payload, AXES, split_axis=0, concat_axis=0, tiled=True)
    got_rows = got[:, :capacity].reshape(slot_count, row_width)
    got_leaf = got[:, capacity, :capacity].reshape(slot_count).astype(jnp.int32)
    got_coupling_t = got_rows[:, : 2 * leaf_cells].T
    got_current = got_rows[:, 2 * leaf_cells :]
    got_coupling = got_rows[:, : 2 * leaf_cells]
    col_leaf = got_leaf.reshape(slot_count, 1)
    got_leaf = got_leaf.reshape(1, slot_count)
    filament = filament_field(got_leaf, got_coupling_t, got_current, leaf_count)

    window, (col_leaf, got_coupling, filament) = stream_window(
        stream.transpose(1, 2, 0), half_cols, (col_leaf, got_coupling, filament)
    )
    currents = plane_curl(window).astype(jnp.bfloat16)
    bordered = to_leaves(currents)
    src_row = jnp.arange(leaf_rows, dtype=jnp.int32)[:, None, None] + near_lists // 3
    src_col = jnp.arange(leaf_cols, dtype=jnp.int32)[None, :, None] + near_lists % 3
    row_ok = ((src_row > 0) | (gx > 0)) & ((src_row < leaf_rows + 1) | (gx < nx - 1))
    col_ok = ((src_col > 0) | (col_index > 0)) & (
        (src_col < leaf_cols + 1) | (col_index < ny * nz - 1)
    )
    scales = (row_ok & col_ok).astype(jnp.int32).reshape(leaf_count, near_count)

    kernels = inductance.reshape(leaf_count, near_count, 2, leaf_cells, leaf_cells)
    codes = near_lists.reshape(leaf_count, near_count)
    total_field, induced = leaf_fields(
        codes, scales, bordered, kernels, filament, col_leaf, got_coupling
    )
    returned = lax.all_to_all(
        induced.reshape(owners, capacity, port_count), AXES, split_axis=0, concat_axis=0, tiled=True
    ).reshape(slot_count, port_count)
    filament_voltage = lax.dot_general(
        placement, returned, (((0,), (0,)), ((), ())), preferred_element_type=jnp.float32
    ).astype(jnp.bfloat16)

    loop_voltage = field_halo(total_field).transpose(2, 0, 1)
    return (loop_voltage, filament_voltage)


def solution(mesh):
    return jax.shard_map(
        body,
        mesh=mesh,
        in_specs=(
            P("groups", "gx", "gy"),
            P(("groups", "gx"), ("gy", "gz"), None, None, None, None),
            P(("groups", "gx"), ("gy", "gz"), None),
            P(("groups", "gx", "gy", "gz")),
            P(("groups", "gx", "gy", "gz"), None),
            P(("groups", "gx", "gy", "gz"), None, None),
        ),
        out_specs=(P("groups", "gx", ("gy", "gz")), P(("groups", "gx", "gy", "gz"), None)),
        check_vma=False,
    )
```

```python
import jax
import jax.numpy as jnp
from jax import lax
from jax.experimental import pallas as pl
from jax.experimental.pallas import tpu as pltpu
from jax.sharding import PartitionSpec as P

LEAF_R = 8
LEAF_C = 16
AXES = ("gx", "gy", "gz")


def plane_curl(padded):
    along_y = padded[1:-1, 2:] - padded[1:-1, :-2]
    along_x = padded[:-2, 1:-1] - padded[2:, 1:-1]
    return jnp.stack([along_y, along_x])


def to_leaves(grid_values):
    components, row_count, col_count, port_count = grid_values.shape
    blocks = grid_values.reshape(
        components, row_count // LEAF_R, LEAF_R, col_count // LEAF_C, LEAF_C, port_count
    )
    blocks = blocks.transpose(1, 3, 0, 2, 4, 5)
    return blocks.reshape(
        row_count // LEAF_R, col_count // LEAF_C, components, LEAF_R * LEAF_C, port_count
    )


def from_leaves(leaves):
    leaf_rows, leaf_cols, components, leaf_cells, port_count = leaves.shape
    blocks = leaves.reshape(leaf_rows, leaf_cols, components, LEAF_R, LEAF_C, port_count)
    blocks = blocks.transpose(2, 0, 3, 1, 4, 5)
    return blocks.reshape(components, leaf_rows * LEAF_R, leaf_cols * LEAF_C, port_count)


def device_grid():
    nx, ny, nz = (lax.axis_size(a) for a in AXES)
    return nx, ny, nz


def pairs_by(fn):
    nx, ny, nz = device_grid()
    out = []
    for x in range(nx):
        for y in range(ny):
            for z in range(nz):
                target = fn(x, y, z)
                if target is None:
                    continue
                tx, ty, tz = target
                if 0 <= tx < nx and 0 <= ty < ny and 0 <= tz < nz:
                    out.append(((x * ny + y) * nz + z, (tx * ny + ty) * nz + tz))
    return out


def send(value, fn):
    return lax.ppermute(value, AXES, pairs_by(fn))


def sideways(x, y, z, dx):
    nz = lax.axis_size("gz")
    if z == nz - 1:
        return (x + dx, y + 1, 0)
    if z == 0:
        return (x + dx, y - 1, nz - 1)
    return None


def stream_window(stream, half, ready):
    gz = lax.axis_index("gz")
    rows, width = stream.shape[0], stream.shape[1]
    hr, hc = LEAF_R + 1, LEAF_C + 1
    mid_w = half + hc
    mid = lax.dynamic_slice_in_dim(stream, gz * (width - mid_w), mid_w, 1)
    side = lax.dynamic_slice_in_dim(stream, gz * (width - hc), hc, 1)
    h_got = send(side, lambda x, y, z: sideways(x, y, z, 0))
    wide = lax.dynamic_slice_in_dim(
        jnp.concatenate([h_got, mid, h_got], 1), gz * hc, mid_w + hc, 1
    )
    v_top = send(wide[rows - hr :], lambda x, y, z: (x + 1, y, z))
    v_bot = send(wide[:hr], lambda x, y, z: (x - 1, y, z))
    (v_top, v_bot), ready = lax.optimization_barrier(((v_top, v_bot), ready))
    return jnp.concatenate([v_top, wide, v_bot], 0), ready


def field_halo(grid_field):
    x_field = grid_field[0]
    y_field = grid_field[1]
    rows = y_field.shape[0]
    cols = x_field.shape[1]

    def step(x, y, z, dc):
        nz = lax.axis_size("gz")
        c = y * nz + z + dc
        return (x, c // nz, c % nz) if c >= 0 else None

    x_left = send(x_field[:, cols - 1 :], lambda x, y, z: step(x, y, z, 1))
    x_right = send(x_field[:, :1], lambda x, y, z: step(x, y, z, -1))
    y_top = send(y_field[rows - 1 :], lambda x, y, z: (x + 1, y, z))
    y_bot = send(y_field[:1], lambda x, y, z: (x - 1, y, z))
    x_pad = jnp.concatenate([x_left, x_field, x_right], 1).astype(jnp.float32)
    y_pad = jnp.concatenate([y_top, y_field, y_bot], 0).astype(jnp.float32)
    return x_pad[:, :-2] - x_pad[:, 2:] + (y_pad[2:] - y_pad[:-2])


def filament_kernel(row_leaf_ref, cpl_t_ref, cur_ref, fil_ref):
    def one_leaf(leaf, carry):
        coupling_t = cpl_t_ref[...]
        coupling_t = jnp.where(row_leaf_ref[...] == leaf, coupling_t, jnp.zeros_like(coupling_t))
        fil_ref[leaf] = jnp.dot(coupling_t, cur_ref[...], preferred_element_type=jnp.float32)
        return carry

    lax.fori_loop(0, fil_ref.shape[0], one_leaf, 0)


def filament_field(row_leaf, coupling_t, current, leaf_count):
    vmem = pl.BlockSpec(memory_space=pltpu.VMEM)
    return pl.pallas_call(
        filament_kernel,
        in_specs=[vmem, vmem, vmem],
        out_specs=vmem,
        out_shape=jax.ShapeDtypeStruct(
            (leaf_count, coupling_t.shape[0], current.shape[1]), jnp.float32
        ),
    )(row_leaf, coupling_t, current)


def leaf_kernel(
    codes_ref, scale_ref, bord_hbm, ind_hbm, fil_hbm,
    field_ref, bord_ref, ind_ref, fil_ref, sems, fil_sems, ind_sems,
):
    leaf_count = ind_ref.shape[0]
    leaf_cols = bord_ref.shape[1] - 2
    near_count = ind_ref.shape[1]
    cells = ind_ref.shape[3]
    ring_rows = bord_ref.shape[0]

    def row_copy(r):
        return pltpu.make_async_copy(bord_hbm.at[r], bord_ref.at[r], sems.at[r])

    def fil_copy(l):
        return pltpu.make_async_copy(fil_hbm.at[l], fil_ref.at[l], fil_sems.at[l])

    for r in range(ring_rows):
        row_copy(r).start()
    for l in range(leaf_count):
        fil_copy(l).start()
        pltpu.make_async_copy(ind_hbm.at[l], ind_ref.at[l], ind_sems.at[l]).start()
    for r in range(3):
        row_copy(r).wait()

    def one_leaf(leaf, carry):
        row = leaf // leaf_cols
        col = leaf % leaf_cols

        @pl.when((col == 0) & (row > 0))
        def _():
            row_copy(row + 2).wait()

        fil_copy(leaf).wait()
        pltpu.make_async_copy(ind_hbm.at[leaf], ind_ref.at[leaf], ind_sems.at[leaf]).wait()
        filament = fil_ref[leaf]
        sources = []
        for n in range(near_count):
            code = codes_ref[leaf, n]
            src_row = jnp.minimum(jnp.maximum(row + code // 3, 0), bord_ref.shape[0] - 1)
            src_col = jnp.minimum(jnp.maximum(col + code % 3, 0), bord_ref.shape[1] - 1)
            keep = scale_ref[leaf, n] > 0
            tile = bord_ref[src_row, src_col]
            sources.append(jnp.where(keep, tile, jnp.zeros_like(tile)))
        for c in range(2):
            weights = jnp.concatenate([ind_ref[leaf, n, c] for n in range(near_count)], axis=1)
            stacked = jnp.concatenate([s[c] for s in sources], axis=0)
            total = filament[c * cells : (c + 1) * cells] + jnp.dot(
                weights, stacked, preferred_element_type=jnp.float32
            )
            field_ref[c, pl.ds(row * LEAF_R, LEAF_R), pl.ds(pl.multiple_of(col * LEAF_C, LEAF_C), LEAF_C)] = (
                total.reshape(LEAF_R, LEAF_C, -1).astype(field_ref.dtype)
            )
        return carry

    lax.fori_loop(0, leaf_count, one_leaf, 0)


def induced_kernel(bord_hbm, row_leaf_ref, cpl_t_ref, volt_ref, own_ref, acc_ref, sems):
    leaf_rows = own_ref.shape[0]
    leaf_cols = own_ref.shape[1] - 2
    cells = own_ref.shape[3]
    copies = [
        pltpu.make_async_copy(bord_hbm.at[r + 1], own_ref.at[r], sems.at[r]) for r in range(leaf_rows)
    ]
    for copy in copies:
        copy.start()
    acc_ref[...] = jnp.zeros_like(acc_ref)

    def one_leaf(row, col):
        coupling_t = cpl_t_ref[...]
        leaf = row * leaf_cols + col
        coupling_t = jnp.where(row_leaf_ref[...] == leaf, coupling_t, jnp.zeros_like(coupling_t))
        own = own_ref[row, col + 1].reshape(2 * cells, -1)
        acc_ref[...] += lax.dot_general(
            own, coupling_t, (((0,), (0,)), ((), ())), preferred_element_type=jnp.float32
        )

    for r in range(leaf_rows):
        copies[r].wait()
        lax.fori_loop(0, leaf_cols, lambda col, carry: (one_leaf(r, col), carry)[1], 0)
    volt_ref[...] = acc_ref[...].T.astype(volt_ref.dtype)


def leaf_fields(codes, scales, bordered, kernels, filament, row_leaf, coupling_t):
    leaf_count, near_count, components, cells, _ = kernels.shape
    leaf_rows = bordered.shape[0] - 2
    leaf_cols = bordered.shape[1] - 2
    port_count = bordered.shape[-1]
    slot_count = coupling_t.shape[1]
    smem = pl.BlockSpec(memory_space=pltpu.SMEM)
    hbm = pl.BlockSpec(memory_space=pl.ANY)
    vmem = pl.BlockSpec(memory_space=pltpu.VMEM)
    field = pl.pallas_call(
        leaf_kernel,
        in_specs=[smem, smem, hbm, hbm, hbm],
        out_specs=vmem,
        out_shape=jax.ShapeDtypeStruct(
            (components, leaf_rows * LEAF_R, leaf_cols * LEAF_C, port_count), jnp.bfloat16
        ),
        scratch_shapes=[
            pltpu.VMEM(bordered.shape, bordered.dtype),
            pltpu.VMEM(kernels.shape, kernels.dtype),
            pltpu.VMEM(filament.shape, filament.dtype),
            pltpu.SemaphoreType.DMA((leaf_rows + 2,)),
            pltpu.SemaphoreType.DMA((leaf_count,)),
            pltpu.SemaphoreType.DMA((leaf_count,)),
        ],
    )(codes, scales, bordered, kernels, filament)
    field, bordered = lax.optimization_barrier((field, bordered))
    volt = pl.pallas_call(
        induced_kernel,
        in_specs=[hbm, vmem, vmem],
        out_specs=vmem,
        out_shape=jax.ShapeDtypeStruct((slot_count, port_count), jnp.bfloat16),
        scratch_shapes=[
            pltpu.VMEM((leaf_rows,) + bordered.shape[1:], bordered.dtype),
            pltpu.VMEM((port_count, slot_count), jnp.float32),
            pltpu.SemaphoreType.DMA((leaf_rows,)),
        ],
    )(bordered, row_leaf, coupling_t)
    return field, volt


def body(stream, inductance, near_lists, filament_leaf, filament_current, filament_coupling):
    port_count = stream.shape[0]
    leaf_rows = inductance.shape[0]
    leaf_cols = inductance.shape[1]
    near_count = inductance.shape[2]
    leaf_cells = inductance.shape[4]
    leaf_count = leaf_rows * leaf_cols
    half_cols = leaf_cols * LEAF_C
    nx, ny, nz = device_grid()
    gx = lax.axis_index("gx")
    col_index = lax.axis_index("gy") * nz + lax.axis_index("gz")
    owners = nx * ny * nz

    filament_count = filament_leaf.shape[0]
    capacity = max(2, 2 * filament_count // owners)
    slot_count = owners * capacity
    plane_cols = leaf_cols * ny * nz
    leaf_row = filament_leaf // plane_cols
    leaf_col = filament_leaf % plane_cols
    owner_ids = leaf_row // leaf_rows * (ny * nz) + leaf_col // leaf_cols
    local_ids = leaf_row % leaf_rows * leaf_cols + leaf_col % leaf_cols
    index = jnp.arange(filament_count, dtype=jnp.int32)
    earlier = (owner_ids[None, :] == owner_ids[:, None]) & (index[None, :] < index[:, None])
    position = jnp.sum(earlier.astype(jnp.int32), axis=1)
    target_slot = owner_ids * capacity + position
    placement_mask = target_slot[None, :] == jnp.arange(slot_count, dtype=jnp.int32)[:, None]
    placement = placement_mask.astype(jnp.bfloat16)
    row_width = 2 * leaf_cells + port_count
    rows_out = jnp.concatenate(
        [filament_coupling.reshape(filament_count, 2 * leaf_cells), filament_current], 1
    )
    sent = jnp.dot(placement, rows_out, preferred_element_type=jnp.float32).astype(jnp.bfloat16)
    sent_leaf = jnp.dot(
        placement, (local_ids + 1).astype(jnp.bfloat16), preferred_element_type=jnp.float32
    ) - 1.0
    leaf_row_block = jnp.pad(
        sent_leaf.astype(jnp.bfloat16).reshape(owners, 1, capacity),
        ((0, 0), (0, 0), (0, row_width - capacity)),
    )
    payload = jnp.concatenate([sent.reshape(owners, capacity, row_width), leaf_row_block], 1)
    got = lax.all_to_all(payload, AXES, split_axis=0, concat_axis=0, tiled=True)
    got_rows = got[:, :capacity].reshape(slot_count, row_width)
    got_leaf = got[:, capacity, :capacity].reshape(slot_count).astype(jnp.int32)
    got_coupling_t = got_rows[:, : 2 * leaf_cells].T
    got_current = got_rows[:, 2 * leaf_cells :]
    got_leaf = got_leaf.reshape(1, slot_count)
    filament = filament_field(got_leaf, got_coupling_t, got_current, leaf_count)

    window, (got_leaf, got_coupling_t, filament) = stream_window(
        stream.transpose(1, 2, 0), half_cols, (got_leaf, got_coupling_t, filament)
    )
    currents = plane_curl(window).astype(jnp.bfloat16)
    bordered = to_leaves(currents)
    src_row = jnp.arange(leaf_rows, dtype=jnp.int32)[:, None, None] + near_lists // 3
    src_col = jnp.arange(leaf_cols, dtype=jnp.int32)[None, :, None] + near_lists % 3
    row_ok = ((src_row > 0) | (gx > 0)) & ((src_row < leaf_rows + 1) | (gx < nx - 1))
    col_ok = ((src_col > 0) | (col_index > 0)) & (
        (src_col < leaf_cols + 1) | (col_index < ny * nz - 1)
    )
    scales = (row_ok & col_ok).astype(jnp.int32).reshape(leaf_count, near_count)

    kernels = inductance.reshape(leaf_count, near_count, 2, leaf_cells, leaf_cells)
    codes = near_lists.reshape(leaf_count, near_count)
    total_field, induced = leaf_fields(
        codes, scales, bordered, kernels, filament, got_leaf, got_coupling_t
    )
    returned = lax.all_to_all(
        induced.reshape(owners, capacity, port_count), AXES, split_axis=0, concat_axis=0, tiled=True
    ).reshape(slot_count, port_count)
    filament_voltage = lax.dot_general(
        placement, returned, (((0,), (0,)), ((), ())), preferred_element_type=jnp.float32
    ).astype(jnp.bfloat16)

    loop_voltage = field_halo(total_field).transpose(2, 0, 1)
    return (loop_voltage, filament_voltage)


def solution(mesh):
    return jax.shard_map(
        body,
        mesh=mesh,
        in_specs=(
            P("groups", "gx", "gy"),
            P(("groups", "gx"), ("gy", "gz"), None, None, None, None),
            P(("groups", "gx"), ("gy", "gz"), None),
            P(("groups", "gx", "gy", "gz")),
            P(("groups", "gx", "gy", "gz"), None),
            P(("groups", "gx", "gy", "gz"), None, None),
        ),
        out_specs=(P("groups", "gx", ("gy", "gz")), P(("groups", "gx", "gy", "gz"), None)),
        check_vma=False,
    )
```

```python
import jax
import jax.numpy as jnp
from jax import lax
from jax.experimental import pallas as pl
from jax.experimental.pallas import tpu as pltpu
from jax.sharding import PartitionSpec as P

LEAF_R = 8
LEAF_C = 16
AXES = ("gx", "gy", "gz")


def plane_curl(padded):
    along_y = padded[1:-1, 2:] - padded[1:-1, :-2]
    along_x = padded[:-2, 1:-1] - padded[2:, 1:-1]
    return jnp.stack([along_y, along_x])


def to_leaves(grid_values):
    components, row_count, col_count, port_count = grid_values.shape
    blocks = grid_values.reshape(
        components, row_count // LEAF_R, LEAF_R, col_count // LEAF_C, LEAF_C, port_count
    )
    blocks = blocks.transpose(1, 3, 0, 2, 4, 5)
    return blocks.reshape(
        row_count // LEAF_R, col_count // LEAF_C, components, LEAF_R * LEAF_C, port_count
    )


def from_leaves(leaves):
    leaf_rows, leaf_cols, components, leaf_cells, port_count = leaves.shape
    blocks = leaves.reshape(leaf_rows, leaf_cols, components, LEAF_R, LEAF_C, port_count)
    blocks = blocks.transpose(2, 0, 3, 1, 4, 5)
    return blocks.reshape(components, leaf_rows * LEAF_R, leaf_cols * LEAF_C, port_count)


def device_grid():
    nx, ny, nz = (lax.axis_size(a) for a in AXES)
    return nx, ny, nz


def pairs_by(fn):
    nx, ny, nz = device_grid()
    out = []
    for x in range(nx):
        for y in range(ny):
            for z in range(nz):
                target = fn(x, y, z)
                if target is None:
                    continue
                tx, ty, tz = target
                if 0 <= tx < nx and 0 <= ty < ny and 0 <= tz < nz:
                    out.append(((x * ny + y) * nz + z, (tx * ny + ty) * nz + tz))
    return out


def send(value, fn):
    return lax.ppermute(value, AXES, pairs_by(fn))


def sideways(x, y, z, dx):
    nz = lax.axis_size("gz")
    if z == nz - 1:
        return (x + dx, y + 1, 0)
    if z == 0:
        return (x + dx, y - 1, nz - 1)
    return None


def stream_window(stream, half, ready):
    gz = lax.axis_index("gz")
    rows, width = stream.shape[0], stream.shape[1]
    hr, hc = LEAF_R + 1, LEAF_C + 1
    mid_w = half + hc
    mid = lax.dynamic_slice_in_dim(stream, gz * (width - mid_w), mid_w, 1)
    side = lax.dynamic_slice_in_dim(stream, gz * (width - hc), hc, 1)
    h_got = send(side, lambda x, y, z: sideways(x, y, z, 0))
    wide = lax.dynamic_slice_in_dim(
        jnp.concatenate([h_got, mid, h_got], 1), gz * hc, mid_w + hc, 1
    )
    v_top = send(wide[rows - hr :], lambda x, y, z: (x + 1, y, z))
    v_bot = send(wide[:hr], lambda x, y, z: (x - 1, y, z))
    (v_top, v_bot), ready = lax.optimization_barrier(((v_top, v_bot), ready))
    return jnp.concatenate([v_top, wide, v_bot], 0), ready


def field_halo(grid_field):
    x_field = grid_field[0]
    y_field = grid_field[1]
    rows = y_field.shape[0]
    cols = x_field.shape[1]

    def step(x, y, z, dc):
        nz = lax.axis_size("gz")
        c = y * nz + z + dc
        return (x, c // nz, c % nz) if c >= 0 else None

    x_left = send(x_field[:, cols - 1 :], lambda x, y, z: step(x, y, z, 1))
    x_right = send(x_field[:, :1], lambda x, y, z: step(x, y, z, -1))
    y_top = send(y_field[rows - 1 :], lambda x, y, z: (x + 1, y, z))
    y_bot = send(y_field[:1], lambda x, y, z: (x - 1, y, z))
    x_pad = jnp.concatenate([x_left, x_field, x_right], 1).astype(jnp.float32)
    y_pad = jnp.concatenate([y_top, y_field, y_bot], 0).astype(jnp.float32)
    return x_pad[:, :-2] - x_pad[:, 2:] + (y_pad[2:] - y_pad[:-2])


def filament_kernel(row_leaf_ref, cpl_t_ref, cur_ref, fil_ref):
    def one_leaf(leaf, carry):
        coupling_t = cpl_t_ref[...]
        coupling_t = jnp.where(row_leaf_ref[...] == leaf, coupling_t, jnp.zeros_like(coupling_t))
        fil_ref[leaf] = jnp.dot(coupling_t, cur_ref[...], preferred_element_type=jnp.float32)
        return carry

    lax.fori_loop(0, fil_ref.shape[0], one_leaf, 0)


def filament_field(row_leaf, coupling_t, current, leaf_count):
    vmem = pl.BlockSpec(memory_space=pltpu.VMEM)
    return pl.pallas_call(
        filament_kernel,
        in_specs=[vmem, vmem, vmem],
        out_specs=vmem,
        out_shape=jax.ShapeDtypeStruct(
            (leaf_count, coupling_t.shape[0], current.shape[1]), jnp.float32
        ),
    )(row_leaf, coupling_t, current)


def leaf_kernel(
    codes_ref, scale_ref, bord_hbm, ind_hbm, fil_hbm,
    field_ref, bord_ref, ind_ref, fil_ref, sems, fil_sems, ind_sems,
):
    leaf_count = ind_ref.shape[0]
    leaf_cols = bord_ref.shape[1] - 2
    near_count = ind_ref.shape[1]
    cells = ind_ref.shape[3]
    ring_rows = bord_ref.shape[0]

    def row_copy(r):
        return pltpu.make_async_copy(bord_hbm.at[r], bord_ref.at[r], sems.at[r])

    def fil_copy(l):
        return pltpu.make_async_copy(fil_hbm.at[l], fil_ref.at[l], fil_sems.at[l])

    for r in range(ring_rows):
        row_copy(r).start()
    for l in range(leaf_count):
        fil_copy(l).start()
        pltpu.make_async_copy(ind_hbm.at[l], ind_ref.at[l], ind_sems.at[l]).start()
    for r in range(3):
        row_copy(r).wait()

    def one_leaf(leaf, carry):
        row = leaf // leaf_cols
        col = leaf % leaf_cols

        @pl.when((col == 0) & (row > 0))
        def _():
            row_copy(row + 2).wait()

        fil_copy(leaf).wait()
        pltpu.make_async_copy(ind_hbm.at[leaf], ind_ref.at[leaf], ind_sems.at[leaf]).wait()
        filament = fil_ref[leaf]
        sources = []
        for n in range(near_count):
            code = codes_ref[leaf, n]
            src_row = jnp.minimum(jnp.maximum(row + code // 3, 0), bord_ref.shape[0] - 1)
            src_col = jnp.minimum(jnp.maximum(col + code % 3, 0), bord_ref.shape[1] - 1)
            keep = scale_ref[leaf, n] > 0
            tile = bord_ref[src_row, src_col]
            sources.append(jnp.where(keep, tile, jnp.zeros_like(tile)))
        for c in range(2):
            weights = jnp.concatenate([ind_ref[leaf, n, c] for n in range(near_count)], axis=1)
            stacked = jnp.concatenate([s[c] for s in sources], axis=0)
            total = filament[c * cells : (c + 1) * cells] + jnp.dot(
                weights, stacked, preferred_element_type=jnp.float32
            )
            field_ref[c, pl.ds(row * LEAF_R, LEAF_R), pl.ds(pl.multiple_of(col * LEAF_C, LEAF_C), LEAF_C)] = (
                total.reshape(LEAF_R, LEAF_C, -1).astype(field_ref.dtype)
            )
        return carry

    lax.fori_loop(0, leaf_count, one_leaf, 0)


def induced_kernel(bord_hbm, row_leaf_ref, cpl_t_ref, volt_ref, own_ref, stack_ref, sems):
    leaf_rows = own_ref.shape[0]
    leaf_cols = own_ref.shape[1] - 2
    copies = [
        pltpu.make_async_copy(bord_hbm.at[r + 1], own_ref.at[r], sems.at[r]) for r in range(leaf_rows)
    ]
    for copy in copies:
        copy.start()
    coupling_t = cpl_t_ref[...]
    slot_leaf = row_leaf_ref[...]
    for leaf in range(leaf_rows * leaf_cols):
        stack_ref[leaf] = jnp.where(slot_leaf == leaf, coupling_t, jnp.zeros_like(coupling_t))
    for copy in copies:
        copy.wait()
    own = own_ref[:, 1 : leaf_cols + 1].reshape(-1, own_ref.shape[-1])
    stacked = stack_ref[...].reshape(own.shape[0], -1)
    volt = lax.dot_general(
        own, stacked, (((0,), (0,)), ((), ())), preferred_element_type=jnp.float32
    )
    volt_ref[...] = volt.T.astype(volt_ref.dtype)


def leaf_fields(codes, scales, bordered, kernels, filament, row_leaf, coupling_t):
    leaf_count, near_count, components, cells, _ = kernels.shape
    leaf_rows = bordered.shape[0] - 2
    leaf_cols = bordered.shape[1] - 2
    port_count = bordered.shape[-1]
    slot_count = coupling_t.shape[1]
    smem = pl.BlockSpec(memory_space=pltpu.SMEM)
    hbm = pl.BlockSpec(memory_space=pl.ANY)
    vmem = pl.BlockSpec(memory_space=pltpu.VMEM)
    field = pl.pallas_call(
        leaf_kernel,
        in_specs=[smem, smem, hbm, hbm, hbm],
        out_specs=vmem,
        out_shape=jax.ShapeDtypeStruct(
            (components, leaf_rows * LEAF_R, leaf_cols * LEAF_C, port_count), jnp.bfloat16
        ),
        scratch_shapes=[
            pltpu.VMEM(bordered.shape, bordered.dtype),
            pltpu.VMEM(kernels.shape, kernels.dtype),
            pltpu.VMEM(filament.shape, filament.dtype),
            pltpu.SemaphoreType.DMA((leaf_rows + 2,)),
            pltpu.SemaphoreType.DMA((leaf_count,)),
            pltpu.SemaphoreType.DMA((leaf_count,)),
        ],
    )(codes, scales, bordered, kernels, filament)
    field, bordered = lax.optimization_barrier((field, bordered))
    volt = pl.pallas_call(
        induced_kernel,
        in_specs=[hbm, vmem, vmem],
        out_specs=vmem,
        out_shape=jax.ShapeDtypeStruct((slot_count, port_count), jnp.bfloat16),
        scratch_shapes=[
            pltpu.VMEM((leaf_rows,) + bordered.shape[1:], bordered.dtype),
            pltpu.VMEM((leaf_count,) + coupling_t.shape, coupling_t.dtype),
            pltpu.SemaphoreType.DMA((leaf_rows,)),
        ],
    )(bordered, row_leaf, coupling_t)
    return field, volt


def body(stream, inductance, near_lists, filament_leaf, filament_current, filament_coupling):
    port_count = stream.shape[0]
    leaf_rows = inductance.shape[0]
    leaf_cols = inductance.shape[1]
    near_count = inductance.shape[2]
    leaf_cells = inductance.shape[4]
    leaf_count = leaf_rows * leaf_cols
    half_cols = leaf_cols * LEAF_C
    nx, ny, nz = device_grid()
    gx = lax.axis_index("gx")
    col_index = lax.axis_index("gy") * nz + lax.axis_index("gz")
    owners = nx * ny * nz

    filament_count = filament_leaf.shape[0]
    capacity = max(2, 2 * filament_count // owners)
    slot_count = owners * capacity
    plane_cols = leaf_cols * ny * nz
    leaf_row = filament_leaf // plane_cols
    leaf_col = filament_leaf % plane_cols
    owner_ids = leaf_row // leaf_rows * (ny * nz) + leaf_col // leaf_cols
    local_ids = leaf_row % leaf_rows * leaf_cols + leaf_col % leaf_cols
    index = jnp.arange(filament_count, dtype=jnp.int32)
    earlier = (owner_ids[None, :] == owner_ids[:, None]) & (index[None, :] < index[:, None])
    position = jnp.sum(earlier.astype(jnp.int32), axis=1)
    target_slot = owner_ids * capacity + position
    placement_mask = target_slot[None, :] == jnp.arange(slot_count, dtype=jnp.int32)[:, None]
    placement = placement_mask.astype(jnp.bfloat16)
    row_width = 2 * leaf_cells + port_count
    rows_out = jnp.concatenate(
        [filament_coupling.reshape(filament_count, 2 * leaf_cells), filament_current], 1
    )
    sent = jnp.dot(placement, rows_out, preferred_element_type=jnp.float32).astype(jnp.bfloat16)
    sent_leaf = jnp.dot(
        placement, (local_ids + 1).astype(jnp.bfloat16), preferred_element_type=jnp.float32
    ) - 1.0
    leaf_row_block = jnp.pad(
        sent_leaf.astype(jnp.bfloat16).reshape(owners, 1, capacity),
        ((0, 0), (0, 0), (0, row_width - capacity)),
    )
    payload = jnp.concatenate([sent.reshape(owners, capacity, row_width), leaf_row_block], 1)
    got = lax.all_to_all(payload, AXES, split_axis=0, concat_axis=0, tiled=True)
    got_rows = got[:, :capacity].reshape(slot_count, row_width)
    got_leaf = got[:, capacity, :capacity].reshape(slot_count).astype(jnp.int32)
    got_coupling_t = got_rows[:, : 2 * leaf_cells].T
    got_current = got_rows[:, 2 * leaf_cells :]
    got_leaf = got_leaf.reshape(1, slot_count)
    filament = filament_field(got_leaf, got_coupling_t, got_current, leaf_count)

    window, (got_leaf, got_coupling_t, filament) = stream_window(
        stream.transpose(1, 2, 0), half_cols, (got_leaf, got_coupling_t, filament)
    )
    currents = plane_curl(window).astype(jnp.bfloat16)
    bordered = to_leaves(currents)
    src_row = jnp.arange(leaf_rows, dtype=jnp.int32)[:, None, None] + near_lists // 3
    src_col = jnp.arange(leaf_cols, dtype=jnp.int32)[None, :, None] + near_lists % 3
    row_ok = ((src_row > 0) | (gx > 0)) & ((src_row < leaf_rows + 1) | (gx < nx - 1))
    col_ok = ((src_col > 0) | (col_index > 0)) & (
        (src_col < leaf_cols + 1) | (col_index < ny * nz - 1)
    )
    scales = (row_ok & col_ok).astype(jnp.int32).reshape(leaf_count, near_count)

    kernels = inductance.reshape(leaf_count, near_count, 2, leaf_cells, leaf_cells)
    codes = near_lists.reshape(leaf_count, near_count)
    total_field, induced = leaf_fields(
        codes, scales, bordered, kernels, filament, got_leaf, got_coupling_t
    )
    returned = lax.all_to_all(
        induced.reshape(owners, capacity, port_count), AXES, split_axis=0, concat_axis=0, tiled=True
    ).reshape(slot_count, port_count)
    filament_voltage = lax.dot_general(
        placement, returned, (((0,), (0,)), ((), ())), preferred_element_type=jnp.float32
    ).astype(jnp.bfloat16)

    loop_voltage = field_halo(total_field).transpose(2, 0, 1)
    return (loop_voltage, filament_voltage)


def solution(mesh):
    return jax.shard_map(
        body,
        mesh=mesh,
        in_specs=(
            P("groups", "gx", "gy"),
            P(("groups", "gx"), ("gy", "gz"), None, None, None, None),
            P(("groups", "gx"), ("gy", "gz"), None),
            P(("groups", "gx", "gy", "gz")),
            P(("groups", "gx", "gy", "gz"), None),
            P(("groups", "gx", "gy", "gz"), None, None),
        ),
        out_specs=(P("groups", "gx", ("gy", "gz")), P(("groups", "gx", "gy", "gz"), None)),
        check_vma=False,
    )
```

```python
import jax
import jax.numpy as jnp
from jax import lax
from jax.experimental import pallas as pl
from jax.experimental.pallas import tpu as pltpu
from jax.sharding import PartitionSpec as P

LEAF_R = 8
LEAF_C = 16
AXES = ("gx", "gy", "gz")


def plane_curl(padded):
    along_y = padded[1:-1, 2:] - padded[1:-1, :-2]
    along_x = padded[:-2, 1:-1] - padded[2:, 1:-1]
    return jnp.stack([along_y, along_x])


def to_leaves(grid_values):
    components, row_count, col_count, port_count = grid_values.shape
    blocks = grid_values.reshape(
        components, row_count // LEAF_R, LEAF_R, col_count // LEAF_C, LEAF_C, port_count
    )
    blocks = blocks.transpose(1, 3, 0, 2, 4, 5)
    return blocks.reshape(
        row_count // LEAF_R, col_count // LEAF_C, components, LEAF_R * LEAF_C, port_count
    )


def from_leaves(leaves):
    leaf_rows, leaf_cols, components, leaf_cells, port_count = leaves.shape
    blocks = leaves.reshape(leaf_rows, leaf_cols, components, LEAF_R, LEAF_C, port_count)
    blocks = blocks.transpose(2, 0, 3, 1, 4, 5)
    return blocks.reshape(components, leaf_rows * LEAF_R, leaf_cols * LEAF_C, port_count)


def device_grid():
    nx, ny, nz = (lax.axis_size(a) for a in AXES)
    return nx, ny, nz


def pairs_by(fn):
    nx, ny, nz = device_grid()
    out = []
    for x in range(nx):
        for y in range(ny):
            for z in range(nz):
                target = fn(x, y, z)
                if target is None:
                    continue
                tx, ty, tz = target
                if 0 <= tx < nx and 0 <= ty < ny and 0 <= tz < nz:
                    out.append(((x * ny + y) * nz + z, (tx * ny + ty) * nz + tz))
    return out


def send(value, fn):
    return lax.ppermute(value, AXES, pairs_by(fn))


def sideways(x, y, z, dx):
    nz = lax.axis_size("gz")
    if z == nz - 1:
        return (x + dx, y + 1, 0)
    if z == 0:
        return (x + dx, y - 1, nz - 1)
    return None


def stream_window(stream, half, ready):
    gz = lax.axis_index("gz")
    rows, width = stream.shape[0], stream.shape[1]
    hr, hc = LEAF_R + 1, LEAF_C + 1
    mid_w = half + hc
    mid = lax.dynamic_slice_in_dim(stream, gz * (width - mid_w), mid_w, 1)
    side = lax.dynamic_slice_in_dim(stream, gz * (width - hc), hc, 1)
    h_got = send(side, lambda x, y, z: sideways(x, y, z, 0))
    wide = lax.dynamic_slice_in_dim(
        jnp.concatenate([h_got, mid, h_got], 1), gz * hc, mid_w + hc, 1
    )
    v_top = send(wide[rows - hr :], lambda x, y, z: (x + 1, y, z))
    v_bot = send(wide[:hr], lambda x, y, z: (x - 1, y, z))
    (v_top, v_bot), ready = lax.optimization_barrier(((v_top, v_bot), ready))
    return jnp.concatenate([v_top, wide, v_bot], 0), ready


def field_halo(grid_field):
    x_field = grid_field[0]
    y_field = grid_field[1]
    rows = y_field.shape[0]
    cols = x_field.shape[1]

    def step(x, y, z, dc):
        nz = lax.axis_size("gz")
        c = y * nz + z + dc
        return (x, c // nz, c % nz) if c >= 0 else None

    x_left = send(x_field[:, cols - 1 :], lambda x, y, z: step(x, y, z, 1))
    x_right = send(x_field[:, :1], lambda x, y, z: step(x, y, z, -1))
    y_top = send(y_field[rows - 1 :], lambda x, y, z: (x + 1, y, z))
    y_bot = send(y_field[:1], lambda x, y, z: (x - 1, y, z))
    x_pad = jnp.concatenate([x_left, x_field, x_right], 1).astype(jnp.float32)
    y_pad = jnp.concatenate([y_top, y_field, y_bot], 0).astype(jnp.float32)
    return x_pad[:, :-2] - x_pad[:, 2:] + (y_pad[2:] - y_pad[:-2])


def filament_kernel(row_leaf_ref, cpl_t_ref, cur_ref, fil_ref, stack_ref):
    coupling_t = cpl_t_ref[...]
    slot_leaf = row_leaf_ref[...]
    for leaf in range(fil_ref.shape[0]):
        stack_ref[leaf] = jnp.where(slot_leaf == leaf, coupling_t, jnp.zeros_like(coupling_t))
    stacked = stack_ref[...].reshape(-1, coupling_t.shape[1])
    fil_ref[...] = jnp.dot(stacked, cur_ref[...], preferred_element_type=jnp.float32).reshape(
        fil_ref.shape
    )


def filament_field(row_leaf, coupling_t, current, leaf_count):
    vmem = pl.BlockSpec(memory_space=pltpu.VMEM)
    return pl.pallas_call(
        filament_kernel,
        in_specs=[vmem, vmem, vmem],
        out_specs=vmem,
        out_shape=jax.ShapeDtypeStruct(
            (leaf_count, coupling_t.shape[0], current.shape[1]), jnp.float32
        ),
        scratch_shapes=[pltpu.VMEM((leaf_count,) + coupling_t.shape, coupling_t.dtype)],
    )(row_leaf, coupling_t, current)


def leaf_kernel(
    codes_ref, scale_ref, bord_hbm, ind_hbm, fil_hbm,
    field_ref, bord_ref, ind_ref, fil_ref, sems, fil_sems, ind_sems,
):
    leaf_count = ind_ref.shape[0]
    leaf_cols = bord_ref.shape[1] - 2
    near_count = ind_ref.shape[1]
    cells = ind_ref.shape[3]
    ring_rows = bord_ref.shape[0]

    def row_copy(r):
        return pltpu.make_async_copy(bord_hbm.at[r], bord_ref.at[r], sems.at[r])

    def fil_copy(l):
        return pltpu.make_async_copy(fil_hbm.at[l], fil_ref.at[l], fil_sems.at[l])

    for r in range(ring_rows):
        row_copy(r).start()
    for l in range(leaf_count):
        fil_copy(l).start()
        pltpu.make_async_copy(ind_hbm.at[l], ind_ref.at[l], ind_sems.at[l]).start()
    for r in range(3):
        row_copy(r).wait()

    def one_leaf(leaf, carry):
        row = leaf // leaf_cols
        col = leaf % leaf_cols

        @pl.when((col == 0) & (row > 0))
        def _():
            row_copy(row + 2).wait()

        fil_copy(leaf).wait()
        pltpu.make_async_copy(ind_hbm.at[leaf], ind_ref.at[leaf], ind_sems.at[leaf]).wait()
        filament = fil_ref[leaf]
        sources = []
        for n in range(near_count):
            code = codes_ref[leaf, n]
            src_row = jnp.minimum(jnp.maximum(row + code // 3, 0), bord_ref.shape[0] - 1)
            src_col = jnp.minimum(jnp.maximum(col + code % 3, 0), bord_ref.shape[1] - 1)
            keep = scale_ref[leaf, n] > 0
            tile = bord_ref[src_row, src_col]
            sources.append(jnp.where(keep, tile, jnp.zeros_like(tile)))
        for c in range(2):
            weights = jnp.concatenate([ind_ref[leaf, n, c] for n in range(near_count)], axis=1)
            stacked = jnp.concatenate([s[c] for s in sources], axis=0)
            total = filament[c * cells : (c + 1) * cells] + jnp.dot(
                weights, stacked, preferred_element_type=jnp.float32
            )
            field_ref[c, pl.ds(row * LEAF_R, LEAF_R), pl.ds(pl.multiple_of(col * LEAF_C, LEAF_C), LEAF_C)] = (
                total.reshape(LEAF_R, LEAF_C, -1).astype(field_ref.dtype)
            )
        return carry

    lax.fori_loop(0, leaf_count, one_leaf, 0)


def induced_kernel(bord_hbm, row_leaf_ref, cpl_t_ref, volt_ref, own_ref, stack_ref, sems):
    leaf_rows = own_ref.shape[0]
    leaf_cols = own_ref.shape[1] - 2
    copies = [
        pltpu.make_async_copy(bord_hbm.at[r + 1], own_ref.at[r], sems.at[r]) for r in range(leaf_rows)
    ]
    for copy in copies:
        copy.start()
    coupling_t = cpl_t_ref[...]
    slot_leaf = row_leaf_ref[...]
    for leaf in range(leaf_rows * leaf_cols):
        stack_ref[leaf] = jnp.where(slot_leaf == leaf, coupling_t, jnp.zeros_like(coupling_t))
    for copy in copies:
        copy.wait()
    own = own_ref[:, 1 : leaf_cols + 1].reshape(-1, own_ref.shape[-1])
    stacked = stack_ref[...].reshape(own.shape[0], -1)
    volt = lax.dot_general(
        own, stacked, (((0,), (0,)), ((), ())), preferred_element_type=jnp.float32
    )
    volt_ref[...] = volt.T.astype(volt_ref.dtype)


def leaf_fields(codes, scales, bordered, kernels, filament, row_leaf, coupling_t):
    leaf_count, near_count, components, cells, _ = kernels.shape
    leaf_rows = bordered.shape[0] - 2
    leaf_cols = bordered.shape[1] - 2
    port_count = bordered.shape[-1]
    slot_count = coupling_t.shape[1]
    smem = pl.BlockSpec(memory_space=pltpu.SMEM)
    hbm = pl.BlockSpec(memory_space=pl.ANY)
    vmem = pl.BlockSpec(memory_space=pltpu.VMEM)
    field = pl.pallas_call(
        leaf_kernel,
        in_specs=[smem, smem, hbm, hbm, hbm],
        out_specs=vmem,
        out_shape=jax.ShapeDtypeStruct(
            (components, leaf_rows * LEAF_R, leaf_cols * LEAF_C, port_count), jnp.bfloat16
        ),
        scratch_shapes=[
            pltpu.VMEM(bordered.shape, bordered.dtype),
            pltpu.VMEM(kernels.shape, kernels.dtype),
            pltpu.VMEM(filament.shape, filament.dtype),
            pltpu.SemaphoreType.DMA((leaf_rows + 2,)),
            pltpu.SemaphoreType.DMA((leaf_count,)),
            pltpu.SemaphoreType.DMA((leaf_count,)),
        ],
    )(codes, scales, bordered, kernels, filament)
    field, bordered = lax.optimization_barrier((field, bordered))
    volt = pl.pallas_call(
        induced_kernel,
        in_specs=[hbm, vmem, vmem],
        out_specs=vmem,
        out_shape=jax.ShapeDtypeStruct((slot_count, port_count), jnp.bfloat16),
        scratch_shapes=[
            pltpu.VMEM((leaf_rows,) + bordered.shape[1:], bordered.dtype),
            pltpu.VMEM((leaf_count,) + coupling_t.shape, coupling_t.dtype),
            pltpu.SemaphoreType.DMA((leaf_rows,)),
        ],
    )(bordered, row_leaf, coupling_t)
    return field, volt


def body(stream, inductance, near_lists, filament_leaf, filament_current, filament_coupling):
    port_count = stream.shape[0]
    leaf_rows = inductance.shape[0]
    leaf_cols = inductance.shape[1]
    near_count = inductance.shape[2]
    leaf_cells = inductance.shape[4]
    leaf_count = leaf_rows * leaf_cols
    half_cols = leaf_cols * LEAF_C
    nx, ny, nz = device_grid()
    gx = lax.axis_index("gx")
    col_index = lax.axis_index("gy") * nz + lax.axis_index("gz")
    owners = nx * ny * nz

    filament_count = filament_leaf.shape[0]
    capacity = max(2, 2 * filament_count // owners)
    slot_count = owners * capacity
    plane_cols = leaf_cols * ny * nz
    leaf_row = filament_leaf // plane_cols
    leaf_col = filament_leaf % plane_cols
    owner_ids = leaf_row // leaf_rows * (ny * nz) + leaf_col // leaf_cols
    local_ids = leaf_row % leaf_rows * leaf_cols + leaf_col % leaf_cols
    index = jnp.arange(filament_count, dtype=jnp.int32)
    earlier = (owner_ids[None, :] == owner_ids[:, None]) & (index[None, :] < index[:, None])
    position = jnp.sum(earlier.astype(jnp.int32), axis=1)
    target_slot = owner_ids * capacity + position
    placement_mask = target_slot[None, :] == jnp.arange(slot_count, dtype=jnp.int32)[:, None]
    placement = placement_mask.astype(jnp.bfloat16)
    row_width = 2 * leaf_cells + port_count
    rows_out = jnp.concatenate(
        [filament_coupling.reshape(filament_count, 2 * leaf_cells), filament_current], 1
    )
    sent = jnp.dot(placement, rows_out, preferred_element_type=jnp.float32).astype(jnp.bfloat16)
    sent_leaf = jnp.dot(
        placement, (local_ids + 1).astype(jnp.bfloat16), preferred_element_type=jnp.float32
    ) - 1.0
    leaf_row_block = jnp.pad(
        sent_leaf.astype(jnp.bfloat16).reshape(owners, 1, capacity),
        ((0, 0), (0, 0), (0, row_width - capacity)),
    )
    payload = jnp.concatenate([sent.reshape(owners, capacity, row_width), leaf_row_block], 1)
    got = lax.all_to_all(payload, AXES, split_axis=0, concat_axis=0, tiled=True)
    got_rows = got[:, :capacity].reshape(slot_count, row_width)
    got_leaf = got[:, capacity, :capacity].reshape(slot_count).astype(jnp.int32)
    got_coupling_t = got_rows[:, : 2 * leaf_cells].T
    got_current = got_rows[:, 2 * leaf_cells :]
    got_leaf = got_leaf.reshape(1, slot_count)
    filament = filament_field(got_leaf, got_coupling_t, got_current, leaf_count)

    window, (got_leaf, got_coupling_t, filament) = stream_window(
        stream.transpose(1, 2, 0), half_cols, (got_leaf, got_coupling_t, filament)
    )
    currents = plane_curl(window).astype(jnp.bfloat16)
    bordered = to_leaves(currents)
    src_row = jnp.arange(leaf_rows, dtype=jnp.int32)[:, None, None] + near_lists // 3
    src_col = jnp.arange(leaf_cols, dtype=jnp.int32)[None, :, None] + near_lists % 3
    row_ok = ((src_row > 0) | (gx > 0)) & ((src_row < leaf_rows + 1) | (gx < nx - 1))
    col_ok = ((src_col > 0) | (col_index > 0)) & (
        (src_col < leaf_cols + 1) | (col_index < ny * nz - 1)
    )
    scales = (row_ok & col_ok).astype(jnp.int32).reshape(leaf_count, near_count)

    kernels = inductance.reshape(leaf_count, near_count, 2, leaf_cells, leaf_cells)
    codes = near_lists.reshape(leaf_count, near_count)
    total_field, induced = leaf_fields(
        codes, scales, bordered, kernels, filament, got_leaf, got_coupling_t
    )
    returned = lax.all_to_all(
        induced.reshape(owners, capacity, port_count), AXES, split_axis=0, concat_axis=0, tiled=True
    ).reshape(slot_count, port_count)
    filament_voltage = lax.dot_general(
        placement, returned, (((0,), (0,)), ((), ())), preferred_element_type=jnp.float32
    ).astype(jnp.bfloat16)

    loop_voltage = field_halo(total_field).transpose(2, 0, 1)
    return (loop_voltage, filament_voltage)


def solution(mesh):
    return jax.shard_map(
        body,
        mesh=mesh,
        in_specs=(
            P("groups", "gx", "gy"),
            P(("groups", "gx"), ("gy", "gz"), None, None, None, None),
            P(("groups", "gx"), ("gy", "gz"), None),
            P(("groups", "gx", "gy", "gz")),
            P(("groups", "gx", "gy", "gz"), None),
            P(("groups", "gx", "gy", "gz"), None, None),
        ),
        out_specs=(P("groups", "gx", ("gy", "gz")), P(("groups", "gx", "gy", "gz"), None)),
        check_vma=False,
    )
```

```python
import jax
import jax.numpy as jnp
from jax import lax
from jax.experimental import pallas as pl
from jax.experimental.pallas import tpu as pltpu
from jax.sharding import PartitionSpec as P

LEAF_R = 8
LEAF_C = 16
AXES = ("gx", "gy", "gz")


def plane_curl(padded):
    along_y = padded[1:-1, 2:] - padded[1:-1, :-2]
    along_x = padded[:-2, 1:-1] - padded[2:, 1:-1]
    return jnp.stack([along_y, along_x])


def to_leaves(grid_values):
    components, row_count, col_count, port_count = grid_values.shape
    blocks = grid_values.reshape(
        components, row_count // LEAF_R, LEAF_R, col_count // LEAF_C, LEAF_C, port_count
    )
    blocks = blocks.transpose(1, 3, 0, 2, 4, 5)
    return blocks.reshape(
        row_count // LEAF_R, col_count // LEAF_C, components, LEAF_R * LEAF_C, port_count
    )


def from_leaves(leaves):
    leaf_rows, leaf_cols, components, leaf_cells, port_count = leaves.shape
    blocks = leaves.reshape(leaf_rows, leaf_cols, components, LEAF_R, LEAF_C, port_count)
    blocks = blocks.transpose(2, 0, 3, 1, 4, 5)
    return blocks.reshape(components, leaf_rows * LEAF_R, leaf_cols * LEAF_C, port_count)


def device_grid():
    nx, ny, nz = (lax.axis_size(a) for a in AXES)
    return nx, ny, nz


def pairs_by(fn):
    nx, ny, nz = device_grid()
    out = []
    for x in range(nx):
        for y in range(ny):
            for z in range(nz):
                target = fn(x, y, z)
                if target is None:
                    continue
                tx, ty, tz = target
                if 0 <= tx < nx and 0 <= ty < ny and 0 <= tz < nz:
                    out.append(((x * ny + y) * nz + z, (tx * ny + ty) * nz + tz))
    return out


def send(value, fn):
    return lax.ppermute(value, AXES, pairs_by(fn))


def sideways(x, y, z, dx):
    nz = lax.axis_size("gz")
    if z == nz - 1:
        return (x + dx, y + 1, 0)
    if z == 0:
        return (x + dx, y - 1, nz - 1)
    return None


def stream_window(stream, half, ready):
    gz = lax.axis_index("gz")
    rows, width = stream.shape[0], stream.shape[1]
    hr, hc = LEAF_R + 1, LEAF_C + 1
    mid_w = half + hc
    mid = lax.dynamic_slice_in_dim(stream, gz * (width - mid_w), mid_w, 1)
    side = lax.dynamic_slice_in_dim(stream, gz * (width - hc), hc, 1)
    h_got = send(side, lambda x, y, z: sideways(x, y, z, 0))
    wide = lax.dynamic_slice_in_dim(
        jnp.concatenate([h_got, mid, h_got], 1), gz * hc, mid_w + hc, 1
    )
    v_top = send(wide[rows - hr :], lambda x, y, z: (x + 1, y, z))
    v_bot = send(wide[:hr], lambda x, y, z: (x - 1, y, z))
    (v_top, v_bot), ready = lax.optimization_barrier(((v_top, v_bot), ready))
    return jnp.concatenate([v_top, wide, v_bot], 0), ready


def field_halo(grid_field):
    x_field = grid_field[0]
    y_field = grid_field[1]
    rows = y_field.shape[0]
    cols = x_field.shape[1]

    def step(x, y, z, dc):
        nz = lax.axis_size("gz")
        c = y * nz + z + dc
        return (x, c // nz, c % nz) if c >= 0 else None

    x_left = send(x_field[:, cols - 1 :], lambda x, y, z: step(x, y, z, 1))
    x_right = send(x_field[:, :1], lambda x, y, z: step(x, y, z, -1))
    y_top = send(y_field[rows - 1 :], lambda x, y, z: (x + 1, y, z))
    y_bot = send(y_field[:1], lambda x, y, z: (x - 1, y, z))
    x_pad = jnp.concatenate([x_left, x_field, x_right], 1).astype(jnp.float32)
    y_pad = jnp.concatenate([y_top, y_field, y_bot], 0).astype(jnp.float32)
    return x_pad[:, :-2] - x_pad[:, 2:] + (y_pad[2:] - y_pad[:-2])


def filament_kernel(row_leaf_ref, cpl_t_ref, cur_ref, fil_ref):
    def one_leaf(leaf, carry):
        coupling_t = cpl_t_ref[...]
        coupling_t = jnp.where(row_leaf_ref[...] == leaf, coupling_t, jnp.zeros_like(coupling_t))
        fil_ref[leaf] = jnp.dot(coupling_t, cur_ref[...], preferred_element_type=jnp.float32)
        return carry

    lax.fori_loop(0, fil_ref.shape[0], one_leaf, 0)


def filament_field(row_leaf, coupling_t, current, leaf_count):
    vmem = pl.BlockSpec(memory_space=pltpu.VMEM)
    return pl.pallas_call(
        filament_kernel,
        in_specs=[vmem, vmem, vmem],
        out_specs=vmem,
        out_shape=jax.ShapeDtypeStruct(
            (leaf_count, coupling_t.shape[0], current.shape[1]), jnp.float32
        ),
    )(row_leaf, coupling_t, current)


def leaf_kernel(
    codes_ref, scale_ref, bord_hbm, ind_hbm, fil_hbm,
    field_ref, bord_ref, ind_ref, fil_ref, sems, fil_sems, ind_sems,
):
    leaf_count = ind_ref.shape[0]
    leaf_cols = bord_ref.shape[1] - 2
    near_count = ind_ref.shape[1]
    cells = ind_ref.shape[3]
    ring_rows = bord_ref.shape[0]

    def row_copy(r):
        return pltpu.make_async_copy(bord_hbm.at[r], bord_ref.at[r], sems.at[r])

    def fil_copy(l):
        return pltpu.make_async_copy(fil_hbm.at[l], fil_ref.at[l], fil_sems.at[l])

    for r in range(ring_rows):
        row_copy(r).start()
    for l in range(leaf_count):
        fil_copy(l).start()
        pltpu.make_async_copy(ind_hbm.at[l], ind_ref.at[l], ind_sems.at[l]).start()
    for r in range(3):
        row_copy(r).wait()

    def one_leaf(leaf, carry):
        row = leaf // leaf_cols
        col = leaf % leaf_cols

        @pl.when((col == 0) & (row > 0))
        def _():
            row_copy(row + 2).wait()

        fil_copy(leaf).wait()
        pltpu.make_async_copy(ind_hbm.at[leaf], ind_ref.at[leaf], ind_sems.at[leaf]).wait()
        filament = fil_ref[leaf]
        sources = []
        for n in range(near_count):
            code = codes_ref[leaf, n]
            src_row = jnp.minimum(jnp.maximum(row + code // 3, 0), bord_ref.shape[0] - 1)
            src_col = jnp.minimum(jnp.maximum(col + code % 3, 0), bord_ref.shape[1] - 1)
            keep = scale_ref[leaf, n] > 0
            tile = bord_ref[src_row, src_col]
            sources.append(jnp.where(keep, tile, jnp.zeros_like(tile)))
        for c in range(2):
            weights = jnp.concatenate([ind_ref[leaf, n, c] for n in range(near_count)], axis=1)
            stacked = jnp.concatenate([s[c] for s in sources], axis=0)
            total = filament[c * cells : (c + 1) * cells] + jnp.dot(
                weights, stacked, preferred_element_type=jnp.float32
            )
            field_ref[c, pl.ds(row * LEAF_R, LEAF_R), pl.ds(pl.multiple_of(col * LEAF_C, LEAF_C), LEAF_C)] = (
                total.reshape(LEAF_R, LEAF_C, -1).astype(field_ref.dtype)
            )
        return carry

    lax.fori_loop(0, leaf_count, one_leaf, 0, unroll=2)


def induced_kernel(bord_hbm, row_leaf_ref, cpl_t_ref, volt_ref, own_ref, stack_ref, sems):
    leaf_rows = own_ref.shape[0]
    leaf_cols = own_ref.shape[1] - 2
    copies = [
        pltpu.make_async_copy(bord_hbm.at[r + 1], own_ref.at[r], sems.at[r]) for r in range(leaf_rows)
    ]
    for copy in copies:
        copy.start()
    coupling_t = cpl_t_ref[...]
    slot_leaf = row_leaf_ref[...]
    for leaf in range(leaf_rows * leaf_cols):
        stack_ref[leaf] = jnp.where(slot_leaf == leaf, coupling_t, jnp.zeros_like(coupling_t))
    for copy in copies:
        copy.wait()
    own = own_ref[:, 1 : leaf_cols + 1].reshape(-1, own_ref.shape[-1])
    stacked = stack_ref[...].reshape(own.shape[0], -1)
    volt = lax.dot_general(
        own, stacked, (((0,), (0,)), ((), ())), preferred_element_type=jnp.float32
    )
    volt_ref[...] = volt.T.astype(volt_ref.dtype)


def leaf_fields(codes, scales, bordered, kernels, filament, row_leaf, coupling_t):
    leaf_count, near_count, components, cells, _ = kernels.shape
    leaf_rows = bordered.shape[0] - 2
    leaf_cols = bordered.shape[1] - 2
    port_count = bordered.shape[-1]
    slot_count = coupling_t.shape[1]
    smem = pl.BlockSpec(memory_space=pltpu.SMEM)
    hbm = pl.BlockSpec(memory_space=pl.ANY)
    vmem = pl.BlockSpec(memory_space=pltpu.VMEM)
    field = pl.pallas_call(
        leaf_kernel,
        in_specs=[smem, smem, hbm, hbm, hbm],
        out_specs=vmem,
        out_shape=jax.ShapeDtypeStruct(
            (components, leaf_rows * LEAF_R, leaf_cols * LEAF_C, port_count), jnp.bfloat16
        ),
        scratch_shapes=[
            pltpu.VMEM(bordered.shape, bordered.dtype),
            pltpu.VMEM(kernels.shape, kernels.dtype),
            pltpu.VMEM(filament.shape, filament.dtype),
            pltpu.SemaphoreType.DMA((leaf_rows + 2,)),
            pltpu.SemaphoreType.DMA((leaf_count,)),
            pltpu.SemaphoreType.DMA((leaf_count,)),
        ],
    )(codes, scales, bordered, kernels, filament)
    field, bordered = lax.optimization_barrier((field, bordered))
    volt = pl.pallas_call(
        induced_kernel,
        in_specs=[hbm, vmem, vmem],
        out_specs=vmem,
        out_shape=jax.ShapeDtypeStruct((slot_count, port_count), jnp.bfloat16),
        scratch_shapes=[
            pltpu.VMEM((leaf_rows,) + bordered.shape[1:], bordered.dtype),
            pltpu.VMEM((leaf_count,) + coupling_t.shape, coupling_t.dtype),
            pltpu.SemaphoreType.DMA((leaf_rows,)),
        ],
    )(bordered, row_leaf, coupling_t)
    return field, volt


def body(stream, inductance, near_lists, filament_leaf, filament_current, filament_coupling):
    port_count = stream.shape[0]
    leaf_rows = inductance.shape[0]
    leaf_cols = inductance.shape[1]
    near_count = inductance.shape[2]
    leaf_cells = inductance.shape[4]
    leaf_count = leaf_rows * leaf_cols
    half_cols = leaf_cols * LEAF_C
    nx, ny, nz = device_grid()
    gx = lax.axis_index("gx")
    col_index = lax.axis_index("gy") * nz + lax.axis_index("gz")
    owners = nx * ny * nz

    filament_count = filament_leaf.shape[0]
    capacity = max(2, 2 * filament_count // owners)
    slot_count = owners * capacity
    plane_cols = leaf_cols * ny * nz
    leaf_row = filament_leaf // plane_cols
    leaf_col = filament_leaf % plane_cols
    owner_ids = leaf_row // leaf_rows * (ny * nz) + leaf_col // leaf_cols
    local_ids = leaf_row % leaf_rows * leaf_cols + leaf_col % leaf_cols
    index = jnp.arange(filament_count, dtype=jnp.int32)
    earlier = (owner_ids[None, :] == owner_ids[:, None]) & (index[None, :] < index[:, None])
    position = jnp.sum(earlier.astype(jnp.int32), axis=1)
    target_slot = owner_ids * capacity + position
    placement_mask = target_slot[None, :] == jnp.arange(slot_count, dtype=jnp.int32)[:, None]
    placement = placement_mask.astype(jnp.bfloat16)
    row_width = 2 * leaf_cells + port_count
    rows_out = jnp.concatenate(
        [filament_coupling.reshape(filament_count, 2 * leaf_cells), filament_current], 1
    )
    sent = jnp.dot(placement, rows_out, preferred_element_type=jnp.float32).astype(jnp.bfloat16)
    sent_leaf = jnp.dot(
        placement, (local_ids + 1).astype(jnp.bfloat16), preferred_element_type=jnp.float32
    ) - 1.0
    leaf_row_block = jnp.pad(
        sent_leaf.astype(jnp.bfloat16).reshape(owners, 1, capacity),
        ((0, 0), (0, 0), (0, row_width - capacity)),
    )
    payload = jnp.concatenate([sent.reshape(owners, capacity, row_width), leaf_row_block], 1)
    got = lax.all_to_all(payload, AXES, split_axis=0, concat_axis=0, tiled=True)
    got_rows = got[:, :capacity].reshape(slot_count, row_width)
    got_leaf = got[:, capacity, :capacity].reshape(slot_count).astype(jnp.int32)
    got_coupling_t = got_rows[:, : 2 * leaf_cells].T
    got_current = got_rows[:, 2 * leaf_cells :]
    got_leaf = got_leaf.reshape(1, slot_count)
    filament = filament_field(got_leaf, got_coupling_t, got_current, leaf_count)

    window, (got_leaf, got_coupling_t, filament) = stream_window(
        stream.transpose(1, 2, 0), half_cols, (got_leaf, got_coupling_t, filament)
    )
    currents = plane_curl(window).astype(jnp.bfloat16)
    bordered = to_leaves(currents)
    src_row = jnp.arange(leaf_rows, dtype=jnp.int32)[:, None, None] + near_lists // 3
    src_col = jnp.arange(leaf_cols, dtype=jnp.int32)[None, :, None] + near_lists % 3
    row_ok = ((src_row > 0) | (gx > 0)) & ((src_row < leaf_rows + 1) | (gx < nx - 1))
    col_ok = ((src_col > 0) | (col_index > 0)) & (
        (src_col < leaf_cols + 1) | (col_index < ny * nz - 1)
    )
    scales = (row_ok & col_ok).astype(jnp.int32).reshape(leaf_count, near_count)

    kernels = inductance.reshape(leaf_count, near_count, 2, leaf_cells, leaf_cells)
    codes = near_lists.reshape(leaf_count, near_count)
    total_field, induced = leaf_fields(
        codes, scales, bordered, kernels, filament, got_leaf, got_coupling_t
    )
    returned = lax.all_to_all(
        induced.reshape(owners, capacity, port_count), AXES, split_axis=0, concat_axis=0, tiled=True
    ).reshape(slot_count, port_count)
    filament_voltage = lax.dot_general(
        placement, returned, (((0,), (0,)), ((), ())), preferred_element_type=jnp.float32
    ).astype(jnp.bfloat16)

    loop_voltage = field_halo(total_field).transpose(2, 0, 1)
    return (loop_voltage, filament_voltage)


def solution(mesh):
    return jax.shard_map(
        body,
        mesh=mesh,
        in_specs=(
            P("groups", "gx", "gy"),
            P(("groups", "gx"), ("gy", "gz"), None, None, None, None),
            P(("groups", "gx"), ("gy", "gz"), None),
            P(("groups", "gx", "gy", "gz")),
            P(("groups", "gx", "gy", "gz"), None),
            P(("groups", "gx", "gy", "gz"), None, None),
        ),
        out_specs=(P("groups", "gx", ("gy", "gz")), P(("groups", "gx", "gy", "gz"), None)),
        check_vma=False,
    )
```

```python
import jax
import jax.numpy as jnp
from jax import lax
from jax.experimental import pallas as pl
from jax.experimental.pallas import tpu as pltpu
from jax.sharding import PartitionSpec as P

LEAF_R = 8
LEAF_C = 16
AXES = ("gx", "gy", "gz")


def plane_curl(padded):
    along_y = padded[1:-1, 2:] - padded[1:-1, :-2]
    along_x = padded[:-2, 1:-1] - padded[2:, 1:-1]
    return jnp.stack([along_y, along_x])


def to_leaves(grid_values):
    components, row_count, col_count, port_count = grid_values.shape
    blocks = grid_values.reshape(
        components, row_count // LEAF_R, LEAF_R, col_count // LEAF_C, LEAF_C, port_count
    )
    blocks = blocks.transpose(1, 3, 0, 2, 4, 5)
    return blocks.reshape(
        row_count // LEAF_R, col_count // LEAF_C, components, LEAF_R * LEAF_C, port_count
    )


def from_leaves(leaves):
    leaf_rows, leaf_cols, components, leaf_cells, port_count = leaves.shape
    blocks = leaves.reshape(leaf_rows, leaf_cols, components, LEAF_R, LEAF_C, port_count)
    blocks = blocks.transpose(2, 0, 3, 1, 4, 5)
    return blocks.reshape(components, leaf_rows * LEAF_R, leaf_cols * LEAF_C, port_count)


def device_grid():
    nx, ny, nz = (lax.axis_size(a) for a in AXES)
    return nx, ny, nz


def pairs_by(fn):
    nx, ny, nz = device_grid()
    out = []
    for x in range(nx):
        for y in range(ny):
            for z in range(nz):
                target = fn(x, y, z)
                if target is None:
                    continue
                tx, ty, tz = target
                if 0 <= tx < nx and 0 <= ty < ny and 0 <= tz < nz:
                    out.append(((x * ny + y) * nz + z, (tx * ny + ty) * nz + tz))
    return out


def send(value, fn):
    return lax.ppermute(value, AXES, pairs_by(fn))


def sideways(x, y, z, dx):
    nz = lax.axis_size("gz")
    if z == nz - 1:
        return (x + dx, y + 1, 0)
    if z == 0:
        return (x + dx, y - 1, nz - 1)
    return None


def stream_window(stream, half, ready):
    gz = lax.axis_index("gz")
    rows, width = stream.shape[0], stream.shape[1]
    hr, hc = LEAF_R + 1, LEAF_C + 1
    mid_w = half + hc
    mid = lax.dynamic_slice_in_dim(stream, gz * (width - mid_w), mid_w, 1)
    side = lax.dynamic_slice_in_dim(stream, gz * (width - hc), hc, 1)
    h_got = send(side, lambda x, y, z: sideways(x, y, z, 0))
    wide = lax.dynamic_slice_in_dim(
        jnp.concatenate([h_got, mid, h_got], 1), gz * hc, mid_w + hc, 1
    )
    v_top = send(wide[rows - hr :], lambda x, y, z: (x + 1, y, z))
    v_bot = send(wide[:hr], lambda x, y, z: (x - 1, y, z))
    (v_top, v_bot), ready = lax.optimization_barrier(((v_top, v_bot), ready))
    return jnp.concatenate([v_top, wide, v_bot], 0), ready


def field_halo(grid_field, edges):
    x_field = grid_field[0]
    y_field = grid_field[1]
    x_first, x_last, y_first, y_last = edges

    def step(x, y, z, dc):
        nz = lax.axis_size("gz")
        c = y * nz + z + dc
        return (x, c // nz, c % nz) if c >= 0 else None

    x_left = send(x_last, lambda x, y, z: step(x, y, z, 1))
    x_right = send(x_first, lambda x, y, z: step(x, y, z, -1))
    y_top = send(y_last, lambda x, y, z: (x + 1, y, z))
    y_bot = send(y_first, lambda x, y, z: (x - 1, y, z))
    x_pad = jnp.concatenate([x_left, x_field, x_right], 1).astype(jnp.float32)
    y_pad = jnp.concatenate([y_top, y_field, y_bot], 0).astype(jnp.float32)
    return x_pad[:, :-2] - x_pad[:, 2:] + (y_pad[2:] - y_pad[:-2])


def filament_kernel(row_leaf_ref, cpl_t_ref, cur_ref, fil_ref):
    def one_leaf(leaf, carry):
        coupling_t = cpl_t_ref[...]
        coupling_t = jnp.where(row_leaf_ref[...] == leaf, coupling_t, jnp.zeros_like(coupling_t))
        fil_ref[leaf] = jnp.dot(coupling_t, cur_ref[...], preferred_element_type=jnp.float32)
        return carry

    lax.fori_loop(0, fil_ref.shape[0], one_leaf, 0)


def filament_field(row_leaf, coupling_t, current, leaf_count):
    vmem = pl.BlockSpec(memory_space=pltpu.VMEM)
    return pl.pallas_call(
        filament_kernel,
        in_specs=[vmem, vmem, vmem],
        out_specs=vmem,
        out_shape=jax.ShapeDtypeStruct(
            (leaf_count, coupling_t.shape[0], current.shape[1]), jnp.float32
        ),
    )(row_leaf, coupling_t, current)


def leaf_kernel(
    codes_ref, scale_ref, bord_hbm, ind_hbm, fil_hbm,
    field_ref, x_first_ref, x_last_ref, y_first_ref, y_last_ref,
    bord_ref, ind_ref, fil_ref, sems, fil_sems, ind_sems,
):
    leaf_count = ind_ref.shape[0]
    leaf_cols = bord_ref.shape[1] - 2
    near_count = ind_ref.shape[1]
    cells = ind_ref.shape[3]
    ring_rows = bord_ref.shape[0]

    def row_copy(r):
        return pltpu.make_async_copy(bord_hbm.at[r], bord_ref.at[r], sems.at[r])

    def fil_copy(l):
        return pltpu.make_async_copy(fil_hbm.at[l], fil_ref.at[l], fil_sems.at[l])

    for r in range(ring_rows):
        row_copy(r).start()
    for l in range(leaf_count):
        fil_copy(l).start()
        pltpu.make_async_copy(ind_hbm.at[l], ind_ref.at[l], ind_sems.at[l]).start()
    for r in range(3):
        row_copy(r).wait()

    def one_leaf(leaf, carry):
        row = leaf // leaf_cols
        col = leaf % leaf_cols

        @pl.when((col == 0) & (row > 0))
        def _():
            row_copy(row + 2).wait()

        fil_copy(leaf).wait()
        pltpu.make_async_copy(ind_hbm.at[leaf], ind_ref.at[leaf], ind_sems.at[leaf]).wait()
        filament = fil_ref[leaf]
        sources = []
        for n in range(near_count):
            code = codes_ref[leaf, n]
            src_row = jnp.minimum(jnp.maximum(row + code // 3, 0), bord_ref.shape[0] - 1)
            src_col = jnp.minimum(jnp.maximum(col + code % 3, 0), bord_ref.shape[1] - 1)
            keep = scale_ref[leaf, n] > 0
            tile = bord_ref[src_row, src_col]
            sources.append(jnp.where(keep, tile, jnp.zeros_like(tile)))
        for c in range(2):
            weights = jnp.concatenate([ind_ref[leaf, n, c] for n in range(near_count)], axis=1)
            stacked = jnp.concatenate([s[c] for s in sources], axis=0)
            total = filament[c * cells : (c + 1) * cells] + jnp.dot(
                weights, stacked, preferred_element_type=jnp.float32
            )
            field_ref[c, pl.ds(row * LEAF_R, LEAF_R), pl.ds(pl.multiple_of(col * LEAF_C, LEAF_C), LEAF_C)] = (
                total.reshape(LEAF_R, LEAF_C, -1).astype(field_ref.dtype)
            )
        return carry

    lax.fori_loop(0, leaf_count, one_leaf, 0, unroll=2)
    rows, cols = field_ref.shape[1], field_ref.shape[2]
    x_first_ref[...] = field_ref[0, :, 0:1]
    x_last_ref[...] = field_ref[0, :, cols - 1 : cols]
    y_first_ref[...] = field_ref[1, 0:1]
    y_last_ref[...] = field_ref[1, rows - 1 : rows]


def induced_kernel(bord_hbm, row_leaf_ref, cpl_t_ref, volt_ref, own_ref, stack_ref, sems):
    leaf_rows = own_ref.shape[0]
    leaf_cols = own_ref.shape[1] - 2
    copies = [
        pltpu.make_async_copy(bord_hbm.at[r + 1], own_ref.at[r], sems.at[r]) for r in range(leaf_rows)
    ]
    for copy in copies:
        copy.start()
    coupling_t = cpl_t_ref[...]
    slot_leaf = row_leaf_ref[...]
    for leaf in range(leaf_rows * leaf_cols):
        stack_ref[leaf] = jnp.where(slot_leaf == leaf, coupling_t, jnp.zeros_like(coupling_t))
    for copy in copies:
        copy.wait()
    own = own_ref[:, 1 : leaf_cols + 1].reshape(-1, own_ref.shape[-1])
    stacked = stack_ref[...].reshape(own.shape[0], -1)
    volt = lax.dot_general(
        own, stacked, (((0,), (0,)), ((), ())), preferred_element_type=jnp.float32
    )
    volt_ref[...] = volt.T.astype(volt_ref.dtype)


def leaf_fields(codes, scales, bordered, kernels, filament, row_leaf, coupling_t):
    leaf_count, near_count, components, cells, _ = kernels.shape
    leaf_rows = bordered.shape[0] - 2
    leaf_cols = bordered.shape[1] - 2
    port_count = bordered.shape[-1]
    slot_count = coupling_t.shape[1]
    smem = pl.BlockSpec(memory_space=pltpu.SMEM)
    hbm = pl.BlockSpec(memory_space=pl.ANY)
    vmem = pl.BlockSpec(memory_space=pltpu.VMEM)
    rows, cols = leaf_rows * LEAF_R, leaf_cols * LEAF_C
    field, *edges = pl.pallas_call(
        leaf_kernel,
        in_specs=[smem, smem, hbm, hbm, hbm],
        out_specs=[vmem] * 5,
        out_shape=[
            jax.ShapeDtypeStruct((components, rows, cols, port_count), jnp.bfloat16),
            jax.ShapeDtypeStruct((rows, 1, port_count), jnp.bfloat16),
            jax.ShapeDtypeStruct((rows, 1, port_count), jnp.bfloat16),
            jax.ShapeDtypeStruct((1, cols, port_count), jnp.bfloat16),
            jax.ShapeDtypeStruct((1, cols, port_count), jnp.bfloat16),
        ],
        scratch_shapes=[
            pltpu.VMEM(bordered.shape, bordered.dtype),
            pltpu.VMEM(kernels.shape, kernels.dtype),
            pltpu.VMEM(filament.shape, filament.dtype),
            pltpu.SemaphoreType.DMA((leaf_rows + 2,)),
            pltpu.SemaphoreType.DMA((leaf_count,)),
            pltpu.SemaphoreType.DMA((leaf_count,)),
        ],
    )(codes, scales, bordered, kernels, filament)
    field, edges, bordered = lax.optimization_barrier((field, edges, bordered))
    volt = pl.pallas_call(
        induced_kernel,
        in_specs=[hbm, vmem, vmem],
        out_specs=vmem,
        out_shape=jax.ShapeDtypeStruct((slot_count, port_count), jnp.bfloat16),
        scratch_shapes=[
            pltpu.VMEM((leaf_rows,) + bordered.shape[1:], bordered.dtype),
            pltpu.VMEM((leaf_count,) + coupling_t.shape, coupling_t.dtype),
            pltpu.SemaphoreType.DMA((leaf_rows,)),
        ],
    )(bordered, row_leaf, coupling_t)
    return (field, edges), volt


def body(stream, inductance, near_lists, filament_leaf, filament_current, filament_coupling):
    port_count = stream.shape[0]
    leaf_rows = inductance.shape[0]
    leaf_cols = inductance.shape[1]
    near_count = inductance.shape[2]
    leaf_cells = inductance.shape[4]
    leaf_count = leaf_rows * leaf_cols
    half_cols = leaf_cols * LEAF_C
    nx, ny, nz = device_grid()
    gx = lax.axis_index("gx")
    col_index = lax.axis_index("gy") * nz + lax.axis_index("gz")
    owners = nx * ny * nz

    filament_count = filament_leaf.shape[0]
    capacity = max(2, 2 * filament_count // owners)
    slot_count = owners * capacity
    plane_cols = leaf_cols * ny * nz
    leaf_row = filament_leaf // plane_cols
    leaf_col = filament_leaf % plane_cols
    owner_ids = leaf_row // leaf_rows * (ny * nz) + leaf_col // leaf_cols
    local_ids = leaf_row % leaf_rows * leaf_cols + leaf_col % leaf_cols
    index = jnp.arange(filament_count, dtype=jnp.int32)
    earlier = (owner_ids[None, :] == owner_ids[:, None]) & (index[None, :] < index[:, None])
    position = jnp.sum(earlier.astype(jnp.int32), axis=1)
    target_slot = owner_ids * capacity + position
    placement_mask = target_slot[None, :] == jnp.arange(slot_count, dtype=jnp.int32)[:, None]
    placement = placement_mask.astype(jnp.bfloat16)
    row_width = 2 * leaf_cells + port_count
    rows_out = jnp.concatenate(
        [filament_coupling.reshape(filament_count, 2 * leaf_cells), filament_current], 1
    )
    sent = jnp.dot(placement, rows_out, preferred_element_type=jnp.float32).astype(jnp.bfloat16)
    sent_leaf = jnp.dot(
        placement, (local_ids + 1).astype(jnp.bfloat16), preferred_element_type=jnp.float32
    ) - 1.0
    leaf_row_block = jnp.pad(
        sent_leaf.astype(jnp.bfloat16).reshape(owners, 1, capacity),
        ((0, 0), (0, 0), (0, row_width - capacity)),
    )
    payload = jnp.concatenate([sent.reshape(owners, capacity, row_width), leaf_row_block], 1)
    got = lax.all_to_all(payload, AXES, split_axis=0, concat_axis=0, tiled=True)
    got_rows = got[:, :capacity].reshape(slot_count, row_width)
    got_leaf = got[:, capacity, :capacity].reshape(slot_count).astype(jnp.int32)
    got_coupling_t = got_rows[:, : 2 * leaf_cells].T
    got_current = got_rows[:, 2 * leaf_cells :]
    got_leaf = got_leaf.reshape(1, slot_count)
    filament = filament_field(got_leaf, got_coupling_t, got_current, leaf_count)

    window, (got_leaf, got_coupling_t, filament) = stream_window(
        stream.transpose(1, 2, 0), half_cols, (got_leaf, got_coupling_t, filament)
    )
    currents = plane_curl(window).astype(jnp.bfloat16)
    bordered = to_leaves(currents)
    src_row = jnp.arange(leaf_rows, dtype=jnp.int32)[:, None, None] + near_lists // 3
    src_col = jnp.arange(leaf_cols, dtype=jnp.int32)[None, :, None] + near_lists % 3
    row_ok = ((src_row > 0) | (gx > 0)) & ((src_row < leaf_rows + 1) | (gx < nx - 1))
    col_ok = ((src_col > 0) | (col_index > 0)) & (
        (src_col < leaf_cols + 1) | (col_index < ny * nz - 1)
    )
    scales = (row_ok & col_ok).astype(jnp.int32).reshape(leaf_count, near_count)

    kernels = inductance.reshape(leaf_count, near_count, 2, leaf_cells, leaf_cells)
    codes = near_lists.reshape(leaf_count, near_count)
    total_field, induced = leaf_fields(
        codes, scales, bordered, kernels, filament, got_leaf, got_coupling_t
    )
    returned = lax.all_to_all(
        induced.reshape(owners, capacity, port_count), AXES, split_axis=0, concat_axis=0, tiled=True
    ).reshape(slot_count, port_count)
    filament_voltage = lax.dot_general(
        placement, returned, (((0,), (0,)), ((), ())), preferred_element_type=jnp.float32
    ).astype(jnp.bfloat16)

    loop_voltage = field_halo(*total_field).transpose(2, 0, 1)
    return (loop_voltage, filament_voltage)


def solution(mesh):
    return jax.shard_map(
        body,
        mesh=mesh,
        in_specs=(
            P("groups", "gx", "gy"),
            P(("groups", "gx"), ("gy", "gz"), None, None, None, None),
            P(("groups", "gx"), ("gy", "gz"), None),
            P(("groups", "gx", "gy", "gz")),
            P(("groups", "gx", "gy", "gz"), None),
            P(("groups", "gx", "gy", "gz"), None, None),
        ),
        out_specs=(P("groups", "gx", ("gy", "gz")), P(("groups", "gx", "gy", "gz"), None)),
        check_vma=False,
    )
```

```python
import jax
import jax.numpy as jnp
from jax import lax
from jax.experimental import pallas as pl
from jax.experimental.pallas import tpu as pltpu
from jax.sharding import PartitionSpec as P

LEAF_R = 8
LEAF_C = 16
AXES = ("gx", "gy", "gz")


def plane_curl(padded):
    along_y = padded[1:-1, 2:] - padded[1:-1, :-2]
    along_x = padded[:-2, 1:-1] - padded[2:, 1:-1]
    return jnp.stack([along_y, along_x])


def to_leaves(grid_values):
    components, row_count, col_count, port_count = grid_values.shape
    blocks = grid_values.reshape(
        components, row_count // LEAF_R, LEAF_R, col_count // LEAF_C, LEAF_C, port_count
    )
    blocks = blocks.transpose(1, 3, 0, 2, 4, 5)
    return blocks.reshape(
        row_count // LEAF_R, col_count // LEAF_C, components, LEAF_R * LEAF_C, port_count
    )


def from_leaves(leaves):
    leaf_rows, leaf_cols, components, leaf_cells, port_count = leaves.shape
    blocks = leaves.reshape(leaf_rows, leaf_cols, components, LEAF_R, LEAF_C, port_count)
    blocks = blocks.transpose(2, 0, 3, 1, 4, 5)
    return blocks.reshape(components, leaf_rows * LEAF_R, leaf_cols * LEAF_C, port_count)


def device_grid():
    nx, ny, nz = (lax.axis_size(a) for a in AXES)
    return nx, ny, nz


def pairs_by(fn):
    nx, ny, nz = device_grid()
    out = []
    for x in range(nx):
        for y in range(ny):
            for z in range(nz):
                target = fn(x, y, z)
                if target is None:
                    continue
                tx, ty, tz = target
                if 0 <= tx < nx and 0 <= ty < ny and 0 <= tz < nz:
                    out.append(((x * ny + y) * nz + z, (tx * ny + ty) * nz + tz))
    return out


def send(value, fn):
    return lax.ppermute(value, AXES, pairs_by(fn))


def sideways(x, y, z, dx):
    nz = lax.axis_size("gz")
    if z == nz - 1:
        return (x + dx, y + 1, 0)
    if z == 0:
        return (x + dx, y - 1, nz - 1)
    return None


def stream_window(stream, half, ready):
    gz = lax.axis_index("gz")
    rows, width = stream.shape[0], stream.shape[1]
    hr, hc = LEAF_R + 1, LEAF_C + 1
    mid_w = half + hc
    mid = lax.dynamic_slice_in_dim(stream, gz * (width - mid_w), mid_w, 1)
    side = lax.dynamic_slice_in_dim(stream, gz * (width - hc), hc, 1)
    h_got = send(side, lambda x, y, z: sideways(x, y, z, 0))
    wide = lax.dynamic_slice_in_dim(
        jnp.concatenate([h_got, mid, h_got], 1), gz * hc, mid_w + hc, 1
    )
    v_top = send(wide[rows - hr :], lambda x, y, z: (x + 1, y, z))
    v_bot = send(wide[:hr], lambda x, y, z: (x - 1, y, z))
    (v_top, v_bot), ready = lax.optimization_barrier(((v_top, v_bot), ready))
    return jnp.concatenate([v_top, wide, v_bot], 0), ready


def field_halo(grid_field, edges):
    x_field = grid_field[0]
    y_field = grid_field[1]
    x_first, x_last, y_first, y_last = edges

    def step(x, y, z, dc):
        nz = lax.axis_size("gz")
        c = y * nz + z + dc
        return (x, c // nz, c % nz) if c >= 0 else None

    x_left = send(x_last, lambda x, y, z: step(x, y, z, 1))
    x_right = send(x_first, lambda x, y, z: step(x, y, z, -1))
    y_top = send(y_last, lambda x, y, z: (x + 1, y, z))
    y_bot = send(y_first, lambda x, y, z: (x - 1, y, z))
    x_pad = jnp.concatenate([x_left, x_field, x_right], 1).astype(jnp.float32)
    y_pad = jnp.concatenate([y_top, y_field, y_bot], 0).astype(jnp.float32)
    return x_pad[:, :-2] - x_pad[:, 2:] + (y_pad[2:] - y_pad[:-2])


def filament_kernel(row_leaf_ref, cpl_t_ref, cur_ref, fil_ref):
    def one_leaf(leaf, carry):
        coupling_t = cpl_t_ref[...]
        coupling_t = jnp.where(row_leaf_ref[...] == leaf, coupling_t, jnp.zeros_like(coupling_t))
        fil_ref[leaf] = jnp.dot(coupling_t, cur_ref[...], preferred_element_type=jnp.float32)
        return carry

    lax.fori_loop(0, fil_ref.shape[0], one_leaf, 0)


def filament_field(row_leaf, coupling_t, current, leaf_count):
    vmem = pl.BlockSpec(memory_space=pltpu.VMEM)
    return pl.pallas_call(
        filament_kernel,
        in_specs=[vmem, vmem, vmem],
        out_specs=vmem,
        out_shape=jax.ShapeDtypeStruct(
            (leaf_count, coupling_t.shape[0], current.shape[1]), jnp.float32
        ),
    )(row_leaf, coupling_t, current)


def leaf_kernel(
    codes_ref, scale_ref, bord_hbm, ind_hbm, fil_hbm,
    field_ref, x_first_ref, x_last_ref, y_first_ref, y_last_ref,
    bord_ref, ind_ref, fil_ref, sems, fil_sems, ind_sems,
):
    leaf_count = ind_ref.shape[0]
    leaf_cols = bord_ref.shape[1] - 2
    near_count = ind_ref.shape[1]
    cells = ind_ref.shape[3]
    ring_rows = bord_ref.shape[0]

    def row_copy(r):
        return pltpu.make_async_copy(bord_hbm.at[r], bord_ref.at[r], sems.at[r])

    def fil_copy(l):
        return pltpu.make_async_copy(fil_hbm.at[l], fil_ref.at[l], fil_sems.at[l])

    for r in range(ring_rows):
        row_copy(r).start()
    for l in range(leaf_count):
        fil_copy(l).start()
        pltpu.make_async_copy(ind_hbm.at[l], ind_ref.at[l], ind_sems.at[l]).start()
    for r in range(3):
        row_copy(r).wait()

    def one_leaf(leaf, carry):
        row = leaf // leaf_cols
        col = leaf % leaf_cols

        @pl.when((col == 0) & (row > 0))
        def _():
            row_copy(row + 2).wait()

        fil_copy(leaf).wait()
        pltpu.make_async_copy(ind_hbm.at[leaf], ind_ref.at[leaf], ind_sems.at[leaf]).wait()
        filament = fil_ref[leaf]
        sources = []
        for n in range(near_count):
            code = codes_ref[leaf, n]
            src_row = jnp.minimum(jnp.maximum(row + code // 3, 0), bord_ref.shape[0] - 1)
            src_col = jnp.minimum(jnp.maximum(col + code % 3, 0), bord_ref.shape[1] - 1)
            keep = scale_ref[leaf, n] > 0
            tile = bord_ref[src_row, src_col]
            sources.append(jnp.where(keep, tile, jnp.zeros_like(tile)))
        for c in range(2):
            weights = jnp.concatenate([ind_ref[leaf, n, c] for n in range(near_count)], axis=1)
            stacked = jnp.concatenate([s[c] for s in sources], axis=0)
            total = filament[c * cells : (c + 1) * cells] + jnp.dot(
                weights, stacked, preferred_element_type=jnp.float32
            )
            field_ref[c, pl.ds(row * LEAF_R, LEAF_R), pl.ds(pl.multiple_of(col * LEAF_C, LEAF_C), LEAF_C)] = (
                total.reshape(LEAF_R, LEAF_C, -1).astype(field_ref.dtype)
            )
        return carry

    lax.fori_loop(0, leaf_count, one_leaf, 0, unroll=4)
    rows, cols = field_ref.shape[1], field_ref.shape[2]
    x_first_ref[...] = field_ref[0, :, 0:1]
    x_last_ref[...] = field_ref[0, :, cols - 1 : cols]
    y_first_ref[...] = field_ref[1, 0:1]
    y_last_ref[...] = field_ref[1, rows - 1 : rows]


def induced_kernel(bord_hbm, row_leaf_ref, cpl_t_ref, volt_ref, own_ref, stack_ref, sems):
    leaf_rows = own_ref.shape[0]
    leaf_cols = own_ref.shape[1] - 2
    copies = [
        pltpu.make_async_copy(bord_hbm.at[r + 1], own_ref.at[r], sems.at[r]) for r in range(leaf_rows)
    ]
    for copy in copies:
        copy.start()
    coupling_t = cpl_t_ref[...]
    slot_leaf = row_leaf_ref[...]
    for leaf in range(leaf_rows * leaf_cols):
        stack_ref[leaf] = jnp.where(slot_leaf == leaf, coupling_t, jnp.zeros_like(coupling_t))
    for copy in copies:
        copy.wait()
    own = own_ref[:, 1 : leaf_cols + 1].reshape(-1, own_ref.shape[-1])
    stacked = stack_ref[...].reshape(own.shape[0], -1)
    volt = lax.dot_general(
        own, stacked, (((0,), (0,)), ((), ())), preferred_element_type=jnp.float32
    )
    volt_ref[...] = volt.T.astype(volt_ref.dtype)


def leaf_fields(codes, scales, bordered, kernels, filament, row_leaf, coupling_t):
    leaf_count, near_count, components, cells, _ = kernels.shape
    leaf_rows = bordered.shape[0] - 2
    leaf_cols = bordered.shape[1] - 2
    port_count = bordered.shape[-1]
    slot_count = coupling_t.shape[1]
    smem = pl.BlockSpec(memory_space=pltpu.SMEM)
    hbm = pl.BlockSpec(memory_space=pl.ANY)
    vmem = pl.BlockSpec(memory_space=pltpu.VMEM)
    rows, cols = leaf_rows * LEAF_R, leaf_cols * LEAF_C
    field, *edges = pl.pallas_call(
        leaf_kernel,
        in_specs=[smem, smem, hbm, hbm, hbm],
        out_specs=[vmem] * 5,
        out_shape=[
            jax.ShapeDtypeStruct((components, rows, cols, port_count), jnp.bfloat16),
            jax.ShapeDtypeStruct((rows, 1, port_count), jnp.bfloat16),
            jax.ShapeDtypeStruct((rows, 1, port_count), jnp.bfloat16),
            jax.ShapeDtypeStruct((1, cols, port_count), jnp.bfloat16),
            jax.ShapeDtypeStruct((1, cols, port_count), jnp.bfloat16),
        ],
        scratch_shapes=[
            pltpu.VMEM(bordered.shape, bordered.dtype),
            pltpu.VMEM(kernels.shape, kernels.dtype),
            pltpu.VMEM(filament.shape, filament.dtype),
            pltpu.SemaphoreType.DMA((leaf_rows + 2,)),
            pltpu.SemaphoreType.DMA((leaf_count,)),
            pltpu.SemaphoreType.DMA((leaf_count,)),
        ],
    )(codes, scales, bordered, kernels, filament)
    field, edges, bordered = lax.optimization_barrier((field, edges, bordered))
    volt = pl.pallas_call(
        induced_kernel,
        in_specs=[hbm, vmem, vmem],
        out_specs=vmem,
        out_shape=jax.ShapeDtypeStruct((slot_count, port_count), jnp.bfloat16),
        scratch_shapes=[
            pltpu.VMEM((leaf_rows,) + bordered.shape[1:], bordered.dtype),
            pltpu.VMEM((leaf_count,) + coupling_t.shape, coupling_t.dtype),
            pltpu.SemaphoreType.DMA((leaf_rows,)),
        ],
    )(bordered, row_leaf, coupling_t)
    return (field, edges), volt


def body(stream, inductance, near_lists, filament_leaf, filament_current, filament_coupling):
    port_count = stream.shape[0]
    leaf_rows = inductance.shape[0]
    leaf_cols = inductance.shape[1]
    near_count = inductance.shape[2]
    leaf_cells = inductance.shape[4]
    leaf_count = leaf_rows * leaf_cols
    half_cols = leaf_cols * LEAF_C
    nx, ny, nz = device_grid()
    gx = lax.axis_index("gx")
    col_index = lax.axis_index("gy") * nz + lax.axis_index("gz")
    owners = nx * ny * nz

    filament_count = filament_leaf.shape[0]
    capacity = max(2, 2 * filament_count // owners)
    slot_count = owners * capacity
    plane_cols = leaf_cols * ny * nz
    leaf_row = filament_leaf // plane_cols
    leaf_col = filament_leaf % plane_cols
    owner_ids = leaf_row // leaf_rows * (ny * nz) + leaf_col // leaf_cols
    local_ids = leaf_row % leaf_rows * leaf_cols + leaf_col % leaf_cols
    index = jnp.arange(filament_count, dtype=jnp.int32)
    earlier = (owner_ids[None, :] == owner_ids[:, None]) & (index[None, :] < index[:, None])
    position = jnp.sum(earlier.astype(jnp.int32), axis=1)
    target_slot = owner_ids * capacity + position
    placement_mask = target_slot[None, :] == jnp.arange(slot_count, dtype=jnp.int32)[:, None]
    placement = placement_mask.astype(jnp.bfloat16)
    row_width = 2 * leaf_cells + port_count
    rows_out = jnp.concatenate(
        [filament_coupling.reshape(filament_count, 2 * leaf_cells), filament_current], 1
    )
    sent = jnp.dot(placement, rows_out, preferred_element_type=jnp.float32).astype(jnp.bfloat16)
    sent_leaf = jnp.dot(
        placement, (local_ids + 1).astype(jnp.bfloat16), preferred_element_type=jnp.float32
    ) - 1.0
    leaf_row_block = jnp.pad(
        sent_leaf.astype(jnp.bfloat16).reshape(owners, 1, capacity),
        ((0, 0), (0, 0), (0, row_width - capacity)),
    )
    payload = jnp.concatenate([sent.reshape(owners, capacity, row_width), leaf_row_block], 1)
    got = lax.all_to_all(payload, AXES, split_axis=0, concat_axis=0, tiled=True)
    got_rows = got[:, :capacity].reshape(slot_count, row_width)
    got_leaf = got[:, capacity, :capacity].reshape(slot_count).astype(jnp.int32)
    got_coupling_t = got_rows[:, : 2 * leaf_cells].T
    got_current = got_rows[:, 2 * leaf_cells :]
    got_leaf = got_leaf.reshape(1, slot_count)
    filament = filament_field(got_leaf, got_coupling_t, got_current, leaf_count)

    window, (got_leaf, got_coupling_t, filament) = stream_window(
        stream.transpose(1, 2, 0), half_cols, (got_leaf, got_coupling_t, filament)
    )
    currents = plane_curl(window).astype(jnp.bfloat16)
    bordered = to_leaves(currents)
    src_row = jnp.arange(leaf_rows, dtype=jnp.int32)[:, None, None] + near_lists // 3
    src_col = jnp.arange(leaf_cols, dtype=jnp.int32)[None, :, None] + near_lists % 3
    row_ok = ((src_row > 0) | (gx > 0)) & ((src_row < leaf_rows + 1) | (gx < nx - 1))
    col_ok = ((src_col > 0) | (col_index > 0)) & (
        (src_col < leaf_cols + 1) | (col_index < ny * nz - 1)
    )
    scales = (row_ok & col_ok).astype(jnp.int32).reshape(leaf_count, near_count)

    kernels = inductance.reshape(leaf_count, near_count, 2, leaf_cells, leaf_cells)
    codes = near_lists.reshape(leaf_count, near_count)
    total_field, induced = leaf_fields(
        codes, scales, bordered, kernels, filament, got_leaf, got_coupling_t
    )
    returned = lax.all_to_all(
        induced.reshape(owners, capacity, port_count), AXES, split_axis=0, concat_axis=0, tiled=True
    ).reshape(slot_count, port_count)
    filament_voltage = lax.dot_general(
        placement, returned, (((0,), (0,)), ((), ())), preferred_element_type=jnp.float32
    ).astype(jnp.bfloat16)

    loop_voltage = field_halo(*total_field).transpose(2, 0, 1)
    return (loop_voltage, filament_voltage)


def solution(mesh):
    return jax.shard_map(
        body,
        mesh=mesh,
        in_specs=(
            P("groups", "gx", "gy"),
            P(("groups", "gx"), ("gy", "gz"), None, None, None, None),
            P(("groups", "gx"), ("gy", "gz"), None),
            P(("groups", "gx", "gy", "gz")),
            P(("groups", "gx", "gy", "gz"), None),
            P(("groups", "gx", "gy", "gz"), None, None),
        ),
        out_specs=(P("groups", "gx", ("gy", "gz")), P(("groups", "gx", "gy", "gz"), None)),
        check_vma=False,
    )
```

```python
import jax
import jax.numpy as jnp
from jax import lax
from jax.experimental import pallas as pl
from jax.experimental.pallas import tpu as pltpu
from jax.sharding import PartitionSpec as P

LEAF_R = 8
LEAF_C = 16
AXES = ("gx", "gy", "gz")


def plane_curl(padded):
    along_y = padded[1:-1, 2:] - padded[1:-1, :-2]
    along_x = padded[:-2, 1:-1] - padded[2:, 1:-1]
    return jnp.stack([along_y, along_x])


def to_leaves(grid_values):
    components, row_count, col_count, port_count = grid_values.shape
    blocks = grid_values.reshape(
        components, row_count // LEAF_R, LEAF_R, col_count // LEAF_C, LEAF_C, port_count
    )
    blocks = blocks.transpose(1, 3, 0, 2, 4, 5)
    return blocks.reshape(
        row_count // LEAF_R, col_count // LEAF_C, components, LEAF_R * LEAF_C, port_count
    )


def from_leaves(leaves):
    leaf_rows, leaf_cols, components, leaf_cells, port_count = leaves.shape
    blocks = leaves.reshape(leaf_rows, leaf_cols, components, LEAF_R, LEAF_C, port_count)
    blocks = blocks.transpose(2, 0, 3, 1, 4, 5)
    return blocks.reshape(components, leaf_rows * LEAF_R, leaf_cols * LEAF_C, port_count)


def device_grid():
    nx, ny, nz = (lax.axis_size(a) for a in AXES)
    return nx, ny, nz


def pairs_by(fn):
    nx, ny, nz = device_grid()
    out = []
    for x in range(nx):
        for y in range(ny):
            for z in range(nz):
                target = fn(x, y, z)
                if target is None:
                    continue
                tx, ty, tz = target
                if 0 <= tx < nx and 0 <= ty < ny and 0 <= tz < nz:
                    out.append(((x * ny + y) * nz + z, (tx * ny + ty) * nz + tz))
    return out


def send(value, fn):
    return lax.ppermute(value, AXES, pairs_by(fn))


def sideways(x, y, z, dx):
    nz = lax.axis_size("gz")
    if z == nz - 1:
        return (x + dx, y + 1, 0)
    if z == 0:
        return (x + dx, y - 1, nz - 1)
    return None


def stream_window(stream, half, ready):
    gz = lax.axis_index("gz")
    rows, width = stream.shape[0], stream.shape[1]
    hr, hc = LEAF_R + 1, LEAF_C + 1
    mid_w = half + hc
    mid = lax.dynamic_slice_in_dim(stream, gz * (width - mid_w), mid_w, 1)
    side = lax.dynamic_slice_in_dim(stream, gz * (width - hc), hc, 1)
    h_got = send(side, lambda x, y, z: sideways(x, y, z, 0))
    wide = lax.dynamic_slice_in_dim(
        jnp.concatenate([h_got, mid, h_got], 1), gz * hc, mid_w + hc, 1
    )
    v_top = send(wide[rows - hr :], lambda x, y, z: (x + 1, y, z))
    v_bot = send(wide[:hr], lambda x, y, z: (x - 1, y, z))
    (v_top, v_bot), ready = lax.optimization_barrier(((v_top, v_bot), ready))
    return jnp.concatenate([v_top, wide, v_bot], 0), ready


def field_halo(grid_field, edges):
    x_field = grid_field[0]
    y_field = grid_field[1]
    x_first, x_last, y_first, y_last = edges

    def step(x, y, z, dc):
        nz = lax.axis_size("gz")
        c = y * nz + z + dc
        return (x, c // nz, c % nz) if c >= 0 else None

    x_left = send(x_last, lambda x, y, z: step(x, y, z, 1))
    x_right = send(x_first, lambda x, y, z: step(x, y, z, -1))
    y_top = send(y_last, lambda x, y, z: (x + 1, y, z))
    y_bot = send(y_first, lambda x, y, z: (x - 1, y, z))
    x_pad = jnp.concatenate([x_left, x_field, x_right], 1).astype(jnp.float32)
    y_pad = jnp.concatenate([y_top, y_field, y_bot], 0).astype(jnp.float32)
    return x_pad[:, :-2] - x_pad[:, 2:] + (y_pad[2:] - y_pad[:-2])


def filament_kernel(row_leaf_ref, cpl_t_ref, cur_ref, fil_ref, stack_ref):
    coupling_t = cpl_t_ref[...]
    slot_leaf = row_leaf_ref[...]
    for leaf in range(fil_ref.shape[0]):
        stack_ref[leaf] = jnp.where(slot_leaf == leaf, coupling_t, jnp.zeros_like(coupling_t))
    stacked = stack_ref[...].reshape(-1, coupling_t.shape[1])
    fil_ref[...] = jnp.dot(stacked, cur_ref[...], preferred_element_type=jnp.float32).reshape(
        fil_ref.shape
    )


def filament_field(row_leaf, coupling_t, current, leaf_count):
    vmem = pl.BlockSpec(memory_space=pltpu.VMEM)
    return pl.pallas_call(
        filament_kernel,
        in_specs=[vmem, vmem, vmem],
        out_specs=vmem,
        out_shape=jax.ShapeDtypeStruct(
            (leaf_count, coupling_t.shape[0], current.shape[1]), jnp.float32
        ),
        scratch_shapes=[pltpu.VMEM((leaf_count,) + coupling_t.shape, coupling_t.dtype)],
    )(row_leaf, coupling_t, current)


def leaf_kernel(
    codes_ref, scale_ref, bord_hbm, ind_hbm, fil_hbm,
    field_ref, x_first_ref, x_last_ref, y_first_ref, y_last_ref,
    bord_ref, ind_ref, fil_ref, sems, fil_sems, ind_sems,
):
    leaf_count = ind_ref.shape[0]
    leaf_cols = bord_ref.shape[1] - 2
    near_count = ind_ref.shape[1]
    cells = ind_ref.shape[3]
    ring_rows = bord_ref.shape[0]

    def row_copy(r):
        return pltpu.make_async_copy(bord_hbm.at[r], bord_ref.at[r], sems.at[r])

    def fil_copy(l):
        return pltpu.make_async_copy(fil_hbm.at[l], fil_ref.at[l], fil_sems.at[l])

    for r in range(ring_rows):
        row_copy(r).start()
    for l in range(leaf_count):
        fil_copy(l).start()
        pltpu.make_async_copy(ind_hbm.at[l], ind_ref.at[l], ind_sems.at[l]).start()
    for r in range(3):
        row_copy(r).wait()

    def one_leaf(leaf, carry):
        row = leaf // leaf_cols
        col = leaf % leaf_cols

        @pl.when((col == 0) & (row > 0))
        def _():
            row_copy(row + 2).wait()

        fil_copy(leaf).wait()
        pltpu.make_async_copy(ind_hbm.at[leaf], ind_ref.at[leaf], ind_sems.at[leaf]).wait()
        filament = fil_ref[leaf]
        sources = []
        for n in range(near_count):
            code = codes_ref[leaf, n]
            src_row = jnp.minimum(jnp.maximum(row + code // 3, 0), bord_ref.shape[0] - 1)
            src_col = jnp.minimum(jnp.maximum(col + code % 3, 0), bord_ref.shape[1] - 1)
            keep = scale_ref[leaf, n] > 0
            tile = bord_ref[src_row, src_col]
            sources.append(jnp.where(keep, tile, jnp.zeros_like(tile)))
        for c in range(2):
            weights = jnp.concatenate([ind_ref[leaf, n, c] for n in range(near_count)], axis=1)
            stacked = jnp.concatenate([s[c] for s in sources], axis=0)
            total = filament[c * cells : (c + 1) * cells] + jnp.dot(
                weights, stacked, preferred_element_type=jnp.float32
            )
            field_ref[c, pl.ds(row * LEAF_R, LEAF_R), pl.ds(pl.multiple_of(col * LEAF_C, LEAF_C), LEAF_C)] = (
                total.reshape(LEAF_R, LEAF_C, -1).astype(field_ref.dtype)
            )
        return carry

    lax.fori_loop(0, leaf_count, one_leaf, 0, unroll=2)
    rows, cols = field_ref.shape[1], field_ref.shape[2]
    x_first_ref[...] = field_ref[0, :, 0:1]
    x_last_ref[...] = field_ref[0, :, cols - 1 : cols]
    y_first_ref[...] = field_ref[1, 0:1]
    y_last_ref[...] = field_ref[1, rows - 1 : rows]


def induced_kernel(bord_hbm, row_leaf_ref, cpl_t_ref, volt_ref, own_ref, stack_ref, sems):
    leaf_rows = own_ref.shape[0]
    leaf_cols = own_ref.shape[1] - 2
    copies = [
        pltpu.make_async_copy(bord_hbm.at[r + 1], own_ref.at[r], sems.at[r]) for r in range(leaf_rows)
    ]
    for copy in copies:
        copy.start()
    coupling_t = cpl_t_ref[...]
    slot_leaf = row_leaf_ref[...]
    for leaf in range(leaf_rows * leaf_cols):
        stack_ref[leaf] = jnp.where(slot_leaf == leaf, coupling_t, jnp.zeros_like(coupling_t))
    for copy in copies:
        copy.wait()
    own = own_ref[:, 1 : leaf_cols + 1].reshape(-1, own_ref.shape[-1])
    stacked = stack_ref[...].reshape(own.shape[0], -1)
    volt = lax.dot_general(
        own, stacked, (((0,), (0,)), ((), ())), preferred_element_type=jnp.float32
    )
    volt_ref[...] = volt.T.astype(volt_ref.dtype)


def leaf_fields(codes, scales, bordered, kernels, filament, row_leaf, coupling_t):
    leaf_count, near_count, components, cells, _ = kernels.shape
    leaf_rows = bordered.shape[0] - 2
    leaf_cols = bordered.shape[1] - 2
    port_count = bordered.shape[-1]
    slot_count = coupling_t.shape[1]
    smem = pl.BlockSpec(memory_space=pltpu.SMEM)
    hbm = pl.BlockSpec(memory_space=pl.ANY)
    vmem = pl.BlockSpec(memory_space=pltpu.VMEM)
    rows, cols = leaf_rows * LEAF_R, leaf_cols * LEAF_C
    field, *edges = pl.pallas_call(
        leaf_kernel,
        in_specs=[smem, smem, hbm, hbm, hbm],
        out_specs=[vmem] * 5,
        out_shape=[
            jax.ShapeDtypeStruct((components, rows, cols, port_count), jnp.bfloat16),
            jax.ShapeDtypeStruct((rows, 1, port_count), jnp.bfloat16),
            jax.ShapeDtypeStruct((rows, 1, port_count), jnp.bfloat16),
            jax.ShapeDtypeStruct((1, cols, port_count), jnp.bfloat16),
            jax.ShapeDtypeStruct((1, cols, port_count), jnp.bfloat16),
        ],
        scratch_shapes=[
            pltpu.VMEM(bordered.shape, bordered.dtype),
            pltpu.VMEM(kernels.shape, kernels.dtype),
            pltpu.VMEM(filament.shape, filament.dtype),
            pltpu.SemaphoreType.DMA((leaf_rows + 2,)),
            pltpu.SemaphoreType.DMA((leaf_count,)),
            pltpu.SemaphoreType.DMA((leaf_count,)),
        ],
    )(codes, scales, bordered, kernels, filament)
    field, edges, bordered = lax.optimization_barrier((field, edges, bordered))
    volt = pl.pallas_call(
        induced_kernel,
        in_specs=[hbm, vmem, vmem],
        out_specs=vmem,
        out_shape=jax.ShapeDtypeStruct((slot_count, port_count), jnp.bfloat16),
        scratch_shapes=[
            pltpu.VMEM((leaf_rows,) + bordered.shape[1:], bordered.dtype),
            pltpu.VMEM((leaf_count,) + coupling_t.shape, coupling_t.dtype),
            pltpu.SemaphoreType.DMA((leaf_rows,)),
        ],
    )(bordered, row_leaf, coupling_t)
    return (field, edges), volt


def body(stream, inductance, near_lists, filament_leaf, filament_current, filament_coupling):
    port_count = stream.shape[0]
    leaf_rows = inductance.shape[0]
    leaf_cols = inductance.shape[1]
    near_count = inductance.shape[2]
    leaf_cells = inductance.shape[4]
    leaf_count = leaf_rows * leaf_cols
    half_cols = leaf_cols * LEAF_C
    nx, ny, nz = device_grid()
    gx = lax.axis_index("gx")
    col_index = lax.axis_index("gy") * nz + lax.axis_index("gz")
    owners = nx * ny * nz

    filament_count = filament_leaf.shape[0]
    capacity = max(2, 2 * filament_count // owners)
    slot_count = owners * capacity
    plane_cols = leaf_cols * ny * nz
    leaf_row = filament_leaf // plane_cols
    leaf_col = filament_leaf % plane_cols
    owner_ids = leaf_row // leaf_rows * (ny * nz) + leaf_col // leaf_cols
    local_ids = leaf_row % leaf_rows * leaf_cols + leaf_col % leaf_cols
    index = jnp.arange(filament_count, dtype=jnp.int32)
    earlier = (owner_ids[None, :] == owner_ids[:, None]) & (index[None, :] < index[:, None])
    position = jnp.sum(earlier.astype(jnp.int32), axis=1)
    target_slot = owner_ids * capacity + position
    placement_mask = target_slot[None, :] == jnp.arange(slot_count, dtype=jnp.int32)[:, None]
    placement = placement_mask.astype(jnp.bfloat16)
    row_width = 2 * leaf_cells + port_count
    rows_out = jnp.concatenate(
        [filament_coupling.reshape(filament_count, 2 * leaf_cells), filament_current], 1
    )
    sent = jnp.dot(placement, rows_out, preferred_element_type=jnp.float32).astype(jnp.bfloat16)
    sent_leaf = jnp.dot(
        placement, (local_ids + 1).astype(jnp.bfloat16), preferred_element_type=jnp.float32
    ) - 1.0
    leaf_row_block = jnp.pad(
        sent_leaf.astype(jnp.bfloat16).reshape(owners, 1, capacity),
        ((0, 0), (0, 0), (0, row_width - capacity)),
    )
    payload = jnp.concatenate([sent.reshape(owners, capacity, row_width), leaf_row_block], 1)
    got = lax.all_to_all(payload, AXES, split_axis=0, concat_axis=0, tiled=True)
    got_rows = got[:, :capacity].reshape(slot_count, row_width)
    got_leaf = got[:, capacity, :capacity].reshape(slot_count).astype(jnp.int32)
    got_coupling_t = got_rows[:, : 2 * leaf_cells].T
    got_current = got_rows[:, 2 * leaf_cells :]
    got_leaf = got_leaf.reshape(1, slot_count)
    filament = filament_field(got_leaf, got_coupling_t, got_current, leaf_count)

    window, (got_leaf, got_coupling_t, filament) = stream_window(
        stream.transpose(1, 2, 0), half_cols, (got_leaf, got_coupling_t, filament)
    )
    currents = plane_curl(window).astype(jnp.bfloat16)
    bordered = to_leaves(currents)
    src_row = jnp.arange(leaf_rows, dtype=jnp.int32)[:, None, None] + near_lists // 3
    src_col = jnp.arange(leaf_cols, dtype=jnp.int32)[None, :, None] + near_lists % 3
    row_ok = ((src_row > 0) | (gx > 0)) & ((src_row < leaf_rows + 1) | (gx < nx - 1))
    col_ok = ((src_col > 0) | (col_index > 0)) & (
        (src_col < leaf_cols + 1) | (col_index < ny * nz - 1)
    )
    scales = (row_ok & col_ok).astype(jnp.int32).reshape(leaf_count, near_count)

    kernels = inductance.reshape(leaf_count, near_count, 2, leaf_cells, leaf_cells)
    codes = near_lists.reshape(leaf_count, near_count)
    total_field, induced = leaf_fields(
        codes, scales, bordered, kernels, filament, got_leaf, got_coupling_t
    )
    returned = lax.all_to_all(
        induced.reshape(owners, capacity, port_count), AXES, split_axis=0, concat_axis=0, tiled=True
    ).reshape(slot_count, port_count)
    filament_voltage = lax.dot_general(
        placement, returned, (((0,), (0,)), ((), ())), preferred_element_type=jnp.float32
    ).astype(jnp.bfloat16)

    loop_voltage = field_halo(*total_field).transpose(2, 0, 1)
    return (loop_voltage, filament_voltage)


def solution(mesh):
    return jax.shard_map(
        body,
        mesh=mesh,
        in_specs=(
            P("groups", "gx", "gy"),
            P(("groups", "gx"), ("gy", "gz"), None, None, None, None),
            P(("groups", "gx"), ("gy", "gz"), None),
            P(("groups", "gx", "gy", "gz")),
            P(("groups", "gx", "gy", "gz"), None),
            P(("groups", "gx", "gy", "gz"), None, None),
        ),
        out_specs=(P("groups", "gx", ("gy", "gz")), P(("groups", "gx", "gy", "gz"), None)),
        check_vma=False,
    )
```

```python
import jax
import jax.numpy as jnp
from jax import lax
from jax.experimental import pallas as pl
from jax.experimental.pallas import tpu as pltpu
from jax.sharding import PartitionSpec as P

LEAF_R = 8
LEAF_C = 16
AXES = ("gx", "gy", "gz")


def plane_curl(padded):
    along_y = padded[1:-1, 2:] - padded[1:-1, :-2]
    along_x = padded[:-2, 1:-1] - padded[2:, 1:-1]
    return jnp.stack([along_y, along_x])


def to_leaves(grid_values):
    components, row_count, col_count, port_count = grid_values.shape
    blocks = grid_values.reshape(
        components, row_count // LEAF_R, LEAF_R, col_count // LEAF_C, LEAF_C, port_count
    )
    blocks = blocks.transpose(1, 3, 0, 2, 4, 5)
    return blocks.reshape(
        row_count // LEAF_R, col_count // LEAF_C, components, LEAF_R * LEAF_C, port_count
    )


def from_leaves(leaves):
    leaf_rows, leaf_cols, components, leaf_cells, port_count = leaves.shape
    blocks = leaves.reshape(leaf_rows, leaf_cols, components, LEAF_R, LEAF_C, port_count)
    blocks = blocks.transpose(2, 0, 3, 1, 4, 5)
    return blocks.reshape(components, leaf_rows * LEAF_R, leaf_cols * LEAF_C, port_count)


def device_grid():
    nx, ny, nz = (lax.axis_size(a) for a in AXES)
    return nx, ny, nz


def pairs_by(fn):
    nx, ny, nz = device_grid()
    out = []
    for x in range(nx):
        for y in range(ny):
            for z in range(nz):
                target = fn(x, y, z)
                if target is None:
                    continue
                tx, ty, tz = target
                if 0 <= tx < nx and 0 <= ty < ny and 0 <= tz < nz:
                    out.append(((x * ny + y) * nz + z, (tx * ny + ty) * nz + tz))
    return out


def send(value, fn):
    return lax.ppermute(value, AXES, pairs_by(fn))


def sideways(x, y, z, dx):
    nz = lax.axis_size("gz")
    if z == nz - 1:
        return (x + dx, y + 1, 0)
    if z == 0:
        return (x + dx, y - 1, nz - 1)
    return None


def stream_window(stream, half, ready):
    gz = lax.axis_index("gz")
    rows, width = stream.shape[0], stream.shape[1]
    hr, hc = LEAF_R + 1, LEAF_C + 1
    mid_w = half + hc
    mid = lax.dynamic_slice_in_dim(stream, gz * (width - mid_w), mid_w, 1)
    side = lax.dynamic_slice_in_dim(stream, gz * (width - hc), hc, 1)
    h_got = send(side, lambda x, y, z: sideways(x, y, z, 0))
    wide = lax.dynamic_slice_in_dim(
        jnp.concatenate([h_got, mid, h_got], 1), gz * hc, mid_w + hc, 1
    )
    v_top = send(wide[rows - hr :], lambda x, y, z: (x + 1, y, z))
    v_bot = send(wide[:hr], lambda x, y, z: (x - 1, y, z))
    (v_top, v_bot), ready = lax.optimization_barrier(((v_top, v_bot), ready))
    return jnp.concatenate([v_top, wide, v_bot], 0), ready


def field_halo(grid_field, edges):
    x_field = grid_field[0]
    y_field = grid_field[1]
    x_first, x_last, y_first, y_last = edges

    def step(x, y, z, dc):
        nz = lax.axis_size("gz")
        c = y * nz + z + dc
        return (x, c // nz, c % nz) if c >= 0 else None

    x_left = send(x_last, lambda x, y, z: step(x, y, z, 1))
    x_right = send(x_first, lambda x, y, z: step(x, y, z, -1))
    y_top = send(y_last, lambda x, y, z: (x + 1, y, z))
    y_bot = send(y_first, lambda x, y, z: (x - 1, y, z))
    x_pad = jnp.concatenate([x_left, x_field, x_right], 1).astype(jnp.float32)
    y_pad = jnp.concatenate([y_top, y_field, y_bot], 0).astype(jnp.float32)
    return x_pad[:, :-2] - x_pad[:, 2:] + (y_pad[2:] - y_pad[:-2])


def filament_kernel(row_leaf_ref, cpl_t_ref, cur_ref, fil_ref):
    def one_leaf(leaf, carry):
        coupling_t = cpl_t_ref[...]
        coupling_t = jnp.where(row_leaf_ref[...] == leaf, coupling_t, jnp.zeros_like(coupling_t))
        fil_ref[leaf] = jnp.dot(coupling_t, cur_ref[...], preferred_element_type=jnp.float32)
        return carry

    lax.fori_loop(0, fil_ref.shape[0], one_leaf, 0)


def filament_field(row_leaf, coupling_t, current, leaf_count):
    vmem = pl.BlockSpec(memory_space=pltpu.VMEM)
    return pl.pallas_call(
        filament_kernel,
        in_specs=[vmem, vmem, vmem],
        out_specs=vmem,
        out_shape=jax.ShapeDtypeStruct(
            (leaf_count, coupling_t.shape[0], current.shape[1]), jnp.float32
        ),
    )(row_leaf, coupling_t, current)


def leaf_kernel(
    codes_ref, scale_ref, bord_hbm, ind_hbm, fil_hbm,
    field_ref, x_first_ref, x_last_ref, y_first_ref, y_last_ref,
    bord_ref, ind_ref, fil_ref, sems, fil_sems, ind_sems,
):
    leaf_count = ind_ref.shape[0]
    leaf_cols = bord_ref.shape[1] - 2
    near_count = ind_ref.shape[1]
    cells = ind_ref.shape[3]
    ring_rows = bord_ref.shape[0]

    def row_copy(r):
        return pltpu.make_async_copy(bord_hbm.at[r], bord_ref.at[r], sems.at[r])

    def fil_copy(l):
        return pltpu.make_async_copy(fil_hbm.at[l], fil_ref.at[l], fil_sems.at[l])

    for r in range(ring_rows):
        row_copy(r).start()
    for l in range(leaf_count):
        fil_copy(l).start()
        pltpu.make_async_copy(ind_hbm.at[l], ind_ref.at[l], ind_sems.at[l]).start()
    for r in range(3):
        row_copy(r).wait()

    def one_leaf(leaf, carry):
        row = leaf // leaf_cols
        col = leaf % leaf_cols

        @pl.when((col == 0) & (row > 0))
        def _():
            row_copy(row + 2).wait()

        fil_copy(leaf).wait()
        pltpu.make_async_copy(ind_hbm.at[leaf], ind_ref.at[leaf], ind_sems.at[leaf]).wait()
        filament = fil_ref[leaf]
        sources = []
        for n in range(near_count):
            code = codes_ref[leaf, n]
            src_row = jnp.minimum(jnp.maximum(row + code // 3, 0), bord_ref.shape[0] - 1)
            src_col = jnp.minimum(jnp.maximum(col + code % 3, 0), bord_ref.shape[1] - 1)
            keep = scale_ref[leaf, n] > 0
            tile = bord_ref[src_row, src_col]
            sources.append(jnp.where(keep, tile, jnp.zeros_like(tile)))
        for c in range(2):
            weights = jnp.concatenate([ind_ref[leaf, n, c] for n in range(near_count)], axis=1)
            stacked = jnp.concatenate([s[c] for s in sources], axis=0)
            total = filament[c * cells : (c + 1) * cells] + jnp.dot(
                weights, stacked, preferred_element_type=jnp.float32
            )
            field_ref[c, pl.ds(row * LEAF_R, LEAF_R), pl.ds(pl.multiple_of(col * LEAF_C, LEAF_C), LEAF_C)] = (
                total.reshape(LEAF_R, LEAF_C, -1).astype(field_ref.dtype)
            )
        return carry

    lax.fori_loop(0, leaf_count, one_leaf, 0, unroll=2)
    rows, cols = field_ref.shape[1], field_ref.shape[2]
    x_first_ref[...] = field_ref[0, :, 0:1]
    x_last_ref[...] = field_ref[0, :, cols - 1 : cols]
    y_first_ref[...] = field_ref[1, 0:1]
    y_last_ref[...] = field_ref[1, rows - 1 : rows]


def induced_kernel(bord_hbm, row_leaf_ref, cpl_t_ref, volt_ref, own_ref, stack_ref, sems):
    leaf_rows = own_ref.shape[0]
    leaf_cols = own_ref.shape[1] - 2
    copies = [
        pltpu.make_async_copy(bord_hbm.at[r + 1], own_ref.at[r], sems.at[r]) for r in range(leaf_rows)
    ]
    for copy in copies:
        copy.start()
    coupling_t = cpl_t_ref[...]
    slot_leaf = row_leaf_ref[...]
    for leaf in range(leaf_rows * leaf_cols):
        stack_ref[leaf] = jnp.where(slot_leaf == leaf, coupling_t, jnp.zeros_like(coupling_t))
    for copy in copies:
        copy.wait()
    own = own_ref[:, 1 : leaf_cols + 1].reshape(-1, own_ref.shape[-1])
    stacked = stack_ref[...].reshape(own.shape[0], -1)
    volt = lax.dot_general(
        own, stacked, (((0,), (0,)), ((), ())), preferred_element_type=jnp.float32
    )
    volt_ref[...] = volt.T.astype(volt_ref.dtype)


def leaf_fields(codes, scales, bordered, kernels, filament, row_leaf, coupling_t):
    leaf_count, near_count, components, cells, _ = kernels.shape
    leaf_rows = bordered.shape[0] - 2
    leaf_cols = bordered.shape[1] - 2
    port_count = bordered.shape[-1]
    slot_count = coupling_t.shape[1]
    smem = pl.BlockSpec(memory_space=pltpu.SMEM)
    hbm = pl.BlockSpec(memory_space=pl.ANY)
    vmem = pl.BlockSpec(memory_space=pltpu.VMEM)
    rows, cols = leaf_rows * LEAF_R, leaf_cols * LEAF_C
    field, *edges = pl.pallas_call(
        leaf_kernel,
        in_specs=[smem, smem, hbm, hbm, hbm],
        out_specs=[vmem] * 5,
        out_shape=[
            jax.ShapeDtypeStruct((components, rows, cols, port_count), jnp.bfloat16),
            jax.ShapeDtypeStruct((rows, 1, port_count), jnp.bfloat16),
            jax.ShapeDtypeStruct((rows, 1, port_count), jnp.bfloat16),
            jax.ShapeDtypeStruct((1, cols, port_count), jnp.bfloat16),
            jax.ShapeDtypeStruct((1, cols, port_count), jnp.bfloat16),
        ],
        scratch_shapes=[
            pltpu.VMEM(bordered.shape, bordered.dtype),
            pltpu.VMEM(kernels.shape, kernels.dtype),
            pltpu.VMEM(filament.shape, filament.dtype),
            pltpu.SemaphoreType.DMA((leaf_rows + 2,)),
            pltpu.SemaphoreType.DMA((leaf_count,)),
            pltpu.SemaphoreType.DMA((leaf_count,)),
        ],
    )(codes, scales, bordered, kernels, filament)

    volt = pl.pallas_call(
        induced_kernel,
        in_specs=[hbm, vmem, vmem],
        out_specs=vmem,
        out_shape=jax.ShapeDtypeStruct((slot_count, port_count), jnp.bfloat16),
        scratch_shapes=[
            pltpu.VMEM((leaf_rows,) + bordered.shape[1:], bordered.dtype),
            pltpu.VMEM((leaf_count,) + coupling_t.shape, coupling_t.dtype),
            pltpu.SemaphoreType.DMA((leaf_rows,)),
        ],
    )(bordered, row_leaf, coupling_t)
    return (field, edges), volt


def body(stream, inductance, near_lists, filament_leaf, filament_current, filament_coupling):
    port_count = stream.shape[0]
    leaf_rows = inductance.shape[0]
    leaf_cols = inductance.shape[1]
    near_count = inductance.shape[2]
    leaf_cells = inductance.shape[4]
    leaf_count = leaf_rows * leaf_cols
    half_cols = leaf_cols * LEAF_C
    nx, ny, nz = device_grid()
    gx = lax.axis_index("gx")
    col_index = lax.axis_index("gy") * nz + lax.axis_index("gz")
    owners = nx * ny * nz

    filament_count = filament_leaf.shape[0]
    capacity = max(2, 2 * filament_count // owners)
    slot_count = owners * capacity
    plane_cols = leaf_cols * ny * nz
    leaf_row = filament_leaf // plane_cols
    leaf_col = filament_leaf % plane_cols
    owner_ids = leaf_row // leaf_rows * (ny * nz) + leaf_col // leaf_cols
    local_ids = leaf_row % leaf_rows * leaf_cols + leaf_col % leaf_cols
    index = jnp.arange(filament_count, dtype=jnp.int32)
    earlier = (owner_ids[None, :] == owner_ids[:, None]) & (index[None, :] < index[:, None])
    position = jnp.sum(earlier.astype(jnp.int32), axis=1)
    target_slot = owner_ids * capacity + position
    placement_mask = target_slot[None, :] == jnp.arange(slot_count, dtype=jnp.int32)[:, None]
    placement = placement_mask.astype(jnp.bfloat16)
    row_width = 2 * leaf_cells + port_count
    rows_out = jnp.concatenate(
        [filament_coupling.reshape(filament_count, 2 * leaf_cells), filament_current], 1
    )
    sent = jnp.dot(placement, rows_out, preferred_element_type=jnp.float32).astype(jnp.bfloat16)
    sent_leaf = jnp.dot(
        placement, (local_ids + 1).astype(jnp.bfloat16), preferred_element_type=jnp.float32
    ) - 1.0
    leaf_row_block = jnp.pad(
        sent_leaf.astype(jnp.bfloat16).reshape(owners, 1, capacity),
        ((0, 0), (0, 0), (0, row_width - capacity)),
    )
    payload = jnp.concatenate([sent.reshape(owners, capacity, row_width), leaf_row_block], 1)
    got = lax.all_to_all(payload, AXES, split_axis=0, concat_axis=0, tiled=True)
    got_rows = got[:, :capacity].reshape(slot_count, row_width)
    got_leaf = got[:, capacity, :capacity].reshape(slot_count).astype(jnp.int32)
    got_coupling_t = got_rows[:, : 2 * leaf_cells].T
    got_current = got_rows[:, 2 * leaf_cells :]
    got_leaf = got_leaf.reshape(1, slot_count)
    filament = filament_field(got_leaf, got_coupling_t, got_current, leaf_count)

    window, (got_leaf, got_coupling_t, filament) = stream_window(
        stream.transpose(1, 2, 0), half_cols, (got_leaf, got_coupling_t, filament)
    )
    currents = plane_curl(window).astype(jnp.bfloat16)
    bordered = to_leaves(currents)
    src_row = jnp.arange(leaf_rows, dtype=jnp.int32)[:, None, None] + near_lists // 3
    src_col = jnp.arange(leaf_cols, dtype=jnp.int32)[None, :, None] + near_lists % 3
    row_ok = ((src_row > 0) | (gx > 0)) & ((src_row < leaf_rows + 1) | (gx < nx - 1))
    col_ok = ((src_col > 0) | (col_index > 0)) & (
        (src_col < leaf_cols + 1) | (col_index < ny * nz - 1)
    )
    scales = (row_ok & col_ok).astype(jnp.int32).reshape(leaf_count, near_count)

    kernels = inductance.reshape(leaf_count, near_count, 2, leaf_cells, leaf_cells)
    codes = near_lists.reshape(leaf_count, near_count)
    total_field, induced = leaf_fields(
        codes, scales, bordered, kernels, filament, got_leaf, got_coupling_t
    )
    returned = lax.all_to_all(
        induced.reshape(owners, capacity, port_count), AXES, split_axis=0, concat_axis=0, tiled=True
    ).reshape(slot_count, port_count)
    filament_voltage = lax.dot_general(
        placement, returned, (((0,), (0,)), ((), ())), preferred_element_type=jnp.float32
    ).astype(jnp.bfloat16)

    loop_voltage = field_halo(*total_field).transpose(2, 0, 1)
    return (loop_voltage, filament_voltage)


def solution(mesh):
    return jax.shard_map(
        body,
        mesh=mesh,
        in_specs=(
            P("groups", "gx", "gy"),
            P(("groups", "gx"), ("gy", "gz"), None, None, None, None),
            P(("groups", "gx"), ("gy", "gz"), None),
            P(("groups", "gx", "gy", "gz")),
            P(("groups", "gx", "gy", "gz"), None),
            P(("groups", "gx", "gy", "gz"), None, None),
        ),
        out_specs=(P("groups", "gx", ("gy", "gz")), P(("groups", "gx", "gy", "gz"), None)),
        check_vma=False,
    )
```
